32 devices in a mesh: groups: 2 (over y), enc: 4 (over z), mp: 4 (over x, core).
Axes of the slice: x: 2, y: 2, z: 4, core: 2. Of those that a mesh axis runs over, the one named last changes fastest.
Arguments:
- hidden: bfloat16 [131072, 1024], P(('groups', 'enc'), 'mp'), parts along dimension 0, may hold values from -6 to 6
- proj_w: bfloat16 [1024, 128], P('mp'), may hold values from -0.1875 to 0.1875
- queries: bfloat16 [256, 32, 128], P(('groups', 'enc', 'mp')), parts along dimension 0, may hold values from -208 to 208
- lengths: int32 [512], P('groups'), parts along dimension 0, may hold values from 193 to 256, as said below
- candidates: int32 [256, 16], P(('groups', 'enc', 'mp')), parts along dimension 0, may hold values from 0 to 1023, as said below
Outputs:
- losses: float32 [256], P(('groups', 'enc', 'mp')), parts along dimension 0
- grad_w: float32 [2048, 128], P(('groups', 'mp')), parts along dimension 0
The draws below stay inside these ranges and needn't reach their ends.
There are 2 independent parts, one for each index of `groups`. The reference program is written for one: setup_inputs(seed, part) draws one part's arguments, and reference() takes and returns one part's arrays. A program takes and returns all parts, laid end to end along the dimension named above; an argument that names none is the same for every part. Nothing has to cross between parts.
Inputs may be any that keep to these rules, and one draw needn't show every extreme that they name: Entries are global block numbers of this part. Of the candidates of the 8 queries of one device (aligned rows), at most 16 lie in the 64 blocks of any one device along enc+mp, where device k holds blocks k * 64 to (k + 1) * 64 - 1; some device receives exactly 16 from every device. Blocks may repeat. `lengths`: some passage has 256 tokens and some has 193.
All inputs are finite; a program needn't handle non-finite values.
Results may differ from the reference program's by a relative error of at most 0.0013.
The reference program's roundings to bfloat16 on the way (of `embedded`, `weights`, `occ_grad` and `de_pre`) count: a program that leaves them out, or rounds other values in their place, can miss the bound.
Values may be sent and summed in bfloat16 or wider, within the bound.
No kernel may reach another device: no remote copies, remote signals or barrier semaphores. Data moves between devices by JAX's collectives and lax.ppermute only.
A program may use at most 128 MiB of HBM per device.

```python
import jax
import jax.numpy as jnp
from jax import lax

D = 1024
E = 128
L = 256
BLK = 64
QLEN = 32
CAND = 16
QRY_DEV = 8
OWNERS = 16
SLOTS = 128
CAP = 16
PAS = 256
TOKENS = 65536
NB = 1024
BLK_DEV = 64
Q = 128
LEN_MIN = 193


def draw_queries(key, part):
    values_drawn = jnp.clip(jax.random.normal(key, (Q, QLEN, E), jnp.float32), -6.0, 6.0) * 3.0
    return values_drawn.astype(jnp.bfloat16)


def draw_lengths(key, part):
    values_drawn = jax.random.randint(key, (PAS,), LEN_MIN, L + 1, jnp.int32)
    return values_drawn.at[0].set(L).at[1].set(LEN_MIN)


def draw_candidates(key, part):
    pool_size = OWNERS * CAP
    key_hot = jax.random.fold_in(key, 11)
    key_rest = jax.random.fold_in(key, 23)
    shuffled = jax.random.permutation(key_hot, OWNERS)
    bonuses = jnp.zeros((OWNERS,), jnp.int32).at[shuffled[:2]].set(4)
    per_slot = jnp.repeat(bonuses, CAP)

    def one_source(source_key):
        key_noise = jax.random.fold_in(source_key, 1)
        key_perm = jax.random.fold_in(source_key, 2)
        key_local = jax.random.fold_in(source_key, 3)
        noise_draw = jax.random.randint(key_noise, (pool_size,), 0, 1024, jnp.int32)
        priority = (noise_draw + per_slot * 1024) * pool_size + jnp.arange(pool_size, dtype=jnp.int32)
        ignored, chosen_idx = lax.top_k(priority, SLOTS)
        owners_of = (chosen_idx // CAP).astype(jnp.int32)
        owners_of = owners_of[jax.random.permutation(key_perm, SLOTS)]
        local_ids = jax.random.randint(key_local, (SLOTS,), 0, BLK_DEV, jnp.int32)
        return owners_of * BLK_DEV + local_ids
    results = jax.vmap(one_source)(jax.random.split(key_rest, OWNERS))
    return results.reshape(Q, CAND)


def steps_of(stream_key, extent, cuts, smallest, top_value):
    def one(position, blocks):
        steps = jax.random.uniform(jax.random.fold_in(jax.random.fold_in(stream_key, 6), position), (blocks,), jnp.float32, smallest / len(cuts), top_value / len(cuts))
        return jnp.repeat(jnp.exp(steps), extent[position] // blocks).reshape((-1,) + (1,) * (len(extent) - position - 1))

    loudness = one(*cuts[0])
    for cut in cuts[1:]:
        loudness = loudness * one(*cut)
    return loudness


def scatter_about(own_key, extent, scale, most, cuts=(), kind=jnp.bfloat16):
    result = jax.random.normal(own_key, extent, jnp.float32) * scale
    if len(cuts) > 0:
        result = steps_of(own_key, extent, cuts, -0.22, 0.18) * result
    return jnp.clip(result, min=-most, max=most).astype(kind)


def setup_inputs(seed: int = 0, part: int = 0) -> dict:
    streams_of = jax.random.split(jax.random.key(seed), 6)
    part_splits = jax.random.split(jax.random.fold_in(streams_of[5], part), 6)
    return {
        "hidden": scatter_about(part_splits[0], (TOKENS, D), 1.0, 6.0, ((0, 4), (1, 4))),
        "proj_w": scatter_about(streams_of[1], (D, E), D ** -0.5, 0.1875, ((0, 4),)),
        "queries": draw_queries(jax.random.fold_in(jax.random.fold_in(streams_of[5], part), 71), part),
        "lengths": draw_lengths(jax.random.fold_in(jax.random.fold_in(streams_of[5], part), 71), part),
        "candidates": draw_candidates(jax.random.fold_in(jax.random.fold_in(streams_of[5], part), 71), part),
    }


def block_valid(block_ids, lengths):
    per_passage = L // BLK
    passage = block_ids // per_passage
    within = block_ids % per_passage
    positions = within[..., None] * BLK + jnp.arange(BLK, dtype=jnp.int32)
    return positions < lengths[passage][..., None]

def soft_max_sim(sim_tile, valid_mask):
    masked = jnp.where(valid_mask, sim_tile, jnp.float32(-1e+30))
    peak = lax.optimization_barrier(jnp.max(masked, -1, keepdims=True))
    shifted = jnp.exp(masked - peak)
    running = lax.optimization_barrier(jnp.sum(shifted, -1, keepdims=True))
    scores = lax.optimization_barrier(jnp.mean(peak[..., 0] + jnp.log(running[..., 0]), -1))
    weights = (shifted / running).astype(jnp.bfloat16)
    return (scores, weights)

def loss_terms(scores):
    margins = scores[:, 1:] - scores[:, :1]
    losses = lax.optimization_barrier(jnp.mean(jax.nn.softplus(margins), 1))
    slopes = jax.nn.sigmoid(margins) / (scores.shape[1] - 1)
    d_score = jnp.concatenate([-lax.optimization_barrier(jnp.sum(slopes, 1, keepdims=True)), slopes], 1)
    return (losses, d_score)

def reference(hidden, proj_w, queries, lengths, candidates):
    e_pre = jnp.dot(hidden, proj_w, preferred_element_type=jnp.float32)
    scale = lax.rsqrt(lax.optimization_barrier(jnp.sum(e_pre * e_pre, -1, keepdims=True)) + 1e-06)
    embedded = (e_pre * scale).astype(jnp.bfloat16).reshape(NB, BLK, E)

    def per_group(carry, inputs):
        query_blk, cand_blk = inputs
        tiles = embedded[cand_blk]
        valid_mask = block_valid(cand_blk, lengths)
        sim_tile = jnp.einsum('qie,qcje->qcij', query_blk.astype(jnp.float32), tiles.astype(jnp.float32))
        scores, weights = soft_max_sim(sim_tile, valid_mask[:, :, None, :])
        losses, d_score = loss_terms(scores)
        occ_grad = jnp.einsum('qcij,qie->qcje', weights.astype(jnp.float32), query_blk.astype(jnp.float32))
        occ_grad = (occ_grad * (d_score / QLEN)[:, :, None, None]).astype(jnp.bfloat16)
        carry = carry.at[cand_blk.reshape(-1)].add(occ_grad.reshape(-1, BLK, E).astype(jnp.float32))
        return (carry, losses)
    grad_emb, losses = lax.scan(per_group, jnp.zeros((NB, BLK, E), jnp.float32), (queries.reshape(OWNERS, QRY_DEV, QLEN, E), candidates.reshape(OWNERS, QRY_DEV, CAND)))
    grad_emb = grad_emb.reshape(TOKENS, E)
    dot_e = lax.optimization_barrier(jnp.sum(e_pre * grad_emb, -1, keepdims=True))
    de_pre = (scale * grad_emb - e_pre * (scale * scale * scale) * dot_e).astype(jnp.bfloat16)
    grad_w = jnp.dot(hidden.T, de_pre, preferred_element_type=jnp.float32)
    return (losses.reshape(Q), grad_w)
```

```python
import jax
import jax.numpy as jnp
from jax import lax
from jax.sharding import PartitionSpec as P

L = 256
BLK = 64


def block_valid(block_ids, lengths):
    per_passage = L // BLK
    passage = block_ids // per_passage
    within = block_ids % per_passage
    positions = within[..., None] * BLK + jnp.arange(BLK, dtype=jnp.int32)
    return positions < lengths[passage][..., None]


def soft_max_sim(sim_tile, valid_mask):
    masked = jnp.where(valid_mask, sim_tile, jnp.float32(-1e30))
    peak = jnp.max(masked, -1, keepdims=True)
    shifted = jnp.exp(masked - peak)
    running = jnp.sum(shifted, -1, keepdims=True)
    scores = jnp.mean(peak[..., 0] + jnp.log(running[..., 0]), -1)
    weights = (shifted / running).astype(jnp.bfloat16)
    return (scores, weights)


def loss_terms(scores):
    margins = scores[:, 1:] - scores[:, :1]
    losses = jnp.mean(jax.nn.softplus(margins), 1)
    slopes = jax.nn.sigmoid(margins) / (scores.shape[1] - 1)
    d_score = jnp.concatenate([-jnp.sum(slopes, 1, keepdims=True), slopes], 1)
    return (losses, d_score)


def left_product(left, right):
    return lax.dot_general(
        left, right, (((0,), (0,)), ((), ())), preferred_element_type=jnp.float32
    )


def local(hidden, proj_w, queries, lengths, candidates):
    mp_count = lax.axis_size("mp")
    owners = lax.axis_size("enc") * mp_count
    row_share = hidden.shape[0] // mp_count
    emb_width = proj_w.shape[1]
    qry_dev = queries.shape[0]
    query_len = queries.shape[1]
    cand_count = candidates.shape[1]
    blk_dev = row_share // BLK
    slot_count = qry_dev * cand_count
    capacity = 2 * slot_count // owners
    me = lax.axis_index("enc") * mp_count + lax.axis_index("mp")

    all_queries = lax.all_gather(queries, ("enc", "mp"), axis=0, tiled=True)
    all_cand = lax.all_gather(candidates, ("enc", "mp"), axis=0, tiled=True)
    all_cand = all_cand.reshape(owners, slot_count)

    e_pre = lax.psum_scatter(
        jnp.dot(hidden, proj_w, preferred_element_type=jnp.float32),
        "mp",
        scatter_dimension=0,
        tiled=True,
    )
    scale = lax.rsqrt(jnp.sum(e_pre * e_pre, -1, keepdims=True) + 1e-06)
    embedded = (e_pre * scale).astype(jnp.bfloat16)
    local_blocks = embedded.reshape(blk_dev, BLK, emb_width)

    slot_ids = jnp.arange(slot_count, dtype=jnp.int32)
    mine = (all_cand // blk_dev) == me
    rank = jnp.cumsum(mine.astype(jnp.int32), axis=1) - 1
    ranks = jnp.arange(capacity, dtype=jnp.int32)
    pick = mine[:, None, :] & (rank[:, None, :] == ranks[None, :, None])
    valid = jnp.any(pick, axis=2)
    slot_of = jnp.sum(jnp.where(pick, slot_ids[None, None, :], 0), axis=2).astype(jnp.int32)
    block_of = jnp.take_along_axis(all_cand, slot_of, axis=1)
    local_of = block_of % blk_dev
    query_of = jnp.arange(owners, dtype=jnp.int32)[:, None] * qry_dev + slot_of // cand_count

    tiles = local_blocks[local_of]
    q_e = all_queries[query_of]
    valid_mask = block_valid(block_of, lengths)
    sim_tile = jnp.einsum("scie,scje->scij", q_e, tiles, preferred_element_type=jnp.float32)
    scores, weights = soft_max_sim(sim_tile, valid_mask[:, :, None, :])

    placed = jnp.sum(jnp.where(pick, scores[:, :, None], jnp.float32(0)), axis=1)
    all_scores = lax.psum(placed, ("enc", "mp")).reshape(owners * qry_dev, cand_count)
    all_losses, d_score = loss_terms(all_scores)
    losses = lax.dynamic_slice_in_dim(all_losses, me * qry_dev, qry_dev)

    d_e = jnp.take_along_axis(d_score.reshape(owners, slot_count), slot_of, axis=1)
    d_e = jnp.where(valid, d_e, jnp.float32(0))
    occ_grad = jnp.einsum("scij,scie->scje", weights, q_e, preferred_element_type=jnp.float32)
    occ_grad = (occ_grad * (d_e / query_len)[:, :, None, None]).astype(jnp.bfloat16)
    onehot = (local_of[:, :, None] == jnp.arange(blk_dev, dtype=jnp.int32)) & valid[:, :, None]
    grad_emb = jnp.einsum(
        "scb,scx->bx",
        onehot.astype(jnp.bfloat16),
        occ_grad.reshape(owners, capacity, BLK * emb_width),
        preferred_element_type=jnp.float32,
    )
    grad_flat = grad_emb.reshape(row_share, emb_width)
    dot_e = jnp.sum(e_pre * grad_flat, -1, keepdims=True)
    de_pre = (scale * grad_flat - e_pre * (scale * scale * scale) * dot_e).astype(jnp.bfloat16)
    partial_w = left_product(hidden, lax.all_gather(de_pre, "mp", axis=0, tiled=True))
    grad_w = lax.psum(partial_w, "enc")
    return (losses, grad_w)


def solution(mesh):
    return jax.shard_map(
        local,
        mesh=mesh,
        in_specs=(
            P(("groups", "enc"), "mp"),
            P("mp", None),
            P(("groups", "enc", "mp"), None, None),
            P("groups"),
            P(("groups", "enc", "mp"), None),
        ),
        out_specs=(P(("groups", "enc", "mp")), P(("groups", "mp"), None)),
        check_vma=False,
    )
```

```python
import jax
import jax.numpy as jnp
from jax import lax
from jax.sharding import PartitionSpec as P

L = 256
BLK = 64


def block_valid(block_ids, lengths):
    per_passage = L // BLK
    passage = block_ids // per_passage
    within = block_ids % per_passage
    positions = within[..., None] * BLK + jnp.arange(BLK, dtype=jnp.int32)
    return positions < lengths[passage][..., None]


def soft_max_sim(sim_tile, valid_mask):
    masked = jnp.where(valid_mask, sim_tile, jnp.float32(-1e30))
    peak = jnp.max(masked, -1, keepdims=True)
    shifted = jnp.exp(masked - peak)
    running = jnp.sum(shifted, -1, keepdims=True)
    scores = jnp.mean(peak[..., 0] + jnp.log(running[..., 0]), -1)
    weights = (shifted / running).astype(jnp.bfloat16)
    return (scores, weights)


def loss_terms(scores):
    margins = scores[:, 1:] - scores[:, :1]
    losses = jnp.mean(jax.nn.softplus(margins), 1)
    slopes = jax.nn.sigmoid(margins) / (scores.shape[1] - 1)
    d_score = jnp.concatenate([-jnp.sum(slopes, 1, keepdims=True), slopes], 1)
    return (losses, d_score)


def left_product(left, right):
    return lax.dot_general(
        left, right, (((0,), (0,)), ((), ())), preferred_element_type=jnp.float32
    )


def xor_perm(value, axis, bit):
    count = lax.axis_size(axis)
    return lax.ppermute(value, axis, [(i, i ^ bit) for i in range(count)])


def is_pow2(count):
    return count & (count - 1) == 0


def reduce_scatter_rows(value, axis):
    count = lax.axis_size(axis)
    if not is_pow2(count):
        return lax.psum_scatter(value, axis, scatter_dimension=0, tiled=True)
    me = lax.axis_index(axis)
    acc = value.reshape((count, -1) + value.shape[1:])
    bit = 1
    while bit < count:
        acc = acc.reshape((acc.shape[0] // 2, 2) + acc.shape[1:])
        low = (me // bit) % 2 == 0
        keep = jnp.where(low, acc[:, 0], acc[:, 1])
        send = jnp.where(low, acc[:, 1], acc[:, 0])
        acc = keep + xor_perm(send, axis, bit)
        bit *= 2
    return acc.reshape((-1,) + value.shape[1:])


def all_gather_rows(value, axis):
    count = lax.axis_size(axis)
    if not is_pow2(count):
        return lax.all_gather(value, axis, axis=0, tiled=True)
    me = lax.axis_index(axis)
    arr = value[None]
    bit = count // 2
    while bit >= 1:
        low = (me // bit) % 2 == 0
        other = xor_perm(arr, axis, bit)
        first = jnp.where(low, arr, other)
        second = jnp.where(low, other, arr)
        arr = jnp.stack([first, second], axis=1).reshape((-1,) + value.shape)
        bit //= 2
    return arr.reshape((-1,) + value.shape[1:])


def all_sum(value, axis):
    count = lax.axis_size(axis)
    if not is_pow2(count):
        return lax.psum(value, axis)
    bit = 1
    while bit < count:
        value = value + xor_perm(value, axis, bit)
        bit *= 2
    return value


def local(hidden, proj_w, queries, lengths, candidates):
    mp_count = lax.axis_size("mp")
    owners = lax.axis_size("enc") * mp_count
    row_share = hidden.shape[0] // mp_count
    emb_width = proj_w.shape[1]
    qry_dev = queries.shape[0]
    query_len = queries.shape[1]
    cand_count = candidates.shape[1]
    blk_dev = row_share // BLK
    slot_count = qry_dev * cand_count
    capacity = 2 * slot_count // owners
    me = lax.axis_index("enc") * mp_count + lax.axis_index("mp")

    all_queries = lax.all_gather(queries, ("enc", "mp"), axis=0, tiled=True)
    all_cand = lax.all_gather(candidates, ("enc", "mp"), axis=0, tiled=True)
    all_cand = all_cand.reshape(owners, slot_count)

    e_pre = reduce_scatter_rows(
        jnp.dot(hidden, proj_w, preferred_element_type=jnp.float32), "mp"
    )
    scale = lax.rsqrt(jnp.sum(e_pre * e_pre, -1, keepdims=True) + 1e-06)
    embedded = (e_pre * scale).astype(jnp.bfloat16)
    local_blocks = embedded.reshape(blk_dev, BLK, emb_width)

    slot_ids = jnp.arange(slot_count, dtype=jnp.int32)
    mine = (all_cand // blk_dev) == me
    rank = jnp.cumsum(mine.astype(jnp.int32), axis=1) - 1
    ranks = jnp.arange(capacity, dtype=jnp.int32)
    pick = mine[:, None, :] & (rank[:, None, :] == ranks[None, :, None])
    valid = jnp.any(pick, axis=2)
    slot_of = jnp.sum(jnp.where(pick, slot_ids[None, None, :], 0), axis=2).astype(jnp.int32)
    block_of = jnp.take_along_axis(all_cand, slot_of, axis=1)
    local_of = block_of % blk_dev
    query_of = jnp.arange(owners, dtype=jnp.int32)[:, None] * qry_dev + slot_of // cand_count

    tiles = local_blocks[local_of]
    q_e = all_queries[query_of]
    valid_mask = block_valid(block_of, lengths)
    sim_tile = jnp.einsum("scie,scje->scij", q_e, tiles, preferred_element_type=jnp.float32)
    scores, weights = soft_max_sim(sim_tile, valid_mask[:, :, None, :])

    placed = jnp.sum(jnp.where(pick, scores[:, :, None], jnp.float32(0)), axis=1)
    all_scores = all_sum(lax.psum(placed, "mp"), "enc").reshape(owners * qry_dev, cand_count)
    all_losses, d_score = loss_terms(all_scores)
    losses = lax.dynamic_slice_in_dim(all_losses, me * qry_dev, qry_dev)

    d_e = jnp.take_along_axis(d_score.reshape(owners, slot_count), slot_of, axis=1)
    d_e = jnp.where(valid, d_e, jnp.float32(0))
    occ_grad = jnp.einsum("scij,scie->scje", weights, q_e, preferred_element_type=jnp.float32)
    occ_grad = (occ_grad * (d_e / query_len)[:, :, None, None]).astype(jnp.bfloat16)
    onehot = (local_of[:, :, None] == jnp.arange(blk_dev, dtype=jnp.int32)) & valid[:, :, None]
    grad_emb = jnp.einsum(
        "scb,scx->bx",
        onehot.astype(jnp.bfloat16),
        occ_grad.reshape(owners, capacity, BLK * emb_width),
        preferred_element_type=jnp.float32,
    )
    grad_flat = grad_emb.reshape(row_share, emb_width)
    dot_e = jnp.sum(e_pre * grad_flat, -1, keepdims=True)
    de_pre = (scale * grad_flat - e_pre * (scale * scale * scale) * dot_e).astype(jnp.bfloat16)
    partial_w = left_product(hidden, all_gather_rows(de_pre, "mp"))
    grad_w = all_sum(partial_w, "enc")
    return (losses, grad_w)


def solution(mesh):
    return jax.shard_map(
        local,
        mesh=mesh,
        in_specs=(
            P(("groups", "enc"), "mp"),
            P("mp", None),
            P(("groups", "enc", "mp"), None, None),
            P("groups"),
            P(("groups", "enc", "mp"), None),
        ),
        out_specs=(P(("groups", "enc", "mp")), P(("groups", "mp"), None)),
        check_vma=False,
    )
```

```python
import jax
import jax.numpy as jnp
from jax import lax
from jax.sharding import PartitionSpec as P

L = 256
BLK = 64


def block_valid(block_ids, lengths):
    per_passage = L // BLK
    passage = block_ids // per_passage
    within = block_ids % per_passage
    positions = within[..., None] * BLK + jnp.arange(BLK, dtype=jnp.int32)
    return positions < lengths[passage][..., None]


def soft_max_sim(sim_tile, valid_mask):
    masked = jnp.where(valid_mask, sim_tile, jnp.float32(-1e30))
    peak = jnp.max(masked, -1, keepdims=True)
    shifted = jnp.exp(masked - peak)
    running = jnp.sum(shifted, -1, keepdims=True)
    scores = jnp.mean(peak[..., 0] + jnp.log(running[..., 0]), -1)
    weights = (shifted / running).astype(jnp.bfloat16)
    return (scores, weights)


def loss_terms(scores):
    margins = scores[:, 1:] - scores[:, :1]
    losses = jnp.mean(jax.nn.softplus(margins), 1)
    slopes = jax.nn.sigmoid(margins) / (scores.shape[1] - 1)
    d_score = jnp.concatenate([-jnp.sum(slopes, 1, keepdims=True), slopes], 1)
    return (losses, d_score)


def left_product(left, right):
    return lax.dot_general(
        left, right, (((0,), (0,)), ((), ())), preferred_element_type=jnp.float32
    )


def xor_perm(value, axis, bit):
    count = lax.axis_size(axis)
    return lax.ppermute(value, axis, [(i, i ^ bit) for i in range(count)])


def is_pow2(count):
    return count & (count - 1) == 0


def reduce_scatter_rows(value, axis):
    count = lax.axis_size(axis)
    if not is_pow2(count):
        return lax.psum_scatter(value, axis, scatter_dimension=0, tiled=True)
    me = lax.axis_index(axis)
    acc = value.reshape((count, -1) + value.shape[1:])
    bit = 1
    while bit < count:
        acc = acc.reshape((acc.shape[0] // 2, 2) + acc.shape[1:])
        low = (me // bit) % 2 == 0
        keep = jnp.where(low, acc[:, 0], acc[:, 1])
        send = jnp.where(low, acc[:, 1], acc[:, 0])
        acc = keep + xor_perm(send, axis, bit)
        bit *= 2
    return acc.reshape((-1,) + value.shape[1:])


def all_gather_rows(value, axis):
    count = lax.axis_size(axis)
    if not is_pow2(count):
        return lax.all_gather(value, axis, axis=0, tiled=True)
    me = lax.axis_index(axis)
    arr = value[None]
    bit = count // 2
    while bit >= 1:
        low = (me // bit) % 2 == 0
        other = xor_perm(arr, axis, bit)
        first = jnp.where(low, arr, other)
        second = jnp.where(low, other, arr)
        arr = jnp.stack([first, second], axis=1).reshape((-1,) + value.shape)
        bit //= 2
    return arr.reshape((-1,) + value.shape[1:])


def all_sum(value, axis):
    count = lax.axis_size(axis)
    if not is_pow2(count):
        return lax.psum(value, axis)
    bit = 1
    while bit < count:
        value = value + xor_perm(value, axis, bit)
        bit *= 2
    return value


def local(hidden, proj_w, queries, lengths, candidates):
    mp_count = lax.axis_size("mp")
    owners = lax.axis_size("enc") * mp_count
    row_share = hidden.shape[0] // mp_count
    emb_width = proj_w.shape[1]
    qry_dev = queries.shape[0]
    query_len = queries.shape[1]
    cand_count = candidates.shape[1]
    blk_dev = row_share // BLK
    slot_count = qry_dev * cand_count
    capacity = 2 * slot_count // owners
    me = lax.axis_index("enc") * mp_count + lax.axis_index("mp")

    all_queries = lax.all_gather(queries, ("enc", "mp"), axis=0, tiled=True)
    all_cand = lax.all_gather(candidates, ("enc", "mp"), axis=0, tiled=True)
    all_cand = all_cand.reshape(owners, slot_count)

    e_pre = reduce_scatter_rows(
        jnp.dot(hidden, proj_w, preferred_element_type=jnp.float32), "mp"
    )
    scale = lax.rsqrt(jnp.sum(e_pre * e_pre, -1, keepdims=True) + 1e-06)
    embedded = (e_pre * scale).astype(jnp.bfloat16)
    local_blocks = embedded.reshape(blk_dev, BLK, emb_width)

    slot_ids = jnp.arange(slot_count, dtype=jnp.int32)
    mine = (all_cand // blk_dev) == me
    rank = jnp.cumsum(mine.astype(jnp.int32), axis=1) - 1
    ranks = jnp.arange(capacity, dtype=jnp.int32)
    pick = mine[:, None, :] & (rank[:, None, :] == ranks[None, :, None])
    valid = jnp.any(pick, axis=2)
    slot_of = jnp.sum(jnp.where(pick, slot_ids[None, None, :], 0), axis=2).astype(jnp.int32)
    block_of = jnp.take_along_axis(all_cand, slot_of, axis=1)
    local_of = block_of % blk_dev
    query_of = jnp.arange(owners, dtype=jnp.int32)[:, None] * qry_dev + slot_of // cand_count

    tiles = local_blocks[local_of]
    q_e = all_queries[query_of]
    valid_mask = block_valid(block_of, lengths)
    sim_tile = jnp.einsum("scie,scje->scij", q_e, tiles, preferred_element_type=jnp.float32)
    scores, weights = soft_max_sim(sim_tile, valid_mask[:, :, None, :])

    occ_raw = jnp.einsum("scij,scie->scje", weights, q_e, preferred_element_type=jnp.float32)

    placed = jnp.sum(jnp.where(pick, scores[:, :, None], jnp.float32(0)), axis=1)
    all_scores = all_sum(lax.psum(placed, "mp"), "enc").reshape(owners * qry_dev, cand_count)
    all_losses, d_score = loss_terms(all_scores)
    losses = lax.dynamic_slice_in_dim(all_losses, me * qry_dev, qry_dev)

    d_e = jnp.take_along_axis(d_score.reshape(owners, slot_count), slot_of, axis=1)
    d_e = jnp.where(valid, d_e, jnp.float32(0))
    occ_grad = (occ_raw * (d_e / query_len)[:, :, None, None]).astype(jnp.bfloat16)
    onehot = (local_of[:, :, None] == jnp.arange(blk_dev, dtype=jnp.int32)) & valid[:, :, None]
    grad_emb = jnp.einsum(
        "scb,scje->bje",
        onehot.astype(jnp.bfloat16),
        occ_grad,
        preferred_element_type=jnp.float32,
    )
    grad_flat = grad_emb.reshape(row_share, emb_width)
    dot_e = jnp.sum(e_pre * grad_flat, -1, keepdims=True)
    de_pre = (scale * grad_flat - e_pre * (scale * scale * scale) * dot_e).astype(jnp.bfloat16)
    partial_w = left_product(hidden, all_gather_rows(de_pre, "mp"))
    grad_w = all_sum(partial_w, "enc")
    return (losses, grad_w)


def solution(mesh):
    return jax.shard_map(
        local,
        mesh=mesh,
        in_specs=(
            P(("groups", "enc"), "mp"),
            P("mp", None),
            P(("groups", "enc", "mp"), None, None),
            P("groups"),
            P(("groups", "enc", "mp"), None),
        ),
        out_specs=(P(("groups", "enc", "mp")), P(("groups", "mp"), None)),
        check_vma=False,
    )
```

```python
import jax
import jax.numpy as jnp
from jax import lax
from jax.sharding import PartitionSpec as P

L = 256
BLK = 64


def block_valid(block_ids, lengths):
    per_passage = L // BLK
    passage = block_ids // per_passage
    within = block_ids % per_passage
    positions = within[..., None] * BLK + jnp.arange(BLK, dtype=jnp.int32)
    return positions < lengths[passage][..., None]


def soft_max_sim(sim_tile, valid_mask):
    masked = jnp.where(valid_mask, sim_tile, jnp.float32(-1e30))
    peak = jnp.max(masked, -1, keepdims=True)
    shifted = jnp.exp(masked - peak)
    running = jnp.sum(shifted, -1, keepdims=True)
    scores = jnp.mean(peak[..., 0] + jnp.log(running[..., 0]), -1)
    weights = (shifted / running).astype(jnp.bfloat16)
    return (scores, weights)


def loss_terms(scores):
    margins = scores[:, 1:] - scores[:, :1]
    losses = jnp.mean(jax.nn.softplus(margins), 1)
    slopes = jax.nn.sigmoid(margins) / (scores.shape[1] - 1)
    d_score = jnp.concatenate([-jnp.sum(slopes, 1, keepdims=True), slopes], 1)
    return (losses, d_score)


def left_product(left, right):
    return lax.dot_general(
        left, right, (((0,), (0,)), ((), ())), preferred_element_type=jnp.float32
    )


def xor_perm(value, axis, bit):
    count = lax.axis_size(axis)
    return lax.ppermute(value, axis, [(i, i ^ bit) for i in range(count)])


def is_pow2(count):
    return count & (count - 1) == 0


def reduce_scatter_rows(value, axis):
    count = lax.axis_size(axis)
    if not is_pow2(count):
        return lax.psum_scatter(value, axis, scatter_dimension=0, tiled=True)
    me = lax.axis_index(axis)
    acc = value.reshape((count, -1) + value.shape[1:])
    bit = 1
    while bit < count:
        acc = acc.reshape((acc.shape[0] // 2, 2) + acc.shape[1:])
        low = (me // bit) % 2 == 0
        keep = jnp.where(low, acc[:, 0], acc[:, 1])
        send = jnp.where(low, acc[:, 1], acc[:, 0])
        acc = keep + xor_perm(send, axis, bit)
        bit *= 2
    return acc.reshape((-1,) + value.shape[1:])


def all_gather_rows(value, axis):
    count = lax.axis_size(axis)
    if not is_pow2(count):
        return lax.all_gather(value, axis, axis=0, tiled=True)
    me = lax.axis_index(axis)
    arr = value[None]
    bit = count // 2
    while bit >= 1:
        low = (me // bit) % 2 == 0
        other = xor_perm(arr, axis, bit)
        first = jnp.where(low, arr, other)
        second = jnp.where(low, other, arr)
        arr = jnp.stack([first, second], axis=1).reshape((-1,) + value.shape)
        bit //= 2
    return arr.reshape((-1,) + value.shape[1:])


def all_sum(value, axis):
    count = lax.axis_size(axis)
    if not is_pow2(count):
        return lax.psum(value, axis)
    bit = 1
    while bit < count:
        value = value + xor_perm(value, axis, bit)
        bit *= 2
    return value


def local(hidden, proj_w, queries, lengths, candidates):
    mp_count = lax.axis_size("mp")
    owners = lax.axis_size("enc") * mp_count
    row_share = hidden.shape[0] // mp_count
    emb_width = proj_w.shape[1]
    qry_dev = queries.shape[0]
    query_len = queries.shape[1]
    cand_count = candidates.shape[1]
    blk_dev = row_share // BLK
    slot_count = qry_dev * cand_count
    capacity = 2 * slot_count // owners
    me = lax.axis_index("enc") * mp_count + lax.axis_index("mp")

    all_queries = all_gather_rows(all_gather_rows(queries, "mp"), "enc")
    all_cand = all_gather_rows(all_gather_rows(candidates, "mp"), "enc")
    all_cand = all_cand.reshape(owners, slot_count)

    chunks = 4 if row_share % (4 * BLK) == 0 else 1
    split_rows = hidden.reshape(mp_count, chunks, row_share // chunks, hidden.shape[1])
    e_pre = jnp.stack(
        [
            reduce_scatter_rows(
                jnp.dot(split_rows[:, k], proj_w, preferred_element_type=jnp.float32).reshape(
                    mp_count * (row_share // chunks), emb_width
                ),
                "mp",
            )
            for k in range(chunks)
        ]
    ).reshape(row_share, emb_width)
    scale = lax.rsqrt(jnp.sum(e_pre * e_pre, -1, keepdims=True) + 1e-06)
    embedded = (e_pre * scale).astype(jnp.bfloat16)
    local_blocks = embedded.reshape(blk_dev, BLK, emb_width)

    slot_ids = jnp.arange(slot_count, dtype=jnp.int32)
    mine = (all_cand // blk_dev) == me
    rank = jnp.cumsum(mine.astype(jnp.int32), axis=1) - 1
    ranks = jnp.arange(capacity, dtype=jnp.int32)
    pick = mine[:, None, :] & (rank[:, None, :] == ranks[None, :, None])
    valid = jnp.any(pick, axis=2)
    slot_of = jnp.sum(jnp.where(pick, slot_ids[None, None, :], 0), axis=2).astype(jnp.int32)
    block_of = jnp.take_along_axis(all_cand, slot_of, axis=1)
    local_of = block_of % blk_dev
    query_of = jnp.arange(owners, dtype=jnp.int32)[:, None] * qry_dev + slot_of // cand_count

    tiles = local_blocks[local_of]
    q_e = all_queries[query_of]
    valid_mask = block_valid(block_of, lengths)
    sim_tile = jnp.einsum("scie,scje->scij", q_e, tiles, preferred_element_type=jnp.float32)
    scores, weights = soft_max_sim(sim_tile, valid_mask[:, :, None, :])

    occ_raw = jnp.einsum("scij,scie->scje", weights, q_e, preferred_element_type=jnp.float32)

    placed = jnp.sum(jnp.where(pick, scores[:, :, None], jnp.float32(0)), axis=1)
    all_scores = all_sum(lax.psum(placed, "mp"), "enc").reshape(owners * qry_dev, cand_count)
    all_losses, d_score = loss_terms(all_scores)
    losses = lax.dynamic_slice_in_dim(all_losses, me * qry_dev, qry_dev)

    d_e = jnp.take_along_axis(d_score.reshape(owners, slot_count), slot_of, axis=1)
    d_e = jnp.where(valid, d_e, jnp.float32(0))
    occ_grad = (occ_raw * (d_e / query_len)[:, :, None, None]).astype(jnp.bfloat16)
    onehot = (local_of[:, :, None] == jnp.arange(blk_dev, dtype=jnp.int32)) & valid[:, :, None]
    grad_emb = jnp.einsum(
        "scb,scje->bje",
        onehot.astype(jnp.bfloat16),
        occ_grad,
        preferred_element_type=jnp.float32,
    )
    grad_flat = grad_emb.reshape(row_share, emb_width)
    dot_e = jnp.sum(e_pre * grad_flat, -1, keepdims=True)
    de_pre = (scale * grad_flat - e_pre * (scale * scale * scale) * dot_e).astype(jnp.bfloat16)
    partial_w = left_product(hidden, all_gather_rows(de_pre, "mp"))
    grad_w = all_sum(partial_w, "enc")
    return (losses, grad_w)


def solution(mesh):
    return jax.shard_map(
        local,
        mesh=mesh,
        in_specs=(
            P(("groups", "enc"), "mp"),
            P("mp", None),
            P(("groups", "enc", "mp"), None, None),
            P("groups"),
            P(("groups", "enc", "mp"), None),
        ),
        out_specs=(P(("groups", "enc", "mp")), P(("groups", "mp"), None)),
        check_vma=False,
    )
```

```python
import jax
import jax.numpy as jnp
from jax import lax
from jax.sharding import PartitionSpec as P

L = 256
BLK = 64


def block_valid(block_ids, lengths):
    per_passage = L // BLK
    passage = block_ids // per_passage
    within = block_ids % per_passage
    positions = within[..., None] * BLK + jnp.arange(BLK, dtype=jnp.int32)
    return positions < lengths[passage][..., None]


def soft_max_sim(sim_tile, valid_mask):
    masked = jnp.where(valid_mask, sim_tile, jnp.float32(-1e30))
    peak = jnp.max(masked, -1, keepdims=True)
    shifted = jnp.exp(masked - peak)
    running = jnp.sum(shifted, -1, keepdims=True)
    scores = jnp.mean(peak[..., 0] + jnp.log(running[..., 0]), -1)
    weights = (shifted / running).astype(jnp.bfloat16)
    return (scores, weights)


def loss_terms(scores):
    margins = scores[:, 1:] - scores[:, :1]
    losses = jnp.mean(jax.nn.softplus(margins), 1)
    slopes = jax.nn.sigmoid(margins) / (scores.shape[1] - 1)
    d_score = jnp.concatenate([-jnp.sum(slopes, 1, keepdims=True), slopes], 1)
    return (losses, d_score)


def left_product(left, right):
    return lax.dot_general(
        left, right, (((0,), (0,)), ((), ())), preferred_element_type=jnp.float32
    )


def xor_perm(value, axis, bit):
    count = lax.axis_size(axis)
    return lax.ppermute(value, axis, [(i, i ^ bit) for i in range(count)])


def is_pow2(count):
    return count & (count - 1) == 0


def halving_steps(values, axis):
    count = lax.axis_size(axis)
    me = lax.axis_index(axis)
    accs = [v.reshape((count, -1) + v.shape[1:]) for v in values]
    bit = 1
    while True:
        keeps, sends = [], []
        for acc in accs:
            acc = acc.reshape((acc.shape[0] // 2, 2) + acc.shape[1:])
            low = (me // bit) % 2 == 0
            keeps.append(jnp.where(low, acc[:, 0], acc[:, 1]))
            sends.append(jnp.where(low, acc[:, 1], acc[:, 0]))
        if bit * 2 >= count:
            return keeps, sends, bit
        accs = [k + xor_perm(t, axis, bit) for k, t in zip(keeps, sends)]
        bit *= 2


def all_gather_rows(value, axis):
    count = lax.axis_size(axis)
    if not is_pow2(count):
        return lax.all_gather(value, axis, axis=0, tiled=True)
    me = lax.axis_index(axis)
    arr = value[None]
    bit = count // 2
    while bit >= 1:
        low = (me // bit) % 2 == 0
        other = xor_perm(arr, axis, bit)
        first = jnp.where(low, arr, other)
        second = jnp.where(low, other, arr)
        arr = jnp.stack([first, second], axis=1).reshape((-1,) + value.shape)
        bit //= 2
    return arr.reshape((-1,) + value.shape[1:])


def all_sum(value, axis):
    count = lax.axis_size(axis)
    if not is_pow2(count):
        return lax.psum(value, axis)
    bit = 1
    while bit < count:
        value = value + xor_perm(value, axis, bit)
        bit *= 2
    return value


def local(hidden, proj_w, queries, lengths, candidates):
    mp_count = lax.axis_size("mp")
    owners = lax.axis_size("enc") * mp_count
    row_share = hidden.shape[0] // mp_count
    emb_width = proj_w.shape[1]
    qry_dev = queries.shape[0]
    query_len = queries.shape[1]
    cand_count = candidates.shape[1]
    blk_dev = row_share // BLK
    slot_count = qry_dev * cand_count
    capacity = 2 * slot_count // owners
    me = lax.axis_index("enc") * mp_count + lax.axis_index("mp")

    chunks = 4 if row_share % (4 * BLK) == 0 else 1
    split_rows = hidden.reshape(mp_count, chunks, row_share // chunks, hidden.shape[1])
    partials = [
        jnp.dot(split_rows[:, k], proj_w, preferred_element_type=jnp.float32).reshape(
            mp_count * (row_share // chunks), emb_width
        )
        for k in range(chunks)
    ]
    if is_pow2(mp_count) and mp_count > 1:
        keeps, sends, bit = halving_steps(partials, "mp")
        last, queries, candidates = lax.optimization_barrier((sends[-1], queries, candidates))
        sends = sends[:-1] + [last]
        pieces = [k + xor_perm(t, "mp", bit) for k, t in zip(keeps, sends)]
        pieces = [p.reshape(-1, emb_width) for p in pieces]
    else:
        pieces = [
            lax.psum_scatter(p, "mp", scatter_dimension=0, tiled=True) for p in partials
        ]
    e_pre = jnp.stack(pieces).reshape(row_share, emb_width)

    packed = jnp.concatenate(
        [
            queries.reshape(qry_dev, query_len * emb_width).astype(jnp.float32),
            candidates.astype(jnp.float32),
        ],
        axis=1,
    )
    packed = lax.all_gather(packed, ("enc", "mp"), axis=0, tiled=True)
    all_queries = (
        packed[:, : query_len * emb_width]
        .astype(jnp.bfloat16)
        .reshape(owners * qry_dev, query_len, emb_width)
    )
    all_cand = packed[:, query_len * emb_width :].astype(jnp.int32)
    all_cand = all_cand.reshape(owners, slot_count)

    scale = lax.rsqrt(jnp.sum(e_pre * e_pre, -1, keepdims=True) + 1e-06)
    embedded = (e_pre * scale).astype(jnp.bfloat16)
    local_blocks = embedded.reshape(blk_dev, BLK, emb_width)

    slot_ids = jnp.arange(slot_count, dtype=jnp.int32)
    mine = (all_cand // blk_dev) == me
    rank = jnp.cumsum(mine.astype(jnp.int32), axis=1) - 1
    ranks = jnp.arange(capacity, dtype=jnp.int32)
    pick = mine[:, None, :] & (rank[:, None, :] == ranks[None, :, None])
    valid = jnp.any(pick, axis=2)
    slot_of = jnp.sum(jnp.where(pick, slot_ids[None, None, :], 0), axis=2).astype(jnp.int32)
    block_of = jnp.take_along_axis(all_cand, slot_of, axis=1)
    local_of = block_of % blk_dev
    query_of = jnp.arange(owners, dtype=jnp.int32)[:, None] * qry_dev + slot_of // cand_count

    tiles = local_blocks[local_of]
    q_e = all_queries[query_of]
    valid_mask = block_valid(block_of, lengths)
    sim_tile = jnp.einsum("scie,scje->scij", q_e, tiles, preferred_element_type=jnp.float32)
    scores, weights = soft_max_sim(sim_tile, valid_mask[:, :, None, :])

    occ_raw = jnp.einsum("scij,scie->scje", weights, q_e, preferred_element_type=jnp.float32)

    placed = jnp.sum(jnp.where(pick, scores[:, :, None], jnp.float32(0)), axis=1)
    all_scores = all_sum(lax.psum(placed, "mp"), "enc").reshape(owners * qry_dev, cand_count)
    all_losses, d_score = loss_terms(all_scores)
    losses = lax.dynamic_slice_in_dim(all_losses, me * qry_dev, qry_dev)

    d_e = jnp.take_along_axis(d_score.reshape(owners, slot_count), slot_of, axis=1)
    d_e = jnp.where(valid, d_e, jnp.float32(0))
    occ_grad = (occ_raw * (d_e / query_len)[:, :, None, None]).astype(jnp.bfloat16)
    onehot = (local_of[:, :, None] == jnp.arange(blk_dev, dtype=jnp.int32)) & valid[:, :, None]
    grad_emb = jnp.einsum(
        "scb,scje->bje",
        onehot.astype(jnp.bfloat16),
        occ_grad,
        preferred_element_type=jnp.float32,
    )
    grad_flat = grad_emb.reshape(row_share, emb_width)
    dot_e = jnp.sum(e_pre * grad_flat, -1, keepdims=True)
    de_pre = (scale * grad_flat - e_pre * (scale * scale * scale) * dot_e).astype(jnp.bfloat16)
    partial_w = left_product(hidden, all_gather_rows(de_pre, "mp"))
    grad_w = all_sum(partial_w, "enc")
    return (losses, grad_w)


def solution(mesh):
    return jax.shard_map(
        local,
        mesh=mesh,
        in_specs=(
            P(("groups", "enc"), "mp"),
            P("mp", None),
            P(("groups", "enc", "mp"), None, None),
            P("groups"),
            P(("groups", "enc", "mp"), None),
        ),
        out_specs=(P(("groups", "enc", "mp")), P(("groups", "mp"), None)),
        check_vma=False,
    )
```

```python
import jax
import jax.numpy as jnp
from jax import lax
from jax.sharding import PartitionSpec as P

L = 256
BLK = 64


def block_valid(block_ids, lengths):
    per_passage = L // BLK
    passage = block_ids // per_passage
    within = block_ids % per_passage
    positions = within[..., None] * BLK + jnp.arange(BLK, dtype=jnp.int32)
    return positions < lengths[passage][..., None]


def soft_max_sim(sim_tile, valid_mask):
    masked = jnp.where(valid_mask, sim_tile, jnp.float32(-1e30))
    peak = jnp.max(masked, -1, keepdims=True)
    shifted = jnp.exp(masked - peak)
    running = jnp.sum(shifted, -1, keepdims=True)
    scores = jnp.mean(peak[..., 0] + jnp.log(running[..., 0]), -1)
    weights = (shifted / running).astype(jnp.bfloat16)
    return (scores, weights)


def loss_terms(scores):
    margins = scores[:, 1:] - scores[:, :1]
    losses = jnp.mean(jax.nn.softplus(margins), 1)
    slopes = jax.nn.sigmoid(margins) / (scores.shape[1] - 1)
    d_score = jnp.concatenate([-jnp.sum(slopes, 1, keepdims=True), slopes], 1)
    return (losses, d_score)


def left_product(left, right):
    return lax.dot_general(
        left, right, (((0,), (0,)), ((), ())), preferred_element_type=jnp.float32
    )


def xor_perm(value, axis, bit):
    count = lax.axis_size(axis)
    return lax.ppermute(value, axis, [(i, i ^ bit) for i in range(count)])


def is_pow2(count):
    return count & (count - 1) == 0


def halving_steps(values, axis):
    count = lax.axis_size(axis)
    me = lax.axis_index(axis)
    accs = [v.reshape((count, -1) + v.shape[1:]) for v in values]
    bit = 1
    while True:
        keeps, sends = [], []
        for acc in accs:
            acc = acc.reshape((acc.shape[0] // 2, 2) + acc.shape[1:])
            low = (me // bit) % 2 == 0
            keeps.append(jnp.where(low, acc[:, 0], acc[:, 1]))
            sends.append(jnp.where(low, acc[:, 1], acc[:, 0]))
        if bit * 2 >= count:
            return keeps, sends, bit
        accs = [k + xor_perm(t, axis, bit) for k, t in zip(keeps, sends)]
        bit *= 2


def all_gather_rows(value, axis):
    count = lax.axis_size(axis)
    if not is_pow2(count):
        return lax.all_gather(value, axis, axis=0, tiled=True)
    me = lax.axis_index(axis)
    arr = value[None]
    bit = count // 2
    while bit >= 1:
        low = (me // bit) % 2 == 0
        other = xor_perm(arr, axis, bit)
        first = jnp.where(low, arr, other)
        second = jnp.where(low, other, arr)
        arr = jnp.stack([first, second], axis=1).reshape((-1,) + value.shape)
        bit //= 2
    return arr.reshape((-1,) + value.shape[1:])


def all_sum(value, axis):
    count = lax.axis_size(axis)
    if count > 4:
        if not is_pow2(count):
            return lax.psum(value, axis)
        bit = 1
        while bit < count:
            value = value + xor_perm(value, axis, bit)
            bit *= 2
        return value
    me = lax.axis_index(axis)
    got = [value] + [
        lax.ppermute(value, axis, [(i, (i + k) % count) for i in range(count)])
        for k in range(1, count)
    ]
    stacked = jnp.stack(got)
    by_source = [
        lax.dynamic_index_in_dim(stacked, (me - src) % count, 0, keepdims=False)
        for src in range(count)
    ]
    total = by_source[0]
    for part in by_source[1:]:
        total = total + part
    return total


def local(hidden, proj_w, queries, lengths, candidates):
    mp_count = lax.axis_size("mp")
    owners = lax.axis_size("enc") * mp_count
    row_share = hidden.shape[0] // mp_count
    emb_width = proj_w.shape[1]
    qry_dev = queries.shape[0]
    query_len = queries.shape[1]
    cand_count = candidates.shape[1]
    blk_dev = row_share // BLK
    slot_count = qry_dev * cand_count
    capacity = 2 * slot_count // owners
    me = lax.axis_index("enc") * mp_count + lax.axis_index("mp")
    all_cand = lax.all_gather(candidates, ("enc", "mp"), axis=0, tiled=True)
    all_cand = all_cand.reshape(owners, slot_count)

    chunks = 4 if row_share % (4 * BLK) == 0 else 1
    split_rows = hidden.reshape(mp_count, chunks, row_share // chunks, hidden.shape[1])
    partials = [
        jnp.dot(split_rows[:, k], proj_w, preferred_element_type=jnp.float32).reshape(
            mp_count * (row_share // chunks), emb_width
        )
        for k in range(chunks)
    ]
    if is_pow2(mp_count) and mp_count > 1:
        keeps, sends, bit = halving_steps(partials, "mp")
        last, queries = lax.optimization_barrier((sends[-1], queries))
        sends = sends[:-1] + [last]
        pieces = [k + xor_perm(t, "mp", bit) for k, t in zip(keeps, sends)]
        pieces = [p.reshape(-1, emb_width) for p in pieces]
    else:
        pieces = [
            lax.psum_scatter(p, "mp", scatter_dimension=0, tiled=True) for p in partials
        ]
    e_pre = jnp.stack(pieces).reshape(row_share, emb_width)

    packed = jnp.concatenate(
        [
            queries.reshape(qry_dev, query_len * emb_width).astype(jnp.float32),
            candidates.astype(jnp.float32),
        ],
        axis=1,
    )
    packed = lax.all_gather(packed, ("enc", "mp"), axis=0, tiled=True)
    all_queries = (
        packed[:, : query_len * emb_width]
        .astype(jnp.bfloat16)
        .reshape(owners * qry_dev, query_len, emb_width)
    )
    late_cand = packed[:, query_len * emb_width :].astype(jnp.int32).reshape(owners, slot_count)

    scale = lax.rsqrt(jnp.sum(e_pre * e_pre, -1, keepdims=True) + 1e-06)
    embedded = (e_pre * scale).astype(jnp.bfloat16)
    local_blocks = embedded.reshape(blk_dev, BLK, emb_width)

    slot_ids = jnp.arange(slot_count, dtype=jnp.int32)
    mine = (all_cand // blk_dev) == me
    rank = jnp.cumsum(mine.astype(jnp.int32), axis=1) - 1
    ranks = jnp.arange(capacity, dtype=jnp.int32)
    pick = mine[:, None, :] & (rank[:, None, :] == ranks[None, :, None])
    valid = jnp.any(pick, axis=2)
    slot_of = jnp.sum(jnp.where(pick, slot_ids[None, None, :], 0), axis=2).astype(jnp.int32)
    block_of = jnp.take_along_axis(all_cand, slot_of, axis=1)
    local_of = block_of % blk_dev
    query_of = jnp.arange(owners, dtype=jnp.int32)[:, None] * qry_dev + slot_of // cand_count

    tiles = local_blocks[local_of]
    q_e = all_queries[query_of]
    valid_mask = block_valid(block_of, lengths)
    sim_tile = jnp.einsum("scie,scje->scij", q_e, tiles, preferred_element_type=jnp.float32)
    scores, weights = soft_max_sim(sim_tile, valid_mask[:, :, None, :])

    occ_raw = jnp.einsum("scij,scie->scje", weights, q_e, preferred_element_type=jnp.float32)

    placed = jnp.sum(jnp.where(pick, scores[:, :, None], jnp.float32(0)), axis=1)
    all_scores = all_sum(lax.psum(placed, "mp"), "enc").reshape(owners * qry_dev, cand_count)
    all_losses, d_score = loss_terms(all_scores)
    losses = lax.dynamic_slice_in_dim(all_losses, me * qry_dev, qry_dev)

    d_e = jnp.take_along_axis(d_score.reshape(owners, slot_count), slot_of, axis=1)
    d_e = jnp.where(valid, d_e, jnp.float32(0))
    occ_grad = (occ_raw * (d_e / query_len)[:, :, None, None]).astype(jnp.bfloat16)
    late_local = jnp.take_along_axis(late_cand, slot_of, axis=1) % blk_dev
    onehot = (late_local[:, :, None] == jnp.arange(blk_dev, dtype=jnp.int32)) & valid[:, :, None]
    grad_emb = jnp.einsum(
        "scb,scje->bje",
        onehot.astype(jnp.bfloat16),
        occ_grad,
        preferred_element_type=jnp.float32,
    )
    grad_flat = grad_emb.reshape(row_share, emb_width)
    dot_e = jnp.sum(e_pre * grad_flat, -1, keepdims=True)
    de_pre = (scale * grad_flat - e_pre * (scale * scale * scale) * dot_e).astype(jnp.bfloat16)
    partial_w = left_product(hidden, all_gather_rows(de_pre, "mp"))
    grad_w = all_sum(partial_w, "enc")
    return (losses, grad_w)


def solution(mesh):
    return jax.shard_map(
        local,
        mesh=mesh,
        in_specs=(
            P(("groups", "enc"), "mp"),
            P("mp", None),
            P(("groups", "enc", "mp"), None, None),
            P("groups"),
            P(("groups", "enc", "mp"), None),
        ),
        out_specs=(P(("groups", "enc", "mp")), P(("groups", "mp"), None)),
        check_vma=False,
    )
```

```python
import jax
import jax.numpy as jnp
from jax import lax
from jax.sharding import PartitionSpec as P

L = 256
BLK = 64


def block_valid(block_ids, lengths):
    per_passage = L // BLK
    passage = block_ids // per_passage
    within = block_ids % per_passage
    positions = within[..., None] * BLK + jnp.arange(BLK, dtype=jnp.int32)
    return positions < lengths[passage][..., None]


def soft_max_sim(sim_tile, valid_mask):
    masked = jnp.where(valid_mask, sim_tile, jnp.float32(-1e30))
    peak = jnp.max(masked, -1, keepdims=True)
    shifted = jnp.exp(masked - peak)
    running = jnp.sum(shifted, -1, keepdims=True)
    scores = jnp.mean(peak[..., 0] + jnp.log(running[..., 0]), -1)
    weights = (shifted / running).astype(jnp.bfloat16)
    return (scores, weights)


def loss_terms(scores):
    margins = scores[:, 1:] - scores[:, :1]
    losses = jnp.mean(jax.nn.softplus(margins), 1)
    slopes = jax.nn.sigmoid(margins) / (scores.shape[1] - 1)
    d_score = jnp.concatenate([-jnp.sum(slopes, 1, keepdims=True), slopes], 1)
    return (losses, d_score)


def left_product(left, right):
    return lax.dot_general(
        left, right, (((0,), (0,)), ((), ())), preferred_element_type=jnp.float32
    )


def xor_perm(value, axis, bit):
    count = lax.axis_size(axis)
    return lax.ppermute(value, axis, [(i, i ^ bit) for i in range(count)])


def is_pow2(count):
    return count & (count - 1) == 0


def halving_steps(values, axis):
    count = lax.axis_size(axis)
    me = lax.axis_index(axis)
    accs = [v.reshape((count, -1) + v.shape[1:]) for v in values]
    bit = 1
    while True:
        keeps, sends = [], []
        for acc in accs:
            acc = acc.reshape((acc.shape[0] // 2, 2) + acc.shape[1:])
            low = (me // bit) % 2 == 0
            keeps.append(jnp.where(low, acc[:, 0], acc[:, 1]))
            sends.append(jnp.where(low, acc[:, 1], acc[:, 0]))
        if bit * 2 >= count:
            return keeps, sends, bit
        accs = [k + xor_perm(t, axis, bit) for k, t in zip(keeps, sends)]
        bit *= 2


def all_gather_rows(value, axis):
    count = lax.axis_size(axis)
    if not is_pow2(count):
        return lax.all_gather(value, axis, axis=0, tiled=True)
    me = lax.axis_index(axis)
    arr = value[None]
    bit = count // 2
    while bit >= 1:
        low = (me // bit) % 2 == 0
        other = xor_perm(arr, axis, bit)
        first = jnp.where(low, arr, other)
        second = jnp.where(low, other, arr)
        arr = jnp.stack([first, second], axis=1).reshape((-1,) + value.shape)
        bit //= 2
    return arr.reshape((-1,) + value.shape[1:])


def all_sum(value, axis):
    count = lax.axis_size(axis)
    if count > 4:
        if not is_pow2(count):
            return lax.psum(value, axis)
        bit = 1
        while bit < count:
            value = value + xor_perm(value, axis, bit)
            bit *= 2
        return value
    me = lax.axis_index(axis)
    got = [value] + [
        lax.ppermute(value, axis, [(i, (i + k) % count) for i in range(count)])
        for k in range(1, count)
    ]
    stacked = jnp.stack(got)
    by_source = [
        lax.dynamic_index_in_dim(stacked, (me - src) % count, 0, keepdims=False)
        for src in range(count)
    ]
    total = by_source[0]
    for part in by_source[1:]:
        total = total + part
    return total


def local(hidden, proj_w, queries, lengths, candidates):
    mp_count = lax.axis_size("mp")
    owners = lax.axis_size("enc") * mp_count
    row_share = hidden.shape[0] // mp_count
    emb_width = proj_w.shape[1]
    qry_dev = queries.shape[0]
    query_len = queries.shape[1]
    cand_count = candidates.shape[1]
    blk_dev = row_share // BLK
    slot_count = qry_dev * cand_count
    capacity = 2 * slot_count // owners
    me = lax.axis_index("enc") * mp_count + lax.axis_index("mp")

    packed = jnp.concatenate(
        [
            queries.reshape(qry_dev, query_len * emb_width).astype(jnp.float32),
            candidates.astype(jnp.float32),
        ],
        axis=1,
    )
    packed = all_gather_rows(packed, "mp")

    chunks = 4 if row_share % (4 * BLK) == 0 else 1
    split_rows = hidden.reshape(mp_count, chunks, row_share // chunks, hidden.shape[1])
    partials = [
        jnp.dot(split_rows[:, k], proj_w, preferred_element_type=jnp.float32).reshape(
            mp_count * (row_share // chunks), emb_width
        )
        for k in range(chunks)
    ]
    if is_pow2(mp_count) and mp_count > 1:
        keeps, sends, bit = halving_steps(partials, "mp")
        last, packed = lax.optimization_barrier((sends[-1], packed))
        sends = sends[:-1] + [last]
        pieces = [k + xor_perm(t, "mp", bit) for k, t in zip(keeps, sends)]
        pieces = [p.reshape(-1, emb_width) for p in pieces]
    else:
        pieces = [
            lax.psum_scatter(p, "mp", scatter_dimension=0, tiled=True) for p in partials
        ]
    e_pre = jnp.stack(pieces).reshape(row_share, emb_width)

    packed = all_gather_rows(packed, "enc")
    all_queries = (
        packed[:, : query_len * emb_width]
        .astype(jnp.bfloat16)
        .reshape(owners * qry_dev, query_len, emb_width)
    )
    all_cand = packed[:, query_len * emb_width :].astype(jnp.int32).reshape(owners, slot_count)

    slot_ids = jnp.arange(slot_count, dtype=jnp.int32)
    mine = (all_cand // blk_dev) == me
    rank = jnp.cumsum(mine.astype(jnp.int32), axis=1) - 1
    ranks = jnp.arange(capacity, dtype=jnp.int32)
    pick = mine[:, None, :] & (rank[:, None, :] == ranks[None, :, None])
    valid = jnp.any(pick, axis=2)
    slot_of = jnp.sum(jnp.where(pick, slot_ids[None, None, :], 0), axis=2).astype(jnp.int32)
    block_of = jnp.take_along_axis(all_cand, slot_of, axis=1)
    local_of = block_of % blk_dev
    query_of = jnp.arange(owners, dtype=jnp.int32)[:, None] * qry_dev + slot_of // cand_count

    q_e = all_queries[query_of]


    scale = lax.rsqrt(jnp.sum(e_pre * e_pre, -1, keepdims=True) + 1e-06)
    embedded = (e_pre * scale).astype(jnp.bfloat16)
    local_blocks = embedded.reshape(blk_dev, BLK, emb_width)

    tiles = local_blocks[local_of]
    valid_mask = block_valid(block_of, lengths)
    sim_tile = jnp.einsum("scie,scje->scij", q_e, tiles, preferred_element_type=jnp.float32)
    scores, weights = soft_max_sim(sim_tile, valid_mask[:, :, None, :])

    occ_raw = jnp.einsum("scij,scie->scje", weights, q_e, preferred_element_type=jnp.float32)

    placed = jnp.sum(jnp.where(pick, scores[:, :, None], jnp.float32(0)), axis=1)
    all_scores = all_sum(all_sum(placed, "mp"), "enc").reshape(owners * qry_dev, cand_count)
    all_losses, d_score = loss_terms(all_scores)
    losses = lax.dynamic_slice_in_dim(all_losses, me * qry_dev, qry_dev)

    d_e = jnp.take_along_axis(d_score.reshape(owners, slot_count), slot_of, axis=1)
    d_e = jnp.where(valid, d_e, jnp.float32(0))
    occ_grad = (occ_raw * (d_e / query_len)[:, :, None, None]).astype(jnp.bfloat16)
    onehot = (local_of[:, :, None] == jnp.arange(blk_dev, dtype=jnp.int32)) & valid[:, :, None]
    grad_emb = jnp.einsum(
        "scb,scje->bje",
        onehot.astype(jnp.bfloat16),
        occ_grad,
        preferred_element_type=jnp.float32,
    )
    grad_flat = grad_emb.reshape(row_share, emb_width)
    dot_e = jnp.sum(e_pre * grad_flat, -1, keepdims=True)
    de_pre = (scale * grad_flat - e_pre * (scale * scale * scale) * dot_e).astype(jnp.bfloat16)
    partial_w = left_product(hidden, all_gather_rows(de_pre, "mp"))
    grad_w = all_sum(partial_w, "enc")
    return (losses, grad_w)


def solution(mesh):
    return jax.shard_map(
        local,
        mesh=mesh,
        in_specs=(
            P(("groups", "enc"), "mp"),
            P("mp", None),
            P(("groups", "enc", "mp"), None, None),
            P("groups"),
            P(("groups", "enc", "mp"), None),
        ),
        out_specs=(P(("groups", "enc", "mp")), P(("groups", "mp"), None)),
        check_vma=False,
    )
```

```python
import jax
import jax.numpy as jnp
from jax import lax
from jax.sharding import PartitionSpec as P

L = 256
BLK = 64


def block_valid(block_ids, lengths):
    per_passage = L // BLK
    passage = block_ids // per_passage
    within = block_ids % per_passage
    positions = within[..., None] * BLK + jnp.arange(BLK, dtype=jnp.int32)
    return positions < lengths[passage][..., None]


def soft_max_sim(sim_tile, valid_mask):
    masked = jnp.where(valid_mask, sim_tile, jnp.float32(-1e30))
    peak = jnp.max(masked, -1, keepdims=True)
    shifted = jnp.exp(masked - peak)
    running = jnp.sum(shifted, -1, keepdims=True)
    scores = jnp.mean(peak[..., 0] + jnp.log(running[..., 0]), -1)
    weights = (shifted / running).astype(jnp.bfloat16)
    return (scores, weights)


def loss_terms(scores):
    margins = scores[:, 1:] - scores[:, :1]
    losses = jnp.mean(jax.nn.softplus(margins), 1)
    slopes = jax.nn.sigmoid(margins) / (scores.shape[1] - 1)
    d_score = jnp.concatenate([-jnp.sum(slopes, 1, keepdims=True), slopes], 1)
    return (losses, d_score)


def left_product(left, right):
    return lax.dot_general(
        left, right, (((0,), (0,)), ((), ())), preferred_element_type=jnp.float32
    )


def xor_perm(value, axis, bit):
    count = lax.axis_size(axis)
    return lax.ppermute(value, axis, [(i, i ^ bit) for i in range(count)])


def is_pow2(count):
    return count & (count - 1) == 0


def halving_steps(values, axis):
    count = lax.axis_size(axis)
    me = lax.axis_index(axis)
    accs = [v.reshape((count, -1) + v.shape[1:]) for v in values]
    bit = 1
    while True:
        keeps, sends = [], []
        for acc in accs:
            acc = acc.reshape((acc.shape[0] // 2, 2) + acc.shape[1:])
            low = (me // bit) % 2 == 0
            keeps.append(jnp.where(low, acc[:, 0], acc[:, 1]))
            sends.append(jnp.where(low, acc[:, 1], acc[:, 0]))
        if bit * 2 >= count:
            return keeps, sends, bit
        accs = [k + xor_perm(t, axis, bit) for k, t in zip(keeps, sends)]
        bit *= 2


def all_gather_rows(value, axis):
    count = lax.axis_size(axis)
    if not is_pow2(count):
        return lax.all_gather(value, axis, axis=0, tiled=True)
    me = lax.axis_index(axis)
    arr = value[None]
    bit = count // 2
    while bit >= 1:
        low = (me // bit) % 2 == 0
        other = xor_perm(arr, axis, bit)
        first = jnp.where(low, arr, other)
        second = jnp.where(low, other, arr)
        arr = jnp.stack([first, second], axis=1).reshape((-1,) + value.shape)
        bit //= 2
    return arr.reshape((-1,) + value.shape[1:])


def all_sum(value, axis):
    count = lax.axis_size(axis)
    if count > 4:
        if not is_pow2(count):
            return lax.psum(value, axis)
        bit = 1
        while bit < count:
            value = value + xor_perm(value, axis, bit)
            bit *= 2
        return value
    me = lax.axis_index(axis)
    got = [value] + [
        lax.ppermute(value, axis, [(i, (i + k) % count) for i in range(count)])
        for k in range(1, count)
    ]
    stacked = jnp.stack(got)
    by_source = [
        lax.dynamic_index_in_dim(stacked, (me - src) % count, 0, keepdims=False)
        for src in range(count)
    ]
    total = by_source[0]
    for part in by_source[1:]:
        total = total + part
    return total


def local(hidden, proj_w, queries, lengths, candidates):
    mp_count = lax.axis_size("mp")
    owners = lax.axis_size("enc") * mp_count
    row_share = hidden.shape[0] // mp_count
    emb_width = proj_w.shape[1]
    qry_dev = queries.shape[0]
    query_len = queries.shape[1]
    cand_count = candidates.shape[1]
    blk_dev = row_share // BLK
    slot_count = qry_dev * cand_count
    capacity = 2 * slot_count // owners
    me = lax.axis_index("enc") * mp_count + lax.axis_index("mp")

    packed = jnp.concatenate(
        [
            queries.reshape(qry_dev, query_len * emb_width).astype(jnp.float32),
            candidates.astype(jnp.float32),
        ],
        axis=1,
    )
    packed = all_gather_rows(packed, "mp")

    chunks = 4 if row_share % (4 * BLK) == 0 else 1
    split_rows = hidden.reshape(mp_count, chunks, row_share // chunks, hidden.shape[1])
    partials = [
        jnp.dot(split_rows[:, k], proj_w, preferred_element_type=jnp.float32).reshape(
            mp_count * (row_share // chunks), emb_width
        )
        for k in range(chunks)
    ]
    if is_pow2(mp_count) and mp_count > 1:
        keeps, sends, bit = halving_steps(partials, "mp")
        first, packed = lax.optimization_barrier((sends[0], packed))
        sends = [first] + sends[1:]
        pieces = [k + xor_perm(t, "mp", bit) for k, t in zip(keeps, sends)]
        pieces = [p.reshape(-1, emb_width) for p in pieces]
    else:
        pieces = [
            lax.psum_scatter(p, "mp", scatter_dimension=0, tiled=True) for p in partials
        ]
    e_pre = jnp.stack(pieces).reshape(row_share, emb_width)

    packed = all_gather_rows(packed, "enc")
    all_queries = (
        packed[:, : query_len * emb_width]
        .astype(jnp.bfloat16)
        .reshape(owners * qry_dev, query_len, emb_width)
    )
    all_cand = packed[:, query_len * emb_width :].astype(jnp.int32).reshape(owners, slot_count)

    slot_ids = jnp.arange(slot_count, dtype=jnp.int32)
    mine = (all_cand // blk_dev) == me
    rank = jnp.cumsum(mine.astype(jnp.int32), axis=1) - 1
    ranks = jnp.arange(capacity, dtype=jnp.int32)
    pick = mine[:, None, :] & (rank[:, None, :] == ranks[None, :, None])
    valid = jnp.any(pick, axis=2)
    slot_of = jnp.sum(jnp.where(pick, slot_ids[None, None, :], 0), axis=2).astype(jnp.int32)
    block_of = jnp.take_along_axis(all_cand, slot_of, axis=1)
    local_of = block_of % blk_dev
    query_of = jnp.arange(owners, dtype=jnp.int32)[:, None] * qry_dev + slot_of // cand_count

    q_e = all_queries[query_of]


    scale = lax.rsqrt(jnp.sum(e_pre * e_pre, -1, keepdims=True) + 1e-06)
    embedded = (e_pre * scale).astype(jnp.bfloat16)
    local_blocks = embedded.reshape(blk_dev, BLK, emb_width)

    tiles = local_blocks[local_of]
    valid_mask = block_valid(block_of, lengths)
    sim_tile = jnp.einsum("scie,scje->scij", q_e, tiles, preferred_element_type=jnp.float32)
    scores, weights = soft_max_sim(sim_tile, valid_mask[:, :, None, :])

    occ_raw = jnp.einsum("scij,scie->scje", weights, q_e, preferred_element_type=jnp.float32)

    placed = jnp.sum(jnp.where(pick, scores[:, :, None], jnp.float32(0)), axis=1)
    all_scores = all_sum(all_sum(placed, "mp"), "enc").reshape(owners * qry_dev, cand_count)
    all_losses, d_score = loss_terms(all_scores)
    losses = lax.dynamic_slice_in_dim(all_losses, me * qry_dev, qry_dev)

    d_e = jnp.take_along_axis(d_score.reshape(owners, slot_count), slot_of, axis=1)
    d_e = jnp.where(valid, d_e, jnp.float32(0))
    occ_grad = (occ_raw * (d_e / query_len)[:, :, None, None]).astype(jnp.bfloat16)
    onehot = (local_of[:, :, None] == jnp.arange(blk_dev, dtype=jnp.int32)) & valid[:, :, None]
    grad_emb = jnp.einsum(
        "scb,scje->bje",
        onehot.astype(jnp.bfloat16),
        occ_grad,
        preferred_element_type=jnp.float32,
    )
    grad_flat = grad_emb.reshape(row_share, emb_width)
    dot_e = jnp.sum(e_pre * grad_flat, -1, keepdims=True)
    de_pre = (scale * grad_flat - e_pre * (scale * scale * scale) * dot_e).astype(jnp.bfloat16)
    partial_w = left_product(hidden, all_gather_rows(de_pre, "mp"))
    grad_w = all_sum(partial_w, "enc")
    return (losses, grad_w)


def solution(mesh):
    return jax.shard_map(
        local,
        mesh=mesh,
        in_specs=(
            P(("groups", "enc"), "mp"),
            P("mp", None),
            P(("groups", "enc", "mp"), None, None),
            P("groups"),
            P(("groups", "enc", "mp"), None),
        ),
        out_specs=(P(("groups", "enc", "mp")), P(("groups", "mp"), None)),
        check_vma=False,
    )
```

```python
import jax
import jax.numpy as jnp
from jax import lax
from jax.sharding import PartitionSpec as P

L = 256
BLK = 64


def block_valid(block_ids, lengths):
    per_passage = L // BLK
    passage = block_ids // per_passage
    within = block_ids % per_passage
    positions = within[..., None] * BLK + jnp.arange(BLK, dtype=jnp.int32)
    return positions < lengths[passage][..., None]


def soft_max_sim(sim_tile, valid_mask):
    masked = jnp.where(valid_mask, sim_tile, jnp.float32(-1e30))
    peak = jnp.max(masked, -1, keepdims=True)
    shifted = jnp.exp(masked - peak)
    running = jnp.sum(shifted, -1, keepdims=True)
    scores = jnp.mean(peak[..., 0] + jnp.log(running[..., 0]), -1)
    weights = (shifted / running).astype(jnp.bfloat16)
    return (scores, weights)


def loss_terms(scores):
    margins = scores[:, 1:] - scores[:, :1]
    losses = jnp.mean(jax.nn.softplus(margins), 1)
    slopes = jax.nn.sigmoid(margins) / (scores.shape[1] - 1)
    d_score = jnp.concatenate([-jnp.sum(slopes, 1, keepdims=True), slopes], 1)
    return (losses, d_score)


def left_product(left, right):
    return lax.dot_general(
        left, right, (((0,), (0,)), ((), ())), preferred_element_type=jnp.float32
    )


def xor_perm(value, axis, bit):
    count = lax.axis_size(axis)
    return lax.ppermute(value, axis, [(i, i ^ bit) for i in range(count)])


def is_pow2(count):
    return count & (count - 1) == 0


def halving_steps(values, axis):
    count = lax.axis_size(axis)
    me = lax.axis_index(axis)
    accs = [v.reshape((count, -1) + v.shape[1:]) for v in values]
    bit = 1
    while True:
        keeps, sends = [], []
        for acc in accs:
            acc = acc.reshape((acc.shape[0] // 2, 2) + acc.shape[1:])
            low = (me // bit) % 2 == 0
            keeps.append(jnp.where(low, acc[:, 0], acc[:, 1]))
            sends.append(jnp.where(low, acc[:, 1], acc[:, 0]))
        if bit * 2 >= count:
            return keeps, sends, bit
        accs = [k + xor_perm(t, axis, bit) for k, t in zip(keeps, sends)]
        bit *= 2


def all_gather_rows(value, axis):
    count = lax.axis_size(axis)
    if not is_pow2(count):
        return lax.all_gather(value, axis, axis=0, tiled=True)
    me = lax.axis_index(axis)
    arr = value[None]
    bit = count // 2
    while bit >= 1:
        low = (me // bit) % 2 == 0
        other = xor_perm(arr, axis, bit)
        first = jnp.where(low, arr, other)
        second = jnp.where(low, other, arr)
        arr = jnp.stack([first, second], axis=1).reshape((-1,) + value.shape)
        bit //= 2
    return arr.reshape((-1,) + value.shape[1:])


def all_gather_many(values, axis):
    count = lax.axis_size(axis)
    if not is_pow2(count):
        return [lax.all_gather(v, axis, axis=0, tiled=True) for v in values]
    me = lax.axis_index(axis)
    arrs = [v[None] for v in values]
    bit = count // 2
    while bit >= 1:
        low = (me // bit) % 2 == 0
        others = lax.ppermute(arrs, axis, [(i, i ^ bit) for i in range(count)])
        arrs = [
            jnp.stack([jnp.where(low, a, o), jnp.where(low, o, a)], axis=1).reshape(
                (-1,) + v.shape
            )
            for a, o, v in zip(arrs, others, values)
        ]
        bit //= 2
    return [a.reshape((-1,) + v.shape[1:]) for a, v in zip(arrs, values)]


def all_sum(value, axis):
    count = lax.axis_size(axis)
    if count > 4:
        if not is_pow2(count):
            return lax.psum(value, axis)
        bit = 1
        while bit < count:
            value = value + xor_perm(value, axis, bit)
            bit *= 2
        return value
    me = lax.axis_index(axis)
    got = [value] + [
        lax.ppermute(value, axis, [(i, (i + k) % count) for i in range(count)])
        for k in range(1, count)
    ]
    stacked = jnp.stack(got)
    by_source = [
        lax.dynamic_index_in_dim(stacked, (me - src) % count, 0, keepdims=False)
        for src in range(count)
    ]
    total = by_source[0]
    for part in by_source[1:]:
        total = total + part
    return total


def local(hidden, proj_w, queries, lengths, candidates):
    mp_count = lax.axis_size("mp")
    owners = lax.axis_size("enc") * mp_count
    row_share = hidden.shape[0] // mp_count
    emb_width = proj_w.shape[1]
    qry_dev = queries.shape[0]
    query_len = queries.shape[1]
    cand_count = candidates.shape[1]
    blk_dev = row_share // BLK
    slot_count = qry_dev * cand_count
    capacity = 2 * slot_count // owners
    me = lax.axis_index("enc") * mp_count + lax.axis_index("mp")

    all_queries, all_cand = all_gather_many(all_gather_many([queries, candidates], "mp"), "enc")
    all_cand = all_cand.reshape(owners, slot_count)

    chunks = 4 if row_share % (4 * BLK) == 0 else 1
    split_rows = hidden.reshape(mp_count, chunks, row_share // chunks, hidden.shape[1])
    partials = [
        jnp.dot(split_rows[:, k], proj_w, preferred_element_type=jnp.float32).reshape(
            mp_count * (row_share // chunks), emb_width
        )
        for k in range(chunks)
    ]
    if is_pow2(mp_count) and mp_count > 1:
        keeps, sends, bit = halving_steps(partials, "mp")
        sends, all_queries, all_cand = lax.optimization_barrier((sends, all_queries, all_cand))
        pieces = [k + xor_perm(t, "mp", bit) for k, t in zip(keeps, sends)]
        pieces = [p.reshape(-1, emb_width) for p in pieces]
    else:
        pieces = [
            lax.psum_scatter(p, "mp", scatter_dimension=0, tiled=True) for p in partials
        ]
    e_pre = jnp.stack(pieces).reshape(row_share, emb_width)

    slot_ids = jnp.arange(slot_count, dtype=jnp.int32)
    mine = (all_cand // blk_dev) == me
    rank = jnp.cumsum(mine.astype(jnp.int32), axis=1) - 1
    ranks = jnp.arange(capacity, dtype=jnp.int32)
    pick = mine[:, None, :] & (rank[:, None, :] == ranks[None, :, None])
    valid = jnp.any(pick, axis=2)
    slot_of = jnp.sum(jnp.where(pick, slot_ids[None, None, :], 0), axis=2).astype(jnp.int32)
    block_of = jnp.take_along_axis(all_cand, slot_of, axis=1)
    local_of = block_of % blk_dev
    query_of = jnp.arange(owners, dtype=jnp.int32)[:, None] * qry_dev + slot_of // cand_count

    q_e = all_queries[query_of]


    scale = lax.rsqrt(jnp.sum(e_pre * e_pre, -1, keepdims=True) + 1e-06)
    embedded = (e_pre * scale).astype(jnp.bfloat16)
    local_blocks = embedded.reshape(blk_dev, BLK, emb_width)

    tiles = local_blocks[local_of]
    valid_mask = block_valid(block_of, lengths)
    sim_tile = jnp.einsum("scie,scje->scij", q_e, tiles, preferred_element_type=jnp.float32)
    scores, weights = soft_max_sim(sim_tile, valid_mask[:, :, None, :])

    occ_raw = jnp.einsum("scij,scie->scje", weights, q_e, preferred_element_type=jnp.float32)

    placed = jnp.sum(jnp.where(pick, scores[:, :, None], jnp.float32(0)), axis=1)
    all_scores = all_sum(all_sum(placed, "mp"), "enc").reshape(owners * qry_dev, cand_count)
    all_losses, d_score = loss_terms(all_scores)
    losses = lax.dynamic_slice_in_dim(all_losses, me * qry_dev, qry_dev)

    d_e = jnp.take_along_axis(d_score.reshape(owners, slot_count), slot_of, axis=1)
    d_e = jnp.where(valid, d_e, jnp.float32(0))
    occ_grad = (occ_raw * (d_e / query_len)[:, :, None, None]).astype(jnp.bfloat16)
    onehot = (local_of[:, :, None] == jnp.arange(blk_dev, dtype=jnp.int32)) & valid[:, :, None]
    grad_emb = jnp.einsum(
        "scb,scje->bje",
        onehot.astype(jnp.bfloat16),
        occ_grad,
        preferred_element_type=jnp.float32,
    )
    grad_flat = grad_emb.reshape(row_share, emb_width)
    dot_e = jnp.sum(e_pre * grad_flat, -1, keepdims=True)
    de_pre = (scale * grad_flat - e_pre * (scale * scale * scale) * dot_e).astype(jnp.bfloat16)
    partial_w = left_product(hidden, all_gather_rows(de_pre, "mp"))
    grad_w = all_sum(partial_w, "enc")
    return (losses, grad_w)


def solution(mesh):
    return jax.shard_map(
        local,
        mesh=mesh,
        in_specs=(
            P(("groups", "enc"), "mp"),
            P("mp", None),
            P(("groups", "enc", "mp"), None, None),
            P("groups"),
            P(("groups", "enc", "mp"), None),
        ),
        out_specs=(P(("groups", "enc", "mp")), P(("groups", "mp"), None)),
        check_vma=False,
    )
```

```python
import jax
import jax.numpy as jnp
from jax import lax
from jax.sharding import PartitionSpec as P

L = 256
BLK = 64


def block_valid(block_ids, lengths):
    per_passage = L // BLK
    passage = block_ids // per_passage
    within = block_ids % per_passage
    positions = within[..., None] * BLK + jnp.arange(BLK, dtype=jnp.int32)
    return positions < lengths[passage][..., None]


def soft_max_sim(sim_tile, valid_mask):
    masked = jnp.where(valid_mask, sim_tile, jnp.float32(-1e30))
    peak = jnp.max(masked, -1, keepdims=True)
    shifted = jnp.exp(masked - peak)
    running = jnp.sum(shifted, -1, keepdims=True)
    scores = jnp.mean(peak[..., 0] + jnp.log(running[..., 0]), -1)
    weights = (shifted / running).astype(jnp.bfloat16)
    return (scores, weights)


def loss_terms(scores):
    margins = scores[:, 1:] - scores[:, :1]
    losses = jnp.mean(jax.nn.softplus(margins), 1)
    slopes = jax.nn.sigmoid(margins) / (scores.shape[1] - 1)
    d_score = jnp.concatenate([-jnp.sum(slopes, 1, keepdims=True), slopes], 1)
    return (losses, d_score)


def left_product(left, right):
    return lax.dot_general(
        left, right, (((0,), (0,)), ((), ())), preferred_element_type=jnp.float32
    )


def xor_perm(value, axis, bit):
    count = lax.axis_size(axis)
    return lax.ppermute(value, axis, [(i, i ^ bit) for i in range(count)])


def is_pow2(count):
    return count & (count - 1) == 0


def reduce_scatter_rows(value, axis):
    count = lax.axis_size(axis)
    if not is_pow2(count):
        return lax.psum_scatter(value, axis, scatter_dimension=0, tiled=True)
    me = lax.axis_index(axis)
    acc = value.reshape((count, -1) + value.shape[1:])
    bit = 1
    while bit < count:
        acc = acc.reshape((acc.shape[0] // 2, 2) + acc.shape[1:])
        low = (me // bit) % 2 == 0
        keep = jnp.where(low, acc[:, 0], acc[:, 1])
        send = jnp.where(low, acc[:, 1], acc[:, 0])
        acc = keep + xor_perm(send, axis, bit)
        bit *= 2
    return acc.reshape((-1,) + value.shape[1:])


def all_gather_rows(value, axis):
    count = lax.axis_size(axis)
    if not is_pow2(count):
        return lax.all_gather(value, axis, axis=0, tiled=True)
    me = lax.axis_index(axis)
    arr = value[None]
    bit = count // 2
    while bit >= 1:
        low = (me // bit) % 2 == 0
        other = xor_perm(arr, axis, bit)
        first = jnp.where(low, arr, other)
        second = jnp.where(low, other, arr)
        arr = jnp.stack([first, second], axis=1).reshape((-1,) + value.shape)
        bit //= 2
    return arr.reshape((-1,) + value.shape[1:])


def all_sum(value, axis):
    count = lax.axis_size(axis)
    if count > 4:
        if not is_pow2(count):
            return lax.psum(value, axis)
        bit = 1
        while bit < count:
            value = value + xor_perm(value, axis, bit)
            bit *= 2
        return value
    me = lax.axis_index(axis)
    got = [value] + [
        lax.ppermute(value, axis, [(i, (i + k) % count) for i in range(count)])
        for k in range(1, count)
    ]
    stacked = jnp.stack(got)
    by_source = [
        lax.dynamic_index_in_dim(stacked, (me - src) % count, 0, keepdims=False)
        for src in range(count)
    ]
    total = by_source[0]
    for part in by_source[1:]:
        total = total + part
    return total


def local(hidden, proj_w, queries, lengths, candidates):
    mp_count = lax.axis_size("mp")
    owners = lax.axis_size("enc") * mp_count
    row_share = hidden.shape[0] // mp_count
    emb_width = proj_w.shape[1]
    qry_dev = queries.shape[0]
    query_len = queries.shape[1]
    cand_count = candidates.shape[1]
    blk_dev = row_share // BLK
    slot_count = qry_dev * cand_count
    capacity = 2 * slot_count // owners
    me = lax.axis_index("enc") * mp_count + lax.axis_index("mp")

    coded = jnp.concatenate(
        [
            (candidates // BLK).astype(jnp.bfloat16),
            (candidates % BLK).astype(jnp.bfloat16),
            jnp.zeros((qry_dev, emb_width - 2 * cand_count), jnp.bfloat16),
        ],
        axis=1,
    )
    packed = jnp.concatenate([queries, coded[:, None, :]], axis=1)
    packed = lax.all_gather(packed, ("enc", "mp"), axis=0, tiled=True)
    all_queries = packed[:, :query_len]
    coded = packed[:, query_len, : 2 * cand_count].astype(jnp.int32)
    all_cand = coded[:, :cand_count] * BLK + coded[:, cand_count:]
    all_cand = all_cand.reshape(owners, slot_count)

    e_pre = reduce_scatter_rows(
        jnp.dot(hidden, proj_w, preferred_element_type=jnp.float32), "mp"
    )
    scale = lax.rsqrt(jnp.sum(e_pre * e_pre, -1, keepdims=True) + 1e-06)
    embedded = (e_pre * scale).astype(jnp.bfloat16)
    local_blocks = embedded.reshape(blk_dev, BLK, emb_width)

    slot_ids = jnp.arange(slot_count, dtype=jnp.int32)
    mine = (all_cand // blk_dev) == me
    rank = jnp.cumsum(mine.astype(jnp.int32), axis=1) - 1
    ranks = jnp.arange(capacity, dtype=jnp.int32)
    pick = mine[:, None, :] & (rank[:, None, :] == ranks[None, :, None])
    valid = jnp.any(pick, axis=2)
    slot_of = jnp.sum(jnp.where(pick, slot_ids[None, None, :], 0), axis=2).astype(jnp.int32)
    block_of = jnp.take_along_axis(all_cand, slot_of, axis=1)
    local_of = block_of % blk_dev
    query_of = jnp.arange(owners, dtype=jnp.int32)[:, None] * qry_dev + slot_of // cand_count

    tiles = local_blocks[local_of]
    q_e = all_queries[query_of]
    valid_mask = block_valid(block_of, lengths)
    sim_tile = jnp.einsum("scie,scje->scij", q_e, tiles, preferred_element_type=jnp.float32)
    scores, weights = soft_max_sim(sim_tile, valid_mask[:, :, None, :])

    occ_raw = jnp.einsum("scij,scie->scje", weights, q_e, preferred_element_type=jnp.float32)

    placed = jnp.sum(jnp.where(pick, scores[:, :, None], jnp.float32(0)), axis=1)
    all_scores = all_sum(lax.psum(placed, "mp"), "enc").reshape(owners * qry_dev, cand_count)
    all_losses, d_score = loss_terms(all_scores)
    losses = lax.dynamic_slice_in_dim(all_losses, me * qry_dev, qry_dev)

    d_e = jnp.take_along_axis(d_score.reshape(owners, slot_count), slot_of, axis=1)
    d_e = jnp.where(valid, d_e, jnp.float32(0))
    occ_grad = (occ_raw * (d_e / query_len)[:, :, None, None]).astype(jnp.bfloat16)
    onehot = (local_of[:, :, None] == jnp.arange(blk_dev, dtype=jnp.int32)) & valid[:, :, None]
    grad_emb = jnp.einsum(
        "scb,scje->bje",
        onehot.astype(jnp.bfloat16),
        occ_grad,
        preferred_element_type=jnp.float32,
    )
    grad_flat = grad_emb.reshape(row_share, emb_width)
    dot_e = jnp.sum(e_pre * grad_flat, -1, keepdims=True)
    de_pre = (scale * grad_flat - e_pre * (scale * scale * scale) * dot_e).astype(jnp.bfloat16)
    partial_w = left_product(hidden, all_gather_rows(de_pre, "mp"))
    grad_w = all_sum(partial_w, "enc")
    return (losses, grad_w)


def solution(mesh):
    return jax.shard_map(
        local,
        mesh=mesh,
        in_specs=(
            P(("groups", "enc"), "mp"),
            P("mp", None),
            P(("groups", "enc", "mp"), None, None),
            P("groups"),
            P(("groups", "enc", "mp"), None),
        ),
        out_specs=(P(("groups", "enc", "mp")), P(("groups", "mp"), None)),
        check_vma=False,
    )
```

```python
import jax
import jax.numpy as jnp
from jax import lax
from jax.sharding import PartitionSpec as P

L = 256
BLK = 64


def block_valid(block_ids, lengths):
    per_passage = L // BLK
    passage = block_ids // per_passage
    within = block_ids % per_passage
    positions = within[..., None] * BLK + jnp.arange(BLK, dtype=jnp.int32)
    return positions < lengths[passage][..., None]


def soft_max_sim(sim_tile, valid_mask):
    masked = jnp.where(valid_mask, sim_tile, jnp.float32(-1e30))
    peak = jnp.max(masked, -1, keepdims=True)
    shifted = jnp.exp(masked - peak)
    running = jnp.sum(shifted, -1, keepdims=True)
    scores = jnp.mean(peak[..., 0] + jnp.log(running[..., 0]), -1)
    weights = (shifted / running).astype(jnp.bfloat16)
    return (scores, weights)


def loss_terms(scores):
    margins = scores[:, 1:] - scores[:, :1]
    losses = jnp.mean(jax.nn.softplus(margins), 1)
    slopes = jax.nn.sigmoid(margins) / (scores.shape[1] - 1)
    d_score = jnp.concatenate([-jnp.sum(slopes, 1, keepdims=True), slopes], 1)
    return (losses, d_score)


def left_product(left, right):
    return lax.dot_general(
        left, right, (((0,), (0,)), ((), ())), preferred_element_type=jnp.float32
    )


def xor_perm(value, axis, bit):
    count = lax.axis_size(axis)
    return lax.ppermute(value, axis, [(i, i ^ bit) for i in range(count)])


def is_pow2(count):
    return count & (count - 1) == 0


def halving_steps(values, axis):
    count = lax.axis_size(axis)
    me = lax.axis_index(axis)
    accs = [v.reshape((count, -1) + v.shape[1:]) for v in values]
    bit = 1
    while True:
        keeps, sends = [], []
        for acc in accs:
            acc = acc.reshape((acc.shape[0] // 2, 2) + acc.shape[1:])
            low = (me // bit) % 2 == 0
            keeps.append(jnp.where(low, acc[:, 0], acc[:, 1]))
            sends.append(jnp.where(low, acc[:, 1], acc[:, 0]))
        if bit * 2 >= count:
            return keeps, sends, bit
        accs = [k + xor_perm(t, axis, bit) for k, t in zip(keeps, sends)]
        bit *= 2


def all_gather_rows(value, axis):
    count = lax.axis_size(axis)
    if not is_pow2(count):
        return lax.all_gather(value, axis, axis=0, tiled=True)
    me = lax.axis_index(axis)
    arr = value[None]
    bit = count // 2
    while bit >= 1:
        low = (me // bit) % 2 == 0
        other = xor_perm(arr, axis, bit)
        first = jnp.where(low, arr, other)
        second = jnp.where(low, other, arr)
        arr = jnp.stack([first, second], axis=1).reshape((-1,) + value.shape)
        bit //= 2
    return arr.reshape((-1,) + value.shape[1:])


def all_sum(value, axis):
    count = lax.axis_size(axis)
    if count > 4:
        if not is_pow2(count):
            return lax.psum(value, axis)
        bit = 1
        while bit < count:
            value = value + xor_perm(value, axis, bit)
            bit *= 2
        return value
    me = lax.axis_index(axis)
    got = [value] + [
        lax.ppermute(value, axis, [(i, (i + k) % count) for i in range(count)])
        for k in range(1, count)
    ]
    stacked = jnp.stack(got)
    by_source = [
        lax.dynamic_index_in_dim(stacked, (me - src) % count, 0, keepdims=False)
        for src in range(count)
    ]
    total = by_source[0]
    for part in by_source[1:]:
        total = total + part
    return total


def local(hidden, proj_w, queries, lengths, candidates):
    mp_count = lax.axis_size("mp")
    owners = lax.axis_size("enc") * mp_count
    row_share = hidden.shape[0] // mp_count
    emb_width = proj_w.shape[1]
    qry_dev = queries.shape[0]
    query_len = queries.shape[1]
    cand_count = candidates.shape[1]
    blk_dev = row_share // BLK
    slot_count = qry_dev * cand_count
    capacity = 2 * slot_count // owners
    me = lax.axis_index("enc") * mp_count + lax.axis_index("mp")

    all_queries = lax.all_gather(queries, ("enc", "mp"), axis=0, tiled=True)
    all_cand = lax.all_gather(candidates, ("enc", "mp"), axis=0, tiled=True)
    all_cand = all_cand.reshape(owners, slot_count)

    chunks = 4 if row_share % (4 * BLK) == 0 else 1
    split_rows = hidden.reshape(mp_count, chunks, row_share // chunks, hidden.shape[1])
    partials = [
        jnp.dot(split_rows[:, k], proj_w, preferred_element_type=jnp.float32).reshape(
            mp_count * (row_share // chunks), emb_width
        )
        for k in range(chunks)
    ]
    if is_pow2(mp_count) and mp_count > 1:
        keeps, sends, bit = halving_steps(partials, "mp")
        pieces = [k + xor_perm(t, "mp", bit) for k, t in zip(keeps, sends)]
        pieces = [p.reshape(-1, emb_width) for p in pieces]
    else:
        pieces = [
            lax.psum_scatter(p, "mp", scatter_dimension=0, tiled=True) for p in partials
        ]
    e_pre = jnp.stack(pieces).reshape(row_share, emb_width)

    scale = lax.rsqrt(jnp.sum(e_pre * e_pre, -1, keepdims=True) + 1e-06)
    embedded = (e_pre * scale).astype(jnp.bfloat16)
    local_blocks = embedded.reshape(blk_dev, BLK, emb_width)

    slot_ids = jnp.arange(slot_count, dtype=jnp.int32)
    mine = (all_cand // blk_dev) == me
    rank = jnp.cumsum(mine.astype(jnp.int32), axis=1) - 1
    ranks = jnp.arange(capacity, dtype=jnp.int32)
    pick = mine[:, None, :] & (rank[:, None, :] == ranks[None, :, None])
    valid = jnp.any(pick, axis=2)
    slot_of = jnp.sum(jnp.where(pick, slot_ids[None, None, :], 0), axis=2).astype(jnp.int32)
    block_of = jnp.take_along_axis(all_cand, slot_of, axis=1)
    local_of = block_of % blk_dev
    query_of = jnp.arange(owners, dtype=jnp.int32)[:, None] * qry_dev + slot_of // cand_count

    tiles = local_blocks[local_of]
    q_e = all_queries[query_of]
    valid_mask = block_valid(block_of, lengths)
    sim_tile = jnp.einsum("scie,scje->scij", q_e, tiles, preferred_element_type=jnp.float32)
    scores, weights = soft_max_sim(sim_tile, valid_mask[:, :, None, :])

    occ_raw = jnp.einsum("scij,scie->scje", weights, q_e, preferred_element_type=jnp.float32)

    placed = jnp.sum(jnp.where(pick, scores[:, :, None], jnp.float32(0)), axis=1)
    all_scores = all_sum(lax.psum(placed, "mp"), "enc").reshape(owners * qry_dev, cand_count)
    all_losses, d_score = loss_terms(all_scores)
    losses = lax.dynamic_slice_in_dim(all_losses, me * qry_dev, qry_dev)

    d_e = jnp.take_along_axis(d_score.reshape(owners, slot_count), slot_of, axis=1)
    d_e = jnp.where(valid, d_e, jnp.float32(0))
    occ_grad = (occ_raw * (d_e / query_len)[:, :, None, None]).astype(jnp.bfloat16)
    onehot = (local_of[:, :, None] == jnp.arange(blk_dev, dtype=jnp.int32)) & valid[:, :, None]
    grad_emb = jnp.einsum(
        "scb,scje->bje",
        onehot.astype(jnp.bfloat16),
        occ_grad,
        preferred_element_type=jnp.float32,
    )
    grad_flat = grad_emb.reshape(row_share, emb_width)
    dot_e = jnp.sum(e_pre * grad_flat, -1, keepdims=True)
    de_pre = (scale * grad_flat - e_pre * (scale * scale * scale) * dot_e).astype(jnp.bfloat16)
    partial_w = left_product(hidden, all_gather_rows(de_pre, "mp"))
    grad_w = all_sum(partial_w, "enc")
    return (losses, grad_w)


def solution(mesh):
    return jax.shard_map(
        local,
        mesh=mesh,
        in_specs=(
            P(("groups", "enc"), "mp"),
            P("mp", None),
            P(("groups", "enc", "mp"), None, None),
            P("groups"),
            P(("groups", "enc", "mp"), None),
        ),
        out_specs=(P(("groups", "enc", "mp")), P(("groups", "mp"), None)),
        check_vma=False,
    )
```

```python
import jax
import jax.numpy as jnp
from jax import lax
from jax.sharding import PartitionSpec as P

L = 256
BLK = 64


def block_valid(block_ids, lengths):
    per_passage = L // BLK
    passage = block_ids // per_passage
    within = block_ids % per_passage
    positions = within[..., None] * BLK + jnp.arange(BLK, dtype=jnp.int32)
    return positions < lengths[passage][..., None]


def soft_max_sim(sim_tile, valid_mask):
    masked = jnp.where(valid_mask, sim_tile, jnp.float32(-1e30))
    peak = jnp.max(masked, -1, keepdims=True)
    shifted = jnp.exp(masked - peak)
    running = jnp.sum(shifted, -1, keepdims=True)
    scores = jnp.mean(peak[..., 0] + jnp.log(running[..., 0]), -1)
    weights = (shifted / running).astype(jnp.bfloat16)
    return (scores, weights)


def loss_terms(scores):
    margins = scores[:, 1:] - scores[:, :1]
    losses = jnp.mean(jax.nn.softplus(margins), 1)
    slopes = jax.nn.sigmoid(margins) / (scores.shape[1] - 1)
    d_score = jnp.concatenate([-jnp.sum(slopes, 1, keepdims=True), slopes], 1)
    return (losses, d_score)


def left_product(left, right):
    return lax.dot_general(
        left, right, (((0,), (0,)), ((), ())), preferred_element_type=jnp.float32
    )


def xor_perm(value, axis, bit):
    count = lax.axis_size(axis)
    return lax.ppermute(value, axis, [(i, i ^ bit) for i in range(count)])


def is_pow2(count):
    return count & (count - 1) == 0


def halving_steps(values, axis):
    count = lax.axis_size(axis)
    me = lax.axis_index(axis)
    accs = [v.reshape((count, -1) + v.shape[1:]) for v in values]
    bit = 1
    while True:
        keeps, sends = [], []
        for acc in accs:
            acc = acc.reshape((acc.shape[0] // 2, 2) + acc.shape[1:])
            low = (me // bit) % 2 == 0
            keeps.append(jnp.where(low, acc[:, 0], acc[:, 1]))
            sends.append(jnp.where(low, acc[:, 1], acc[:, 0]))
        if bit * 2 >= count:
            return keeps, sends, bit
        accs = [k + xor_perm(t, axis, bit) for k, t in zip(keeps, sends)]
        bit *= 2


def all_gather_rows(value, axis):
    count = lax.axis_size(axis)
    if not is_pow2(count):
        return lax.all_gather(value, axis, axis=0, tiled=True)
    me = lax.axis_index(axis)
    arr = value[None]
    bit = count // 2
    while bit >= 1:
        low = (me // bit) % 2 == 0
        other = xor_perm(arr, axis, bit)
        first = jnp.where(low, arr, other)
        second = jnp.where(low, other, arr)
        arr = jnp.stack([first, second], axis=1).reshape((-1,) + value.shape)
        bit //= 2
    return arr.reshape((-1,) + value.shape[1:])


def all_gather_many(values, axis):
    count = lax.axis_size(axis)
    if not is_pow2(count):
        return [lax.all_gather(v, axis, axis=0, tiled=True) for v in values]
    me = lax.axis_index(axis)
    arrs = [v[None] for v in values]
    bit = count // 2
    while bit >= 1:
        low = (me // bit) % 2 == 0
        others = lax.ppermute(arrs, axis, [(i, i ^ bit) for i in range(count)])
        arrs = [
            jnp.stack([jnp.where(low, a, o), jnp.where(low, o, a)], axis=1).reshape(
                (-1,) + v.shape
            )
            for a, o, v in zip(arrs, others, values)
        ]
        bit //= 2
    return [a.reshape((-1,) + v.shape[1:]) for a, v in zip(arrs, values)]


def all_sum(value, axis):
    count = lax.axis_size(axis)
    if count > 4:
        if not is_pow2(count):
            return lax.psum(value, axis)
        bit = 1
        while bit < count:
            value = value + xor_perm(value, axis, bit)
            bit *= 2
        return value
    me = lax.axis_index(axis)
    got = [value] + [
        lax.ppermute(value, axis, [(i, (i + k) % count) for i in range(count)])
        for k in range(1, count)
    ]
    stacked = jnp.stack(got)
    by_source = [
        lax.dynamic_index_in_dim(stacked, (me - src) % count, 0, keepdims=False)
        for src in range(count)
    ]
    total = by_source[0]
    for part in by_source[1:]:
        total = total + part
    return total


def local(hidden, proj_w, queries, lengths, candidates):
    mp_count = lax.axis_size("mp")
    owners = lax.axis_size("enc") * mp_count
    row_share = hidden.shape[0] // mp_count
    emb_width = proj_w.shape[1]
    qry_dev = queries.shape[0]
    query_len = queries.shape[1]
    cand_count = candidates.shape[1]
    blk_dev = row_share // BLK
    slot_count = qry_dev * cand_count
    capacity = 2 * slot_count // owners
    me = lax.axis_index("enc") * mp_count + lax.axis_index("mp")

    gathered = all_gather_many([queries, candidates], "mp")

    chunks = 4 if row_share % (4 * BLK) == 0 else 1
    split_rows = hidden.reshape(mp_count, chunks, row_share // chunks, hidden.shape[1])
    partials = [
        jnp.dot(split_rows[:, k], proj_w, preferred_element_type=jnp.float32).reshape(
            mp_count * (row_share // chunks), emb_width
        )
        for k in range(chunks)
    ]
    if is_pow2(mp_count) and mp_count > 1:
        keeps, sends, bit = halving_steps(partials, "mp")
        last, gathered = lax.optimization_barrier((sends[-1], gathered))
        sends = sends[:-1] + [last]
        pieces = [k + xor_perm(t, "mp", bit) for k, t in zip(keeps, sends)]
        pieces = [p.reshape(-1, emb_width) for p in pieces]
    else:
        pieces = [
            lax.psum_scatter(p, "mp", scatter_dimension=0, tiled=True) for p in partials
        ]
    e_pre = jnp.stack(pieces).reshape(row_share, emb_width)

    all_queries, all_cand = all_gather_many(gathered, "enc")
    all_cand = all_cand.reshape(owners, slot_count)

    slot_ids = jnp.arange(slot_count, dtype=jnp.int32)
    mine = (all_cand // blk_dev) == me
    rank = jnp.cumsum(mine.astype(jnp.int32), axis=1) - 1
    ranks = jnp.arange(capacity, dtype=jnp.int32)
    pick = mine[:, None, :] & (rank[:, None, :] == ranks[None, :, None])
    valid = jnp.any(pick, axis=2)
    slot_of = jnp.sum(jnp.where(pick, slot_ids[None, None, :], 0), axis=2).astype(jnp.int32)
    block_of = jnp.take_along_axis(all_cand, slot_of, axis=1)
    local_of = block_of % blk_dev
    query_of = jnp.arange(owners, dtype=jnp.int32)[:, None] * qry_dev + slot_of // cand_count

    q_e = all_queries[query_of]


    scale = lax.rsqrt(jnp.sum(e_pre * e_pre, -1, keepdims=True) + 1e-06)
    embedded = (e_pre * scale).astype(jnp.bfloat16)
    local_blocks = embedded.reshape(blk_dev, BLK, emb_width)

    tiles = local_blocks[local_of]
    valid_mask = block_valid(block_of, lengths)
    sim_tile = jnp.einsum("scie,scje->scij", q_e, tiles, preferred_element_type=jnp.float32)
    scores, weights = soft_max_sim(sim_tile, valid_mask[:, :, None, :])

    occ_raw = jnp.einsum("scij,scie->scje", weights, q_e, preferred_element_type=jnp.float32)

    placed = jnp.sum(jnp.where(pick, scores[:, :, None], jnp.float32(0)), axis=1)
    all_scores = all_sum(all_sum(placed, "mp"), "enc").reshape(owners * qry_dev, cand_count)
    all_losses, d_score = loss_terms(all_scores)
    losses = lax.dynamic_slice_in_dim(all_losses, me * qry_dev, qry_dev)

    d_e = jnp.take_along_axis(d_score.reshape(owners, slot_count), slot_of, axis=1)
    d_e = jnp.where(valid, d_e, jnp.float32(0))
    occ_grad = (occ_raw * (d_e / query_len)[:, :, None, None]).astype(jnp.bfloat16)
    onehot = (local_of[:, :, None] == jnp.arange(blk_dev, dtype=jnp.int32)) & valid[:, :, None]
    grad_emb = jnp.einsum(
        "scb,scje->bje",
        onehot.astype(jnp.bfloat16),
        occ_grad,
        preferred_element_type=jnp.float32,
    )
    grad_flat = grad_emb.reshape(row_share, emb_width)
    dot_e = jnp.sum(e_pre * grad_flat, -1, keepdims=True)
    de_pre = (scale * grad_flat - e_pre * (scale * scale * scale) * dot_e).astype(jnp.bfloat16)
    partial_w = left_product(hidden, all_gather_rows(de_pre, "mp"))
    grad_w = all_sum(partial_w, "enc")
    return (losses, grad_w)


def solution(mesh):
    return jax.shard_map(
        local,
        mesh=mesh,
        in_specs=(
            P(("groups", "enc"), "mp"),
            P("mp", None),
            P(("groups", "enc", "mp"), None, None),
            P("groups"),
            P(("groups", "enc", "mp"), None),
        ),
        out_specs=(P(("groups", "enc", "mp")), P(("groups", "mp"), None)),
        check_vma=False,
    )
```

```python
import jax
import jax.numpy as jnp
from jax import lax
from jax.sharding import PartitionSpec as P

L = 256
BLK = 64


def block_valid(block_ids, lengths):
    per_passage = L // BLK
    passage = block_ids // per_passage
    within = block_ids % per_passage
    positions = within[..., None] * BLK + jnp.arange(BLK, dtype=jnp.int32)
    return positions < lengths[passage][..., None]


def soft_max_sim(sim_tile, valid_mask):
    masked = jnp.where(valid_mask, sim_tile, jnp.float32(-1e30))
    peak = jnp.max(masked, -1, keepdims=True)
    shifted = jnp.exp(masked - peak)
    running = jnp.sum(shifted, -1, keepdims=True)
    scores = jnp.mean(peak[..., 0] + jnp.log(running[..., 0]), -1)
    weights = (shifted / running).astype(jnp.bfloat16)
    return (scores, weights)


def loss_terms(scores):
    margins = scores[:, 1:] - scores[:, :1]
    losses = jnp.mean(jax.nn.softplus(margins), 1)
    slopes = jax.nn.sigmoid(margins) / (scores.shape[1] - 1)
    d_score = jnp.concatenate([-jnp.sum(slopes, 1, keepdims=True), slopes], 1)
    return (losses, d_score)


def left_product(left, right):
    return lax.dot_general(
        left, right, (((0,), (0,)), ((), ())), preferred_element_type=jnp.float32
    )


def xor_perm(value, axis, bit):
    count = lax.axis_size(axis)
    return lax.ppermute(value, axis, [(i, i ^ bit) for i in range(count)])


def is_pow2(count):
    return count & (count - 1) == 0


def halving_steps(values, axis):
    count = lax.axis_size(axis)
    me = lax.axis_index(axis)
    accs = [v.reshape((count, -1) + v.shape[1:]) for v in values]
    bit = 1
    while True:
        keeps, sends = [], []
        for acc in accs:
            acc = acc.reshape((acc.shape[0] // 2, 2) + acc.shape[1:])
            low = (me // bit) % 2 == 0
            keeps.append(jnp.where(low, acc[:, 0], acc[:, 1]))
            sends.append(jnp.where(low, acc[:, 1], acc[:, 0]))
        if bit * 2 >= count:
            return keeps, sends, bit
        accs = [k + xor_perm(t, axis, bit) for k, t in zip(keeps, sends)]
        bit *= 2


def all_gather_rows(value, axis):
    count = lax.axis_size(axis)
    if not is_pow2(count):
        return lax.all_gather(value, axis, axis=0, tiled=True)
    me = lax.axis_index(axis)
    arr = value[None]
    bit = count // 2
    while bit >= 1:
        low = (me // bit) % 2 == 0
        other = xor_perm(arr, axis, bit)
        first = jnp.where(low, arr, other)
        second = jnp.where(low, other, arr)
        arr = jnp.stack([first, second], axis=1).reshape((-1,) + value.shape)
        bit //= 2
    return arr.reshape((-1,) + value.shape[1:])


def all_gather_many(values, axis):
    count = lax.axis_size(axis)
    if not is_pow2(count):
        return [lax.all_gather(v, axis, axis=0, tiled=True) for v in values]
    me = lax.axis_index(axis)
    arrs = [v[None] for v in values]
    bit = count // 2
    while bit >= 1:
        low = (me // bit) % 2 == 0
        others = lax.ppermute(arrs, axis, [(i, i ^ bit) for i in range(count)])
        arrs = [
            jnp.stack([jnp.where(low, a, o), jnp.where(low, o, a)], axis=1).reshape(
                (-1,) + v.shape
            )
            for a, o, v in zip(arrs, others, values)
        ]
        bit //= 2
    return [a.reshape((-1,) + v.shape[1:]) for a, v in zip(arrs, values)]


def all_sum(value, axis):
    count = lax.axis_size(axis)
    if count > 4:
        if not is_pow2(count):
            return lax.psum(value, axis)
        bit = 1
        while bit < count:
            value = value + xor_perm(value, axis, bit)
            bit *= 2
        return value
    me = lax.axis_index(axis)
    got = [value] + [
        lax.ppermute(value, axis, [(i, (i + k) % count) for i in range(count)])
        for k in range(1, count)
    ]
    stacked = jnp.stack(got)
    by_source = [
        lax.dynamic_index_in_dim(stacked, (me - src) % count, 0, keepdims=False)
        for src in range(count)
    ]
    total = by_source[0]
    for part in by_source[1:]:
        total = total + part
    return total


def local(hidden, proj_w, queries, lengths, candidates):
    mp_count = lax.axis_size("mp")
    owners = lax.axis_size("enc") * mp_count
    row_share = hidden.shape[0] // mp_count
    emb_width = proj_w.shape[1]
    qry_dev = queries.shape[0]
    query_len = queries.shape[1]
    cand_count = candidates.shape[1]
    blk_dev = row_share // BLK
    slot_count = qry_dev * cand_count
    capacity = 2 * slot_count // owners
    me = lax.axis_index("enc") * mp_count + lax.axis_index("mp")

    gathered = all_gather_many([queries, candidates], "mp")

    chunks = 4 if row_share % (4 * BLK) == 0 else 1
    split_rows = hidden.reshape(mp_count, chunks, row_share // chunks, hidden.shape[1])
    partials = [
        jnp.dot(split_rows[:, k], proj_w, preferred_element_type=jnp.float32).reshape(
            mp_count * (row_share // chunks), emb_width
        )
        for k in range(chunks)
    ]
    if is_pow2(mp_count) and mp_count > 1:
        keeps, sends, bit = halving_steps(partials, "mp")
        last, gathered = lax.optimization_barrier((sends[-1], gathered))
        sends = sends[:-1] + [last]
        pieces = [k + xor_perm(t, "mp", bit) for k, t in zip(keeps, sends)]
        pieces = [p.reshape(-1, emb_width) for p in pieces]
    else:
        pieces = [
            lax.psum_scatter(p, "mp", scatter_dimension=0, tiled=True) for p in partials
        ]
    e_pre = jnp.stack(pieces).reshape(row_share, emb_width)

    all_queries, all_cand = all_gather_many(gathered, "enc")
    all_cand = all_cand.reshape(owners, slot_count)

    slot_ids = jnp.arange(slot_count, dtype=jnp.int32)
    mine = (all_cand // blk_dev) == me
    rank = jnp.cumsum(mine.astype(jnp.int32), axis=1) - 1
    ranks = jnp.arange(capacity, dtype=jnp.int32)
    pick = mine[:, None, :] & (rank[:, None, :] == ranks[None, :, None])
    valid = jnp.any(pick, axis=2)
    slot_of = jnp.sum(jnp.where(pick, slot_ids[None, None, :], 0), axis=2).astype(jnp.int32)
    block_of = jnp.take_along_axis(all_cand, slot_of, axis=1)
    local_of = block_of % blk_dev
    query_of = jnp.arange(owners, dtype=jnp.int32)[:, None] * qry_dev + slot_of // cand_count

    q_e = all_queries[query_of]


    scale = lax.rsqrt(jnp.sum(e_pre * e_pre, -1, keepdims=True) + 1e-06)
    embedded = (e_pre * scale).astype(jnp.bfloat16)
    local_blocks = embedded.reshape(blk_dev, BLK, emb_width)

    tiles = local_blocks[local_of]
    valid_mask = block_valid(block_of, lengths)
    sim_tile = jnp.einsum("scie,scje->scij", q_e, tiles, preferred_element_type=jnp.float32)
    scores, weights = soft_max_sim(sim_tile, valid_mask[:, :, None, :])

    occ_raw = jnp.einsum("scij,scie->scje", weights, q_e, preferred_element_type=jnp.float32)

    placed = jnp.sum(jnp.where(pick, scores[:, :, None], jnp.float32(0)), axis=1)
    all_scores = all_sum(all_sum(placed, "mp"), "enc").reshape(owners * qry_dev, cand_count)
    all_losses, d_score = loss_terms(all_scores)
    losses = lax.dynamic_slice_in_dim(all_losses, me * qry_dev, qry_dev)

    d_e = jnp.take_along_axis(d_score.reshape(owners, slot_count), slot_of, axis=1)
    d_e = jnp.where(valid, d_e, jnp.float32(0))
    occ_grad = (occ_raw * (d_e / query_len)[:, :, None, None]).astype(jnp.bfloat16)
    onehot = (local_of[:, :, None] == jnp.arange(blk_dev, dtype=jnp.int32)) & valid[:, :, None]
    onehot = onehot.astype(jnp.bfloat16)
    halves = 2 if blk_dev % 2 == 0 else 1
    half_blk = blk_dev // halves
    half_rows = half_blk * BLK
    split_hidden = hidden.reshape(mp_count, halves, half_rows, hidden.shape[1])
    cubed = e_pre * (scale * scale * scale)
    partial_w = None
    for h in range(halves):
        grad_emb = jnp.einsum(
            "scb,scje->bje",
            onehot[:, :, h * half_blk : (h + 1) * half_blk],
            occ_grad,
            preferred_element_type=jnp.float32,
        )
        grad_flat = grad_emb.reshape(half_rows, emb_width)
        rows = slice(h * half_rows, (h + 1) * half_rows)
        dot_e = jnp.sum(e_pre[rows] * grad_flat, -1, keepdims=True)
        de_pre = (scale[rows] * grad_flat - cubed[rows] * dot_e).astype(jnp.bfloat16)
        term = left_product(
            split_hidden[:, h].reshape(mp_count * half_rows, hidden.shape[1]),
            all_gather_rows(de_pre, "mp"),
        )
        partial_w = term if partial_w is None else partial_w + term
    grad_w = all_sum(partial_w, "enc")
    return (losses, grad_w)


def solution(mesh):
    return jax.shard_map(
        local,
        mesh=mesh,
        in_specs=(
            P(("groups", "enc"), "mp"),
            P("mp", None),
            P(("groups", "enc", "mp"), None, None),
            P("groups"),
            P(("groups", "enc", "mp"), None),
        ),
        out_specs=(P(("groups", "enc", "mp")), P(("groups", "mp"), None)),
        check_vma=False,
    )
```

```python
import jax
import jax.numpy as jnp
from jax import lax
from jax.sharding import PartitionSpec as P

L = 256
BLK = 64


def block_valid(block_ids, lengths):
    per_passage = L // BLK
    passage = block_ids // per_passage
    within = block_ids % per_passage
    positions = within[..., None] * BLK + jnp.arange(BLK, dtype=jnp.int32)
    return positions < lengths[passage][..., None]


def soft_max_sim(sim_tile, valid_mask):
    masked = jnp.where(valid_mask, sim_tile, jnp.float32(-1e30))
    peak = jnp.max(masked, -1, keepdims=True)
    shifted = jnp.exp(masked - peak)
    running = jnp.sum(shifted, -1, keepdims=True)
    scores = jnp.mean(peak[..., 0] + jnp.log(running[..., 0]), -1)
    weights = (shifted / running).astype(jnp.bfloat16)
    return (scores, weights)


def loss_terms(scores):
    margins = scores[:, 1:] - scores[:, :1]
    losses = jnp.mean(jax.nn.softplus(margins), 1)
    slopes = jax.nn.sigmoid(margins) / (scores.shape[1] - 1)
    d_score = jnp.concatenate([-jnp.sum(slopes, 1, keepdims=True), slopes], 1)
    return (losses, d_score)


def left_product(left, right):
    return lax.dot_general(
        left, right, (((0,), (0,)), ((), ())), preferred_element_type=jnp.float32
    )


def xor_perm(value, axis, bit):
    count = lax.axis_size(axis)
    return lax.ppermute(value, axis, [(i, i ^ bit) for i in range(count)])


def is_pow2(count):
    return count & (count - 1) == 0


def halving_steps(values, axis):
    count = lax.axis_size(axis)
    me = lax.axis_index(axis)
    accs = [v.reshape((count, -1) + v.shape[1:]) for v in values]
    bit = 1
    while True:
        keeps, sends = [], []
        for acc in accs:
            acc = acc.reshape((acc.shape[0] // 2, 2) + acc.shape[1:])
            low = (me // bit) % 2 == 0
            keeps.append(jnp.where(low, acc[:, 0], acc[:, 1]))
            sends.append(jnp.where(low, acc[:, 1], acc[:, 0]))
        if bit * 2 >= count:
            return keeps, sends, bit
        accs = [k + xor_perm(t, axis, bit) for k, t in zip(keeps, sends)]
        bit *= 2


def all_gather_rows(value, axis):
    count = lax.axis_size(axis)
    if not is_pow2(count):
        return lax.all_gather(value, axis, axis=0, tiled=True)
    me = lax.axis_index(axis)
    arr = value[None]
    bit = count // 2
    while bit >= 1:
        low = (me // bit) % 2 == 0
        other = xor_perm(arr, axis, bit)
        first = jnp.where(low, arr, other)
        second = jnp.where(low, other, arr)
        arr = jnp.stack([first, second], axis=1).reshape((-1,) + value.shape)
        bit //= 2
    return arr.reshape((-1,) + value.shape[1:])


def all_gather_many(values, axis):
    count = lax.axis_size(axis)
    if not is_pow2(count):
        return [lax.all_gather(v, axis, axis=0, tiled=True) for v in values]
    me = lax.axis_index(axis)
    arrs = [v[None] for v in values]
    bit = count // 2
    while bit >= 1:
        low = (me // bit) % 2 == 0
        others = lax.ppermute(arrs, axis, [(i, i ^ bit) for i in range(count)])
        arrs = [
            jnp.stack([jnp.where(low, a, o), jnp.where(low, o, a)], axis=1).reshape(
                (-1,) + v.shape
            )
            for a, o, v in zip(arrs, others, values)
        ]
        bit //= 2
    return [a.reshape((-1,) + v.shape[1:]) for a, v in zip(arrs, values)]


def all_sum(value, axis):
    count = lax.axis_size(axis)
    if count > 4:
        if not is_pow2(count):
            return lax.psum(value, axis)
        bit = 1
        while bit < count:
            value = value + xor_perm(value, axis, bit)
            bit *= 2
        return value
    me = lax.axis_index(axis)
    got = [value] + [
        lax.ppermute(value, axis, [(i, (i + k) % count) for i in range(count)])
        for k in range(1, count)
    ]
    stacked = jnp.stack(got)
    by_source = [
        lax.dynamic_index_in_dim(stacked, (me - src) % count, 0, keepdims=False)
        for src in range(count)
    ]
    total = by_source[0]
    for part in by_source[1:]:
        total = total + part
    return total


def local(hidden, proj_w, queries, lengths, candidates):
    mp_count = lax.axis_size("mp")
    owners = lax.axis_size("enc") * mp_count
    row_share = hidden.shape[0] // mp_count
    emb_width = proj_w.shape[1]
    qry_dev = queries.shape[0]
    query_len = queries.shape[1]
    cand_count = candidates.shape[1]
    blk_dev = row_share // BLK
    slot_count = qry_dev * cand_count
    capacity = 2 * slot_count // owners
    me = lax.axis_index("enc") * mp_count + lax.axis_index("mp")

    gathered = all_gather_many([queries, candidates], "mp")

    chunks = 8 if row_share % (8 * BLK) == 0 else 1
    split_rows = hidden.reshape(mp_count, chunks, row_share // chunks, hidden.shape[1])
    partials = [
        jnp.dot(split_rows[:, k], proj_w, preferred_element_type=jnp.float32).reshape(
            mp_count * (row_share // chunks), emb_width
        )
        for k in range(chunks)
    ]
    if is_pow2(mp_count) and mp_count > 1:
        keeps, sends, bit = halving_steps(partials, "mp")
        last, gathered = lax.optimization_barrier((sends[-1], gathered))
        sends = sends[:-1] + [last]
        pieces = [k + xor_perm(t, "mp", bit) for k, t in zip(keeps, sends)]
        pieces = [p.reshape(-1, emb_width) for p in pieces]
    else:
        pieces = [
            lax.psum_scatter(p, "mp", scatter_dimension=0, tiled=True) for p in partials
        ]
    e_pre = jnp.stack(pieces).reshape(row_share, emb_width)

    all_queries, all_cand = all_gather_many(gathered, "enc")
    all_cand = all_cand.reshape(owners, slot_count)

    slot_ids = jnp.arange(slot_count, dtype=jnp.int32)
    mine = (all_cand // blk_dev) == me
    rank = jnp.cumsum(mine.astype(jnp.int32), axis=1) - 1
    ranks = jnp.arange(capacity, dtype=jnp.int32)
    pick = mine[:, None, :] & (rank[:, None, :] == ranks[None, :, None])
    valid = jnp.any(pick, axis=2)
    slot_of = jnp.sum(jnp.where(pick, slot_ids[None, None, :], 0), axis=2).astype(jnp.int32)
    block_of = jnp.take_along_axis(all_cand, slot_of, axis=1)
    local_of = block_of % blk_dev
    query_of = jnp.arange(owners, dtype=jnp.int32)[:, None] * qry_dev + slot_of // cand_count

    q_e = all_queries[query_of]


    scale = lax.rsqrt(jnp.sum(e_pre * e_pre, -1, keepdims=True) + 1e-06)
    embedded = (e_pre * scale).astype(jnp.bfloat16)
    local_blocks = embedded.reshape(blk_dev, BLK, emb_width)

    tiles = local_blocks[local_of]
    valid_mask = block_valid(block_of, lengths)
    sim_tile = jnp.einsum("scie,scje->scij", q_e, tiles, preferred_element_type=jnp.float32)
    scores, weights = soft_max_sim(sim_tile, valid_mask[:, :, None, :])

    occ_raw = jnp.einsum("scij,scie->scje", weights, q_e, preferred_element_type=jnp.float32)

    placed = jnp.sum(jnp.where(pick, scores[:, :, None], jnp.float32(0)), axis=1)
    all_scores = all_sum(all_sum(placed, "mp"), "enc").reshape(owners * qry_dev, cand_count)
    all_losses, d_score = loss_terms(all_scores)
    losses = lax.dynamic_slice_in_dim(all_losses, me * qry_dev, qry_dev)

    d_e = jnp.take_along_axis(d_score.reshape(owners, slot_count), slot_of, axis=1)
    d_e = jnp.where(valid, d_e, jnp.float32(0))
    occ_grad = (occ_raw * (d_e / query_len)[:, :, None, None]).astype(jnp.bfloat16)
    onehot = (local_of[:, :, None] == jnp.arange(blk_dev, dtype=jnp.int32)) & valid[:, :, None]
    grad_emb = jnp.einsum(
        "scb,scje->bje",
        onehot.astype(jnp.bfloat16),
        occ_grad,
        preferred_element_type=jnp.float32,
    )
    grad_flat = grad_emb.reshape(row_share, emb_width)
    dot_e = jnp.sum(e_pre * grad_flat, -1, keepdims=True)
    de_pre = (scale * grad_flat - e_pre * (scale * scale * scale) * dot_e).astype(jnp.bfloat16)
    partial_w = left_product(hidden, all_gather_rows(de_pre, "mp"))
    grad_w = all_sum(partial_w, "enc")
    return (losses, grad_w)


def solution(mesh):
    return jax.shard_map(
        local,
        mesh=mesh,
        in_specs=(
            P(("groups", "enc"), "mp"),
            P("mp", None),
            P(("groups", "enc", "mp"), None, None),
            P("groups"),
            P(("groups", "enc", "mp"), None),
        ),
        out_specs=(P(("groups", "enc", "mp")), P(("groups", "mp"), None)),
        check_vma=False,
    )
```

```python
import jax
import jax.numpy as jnp
from jax import lax
from jax.sharding import PartitionSpec as P

L = 256
BLK = 64


def block_valid(block_ids, lengths):
    per_passage = L // BLK
    passage = block_ids // per_passage
    within = block_ids % per_passage
    positions = within[..., None] * BLK + jnp.arange(BLK, dtype=jnp.int32)
    return positions < lengths[passage][..., None]


def soft_max_sim(sim_tile, valid_mask):
    masked = jnp.where(valid_mask, sim_tile, jnp.float32(-1e30))
    peak = jnp.max(masked, -1, keepdims=True)
    shifted = jnp.exp(masked - peak)
    running = jnp.sum(shifted, -1, keepdims=True)
    scores = jnp.mean(peak[..., 0] + jnp.log(running[..., 0]), -1)
    weights = (shifted / running).astype(jnp.bfloat16)
    return (scores, weights)


def loss_terms(scores):
    margins = scores[:, 1:] - scores[:, :1]
    losses = jnp.mean(jax.nn.softplus(margins), 1)
    slopes = jax.nn.sigmoid(margins) / (scores.shape[1] - 1)
    d_score = jnp.concatenate([-jnp.sum(slopes, 1, keepdims=True), slopes], 1)
    return (losses, d_score)


def left_product(left, right):
    return lax.dot_general(
        left, right, (((0,), (0,)), ((), ())), preferred_element_type=jnp.float32
    )


def xor_perm(value, axis, bit):
    count = lax.axis_size(axis)
    return lax.ppermute(value, axis, [(i, i ^ bit) for i in range(count)])


def is_pow2(count):
    return count & (count - 1) == 0


def halving_steps(values, axis):
    count = lax.axis_size(axis)
    me = lax.axis_index(axis)
    accs = [v.reshape((count, -1) + v.shape[1:]) for v in values]
    bit = 1
    while True:
        keeps, sends = [], []
        for acc in accs:
            acc = acc.reshape((acc.shape[0] // 2, 2) + acc.shape[1:])
            low = (me // bit) % 2 == 0
            keeps.append(jnp.where(low, acc[:, 0], acc[:, 1]))
            sends.append(jnp.where(low, acc[:, 1], acc[:, 0]))
        if bit * 2 >= count:
            return keeps, sends, bit
        accs = [k + xor_perm(t, axis, bit) for k, t in zip(keeps, sends)]
        bit *= 2


def all_gather_rows(value, axis):
    count = lax.axis_size(axis)
    if not is_pow2(count):
        return lax.all_gather(value, axis, axis=0, tiled=True)
    me = lax.axis_index(axis)
    arr = value[None]
    bit = count // 2
    while bit >= 1:
        low = (me // bit) % 2 == 0
        other = xor_perm(arr, axis, bit)
        first = jnp.where(low, arr, other)
        second = jnp.where(low, other, arr)
        arr = jnp.stack([first, second], axis=1).reshape((-1,) + value.shape)
        bit //= 2
    return arr.reshape((-1,) + value.shape[1:])


def all_gather_many(values, axis):
    count = lax.axis_size(axis)
    if not is_pow2(count):
        return [lax.all_gather(v, axis, axis=0, tiled=True) for v in values]
    me = lax.axis_index(axis)
    arrs = [v[None] for v in values]
    bit = count // 2
    while bit >= 1:
        low = (me // bit) % 2 == 0
        others = lax.ppermute(arrs, axis, [(i, i ^ bit) for i in range(count)])
        arrs = [
            jnp.stack([jnp.where(low, a, o), jnp.where(low, o, a)], axis=1).reshape(
                (-1,) + v.shape
            )
            for a, o, v in zip(arrs, others, values)
        ]
        bit //= 2
    return [a.reshape((-1,) + v.shape[1:]) for a, v in zip(arrs, values)]


def all_sum(value, axis):
    count = lax.axis_size(axis)
    if count > 4:
        if not is_pow2(count):
            return lax.psum(value, axis)
        bit = 1
        while bit < count:
            value = value + xor_perm(value, axis, bit)
            bit *= 2
        return value
    me = lax.axis_index(axis)
    got = [value] + [
        lax.ppermute(value, axis, [(i, (i + k) % count) for i in range(count)])
        for k in range(1, count)
    ]
    stacked = jnp.stack(got)
    by_source = [
        lax.dynamic_index_in_dim(stacked, (me - src) % count, 0, keepdims=False)
        for src in range(count)
    ]
    total = by_source[0]
    for part in by_source[1:]:
        total = total + part
    return total


def local(hidden, proj_w, queries, lengths, candidates):
    mp_count = lax.axis_size("mp")
    owners = lax.axis_size("enc") * mp_count
    row_share = hidden.shape[0] // mp_count
    emb_width = proj_w.shape[1]
    qry_dev = queries.shape[0]
    query_len = queries.shape[1]
    cand_count = candidates.shape[1]
    blk_dev = row_share // BLK
    slot_count = qry_dev * cand_count
    capacity = 2 * slot_count // owners
    me = lax.axis_index("enc") * mp_count + lax.axis_index("mp")

    gathered = all_gather_many([queries, candidates], "mp")

    chunks = 2 if row_share % (2 * BLK) == 0 else 1
    split_rows = hidden.reshape(mp_count, chunks, row_share // chunks, hidden.shape[1])
    partials = [
        jnp.dot(split_rows[:, k], proj_w, preferred_element_type=jnp.float32).reshape(
            mp_count * (row_share // chunks), emb_width
        )
        for k in range(chunks)
    ]
    if is_pow2(mp_count) and mp_count > 1:
        keeps, sends, bit = halving_steps(partials, "mp")
        last, gathered = lax.optimization_barrier((sends[-1], gathered))
        sends = sends[:-1] + [last]
        pieces = [k + xor_perm(t, "mp", bit) for k, t in zip(keeps, sends)]
        pieces = [p.reshape(-1, emb_width) for p in pieces]
    else:
        pieces = [
            lax.psum_scatter(p, "mp", scatter_dimension=0, tiled=True) for p in partials
        ]
    e_pre = jnp.stack(pieces).reshape(row_share, emb_width)

    all_queries, all_cand = all_gather_many(gathered, "enc")
    all_cand = all_cand.reshape(owners, slot_count)

    slot_ids = jnp.arange(slot_count, dtype=jnp.int32)
    mine = (all_cand // blk_dev) == me
    rank = jnp.cumsum(mine.astype(jnp.int32), axis=1) - 1
    ranks = jnp.arange(capacity, dtype=jnp.int32)
    pick = mine[:, None, :] & (rank[:, None, :] == ranks[None, :, None])
    valid = jnp.any(pick, axis=2)
    slot_of = jnp.sum(jnp.where(pick, slot_ids[None, None, :], 0), axis=2).astype(jnp.int32)
    block_of = jnp.take_along_axis(all_cand, slot_of, axis=1)
    local_of = block_of % blk_dev
    query_of = jnp.arange(owners, dtype=jnp.int32)[:, None] * qry_dev + slot_of // cand_count

    q_e = all_queries[query_of]


    scale = lax.rsqrt(jnp.sum(e_pre * e_pre, -1, keepdims=True) + 1e-06)
    embedded = (e_pre * scale).astype(jnp.bfloat16)
    local_blocks = embedded.reshape(blk_dev, BLK, emb_width)

    tiles = local_blocks[local_of]
    valid_mask = block_valid(block_of, lengths)
    sim_tile = jnp.einsum("scie,scje->scij", q_e, tiles, preferred_element_type=jnp.float32)
    scores, weights = soft_max_sim(sim_tile, valid_mask[:, :, None, :])

    occ_raw = jnp.einsum("scij,scie->scje", weights, q_e, preferred_element_type=jnp.float32)

    placed = jnp.sum(jnp.where(pick, scores[:, :, None], jnp.float32(0)), axis=1)
    all_scores = all_sum(all_sum(placed, "mp"), "enc").reshape(owners * qry_dev, cand_count)
    all_losses, d_score = loss_terms(all_scores)
    losses = lax.dynamic_slice_in_dim(all_losses, me * qry_dev, qry_dev)

    d_e = jnp.take_along_axis(d_score.reshape(owners, slot_count), slot_of, axis=1)
    d_e = jnp.where(valid, d_e, jnp.float32(0))
    occ_grad = (occ_raw * (d_e / query_len)[:, :, None, None]).astype(jnp.bfloat16)
    onehot = (local_of[:, :, None] == jnp.arange(blk_dev, dtype=jnp.int32)) & valid[:, :, None]
    grad_emb = jnp.einsum(
        "scb,scje->bje",
        onehot.astype(jnp.bfloat16),
        occ_grad,
        preferred_element_type=jnp.float32,
    )
    grad_flat = grad_emb.reshape(row_share, emb_width)
    dot_e = jnp.sum(e_pre * grad_flat, -1, keepdims=True)
    de_pre = (scale * grad_flat - e_pre * (scale * scale * scale) * dot_e).astype(jnp.bfloat16)
    partial_w = left_product(hidden, all_gather_rows(de_pre, "mp"))
    grad_w = all_sum(partial_w, "enc")
    return (losses, grad_w)


def solution(mesh):
    return jax.shard_map(
        local,
        mesh=mesh,
        in_specs=(
            P(("groups", "enc"), "mp"),
            P("mp", None),
            P(("groups", "enc", "mp"), None, None),
            P("groups"),
            P(("groups", "enc", "mp"), None),
        ),
        out_specs=(P(("groups", "enc", "mp")), P(("groups", "mp"), None)),
        check_vma=False,
    )
```

```python
import jax
import jax.numpy as jnp
from jax import lax
from jax.sharding import PartitionSpec as P

L = 256
BLK = 64


def block_valid(block_ids, lengths):
    per_passage = L // BLK
    passage = block_ids // per_passage
    within = block_ids % per_passage
    positions = within[..., None] * BLK + jnp.arange(BLK, dtype=jnp.int32)
    return positions < lengths[passage][..., None]


def soft_max_sim(sim_tile, valid_mask):
    masked = jnp.where(valid_mask, sim_tile, jnp.float32(-1e30))
    peak = jnp.max(masked, -1, keepdims=True)
    shifted = jnp.exp(masked - peak)
    running = jnp.sum(shifted, -1, keepdims=True)
    scores = jnp.mean(peak[..., 0] + jnp.log(running[..., 0]), -1)
    weights = (shifted / running).astype(jnp.bfloat16)
    return (scores, weights)


def loss_terms(scores):
    margins = scores[:, 1:] - scores[:, :1]
    losses = jnp.mean(jax.nn.softplus(margins), 1)
    slopes = jax.nn.sigmoid(margins) / (scores.shape[1] - 1)
    d_score = jnp.concatenate([-jnp.sum(slopes, 1, keepdims=True), slopes], 1)
    return (losses, d_score)


def left_product(left, right):
    return lax.dot_general(
        left, right, (((0,), (0,)), ((), ())), preferred_element_type=jnp.float32
    )


def xor_perm(value, axis, bit):
    count = lax.axis_size(axis)
    return lax.ppermute(value, axis, [(i, i ^ bit) for i in range(count)])


def is_pow2(count):
    return count & (count - 1) == 0


def halving_steps(values, axis):
    count = lax.axis_size(axis)
    me = lax.axis_index(axis)
    accs = [v.reshape((count, -1) + v.shape[1:]) for v in values]
    bit = 1
    while True:
        keeps, sends = [], []
        for acc in accs:
            acc = acc.reshape((acc.shape[0] // 2, 2) + acc.shape[1:])
            low = (me // bit) % 2 == 0
            keeps.append(jnp.where(low, acc[:, 0], acc[:, 1]))
            sends.append(jnp.where(low, acc[:, 1], acc[:, 0]))
        if bit * 2 >= count:
            return keeps, sends, bit
        accs = [k + xor_perm(t, axis, bit) for k, t in zip(keeps, sends)]
        bit *= 2


def all_gather_rows(value, axis):
    count = lax.axis_size(axis)
    if not is_pow2(count):
        return lax.all_gather(value, axis, axis=0, tiled=True)
    me = lax.axis_index(axis)
    arr = value[None]
    bit = count // 2
    while bit >= 1:
        low = (me // bit) % 2 == 0
        other = xor_perm(arr, axis, bit)
        first = jnp.where(low, arr, other)
        second = jnp.where(low, other, arr)
        arr = jnp.stack([first, second], axis=1).reshape((-1,) + value.shape)
        bit //= 2
    return arr.reshape((-1,) + value.shape[1:])


def all_gather_many(values, axis):
    count = lax.axis_size(axis)
    if not is_pow2(count):
        return [lax.all_gather(v, axis, axis=0, tiled=True) for v in values]
    me = lax.axis_index(axis)
    arrs = [v[None] for v in values]
    bit = count // 2
    while bit >= 1:
        low = (me // bit) % 2 == 0
        others = lax.ppermute(arrs, axis, [(i, i ^ bit) for i in range(count)])
        arrs = [
            jnp.stack([jnp.where(low, a, o), jnp.where(low, o, a)], axis=1).reshape(
                (-1,) + v.shape
            )
            for a, o, v in zip(arrs, others, values)
        ]
        bit //= 2
    return [a.reshape((-1,) + v.shape[1:]) for a, v in zip(arrs, values)]


def all_sum(value, axis):
    count = lax.axis_size(axis)
    if count > 4:
        if not is_pow2(count):
            return lax.psum(value, axis)
        bit = 1
        while bit < count:
            value = value + xor_perm(value, axis, bit)
            bit *= 2
        return value
    me = lax.axis_index(axis)
    got = [value] + [
        lax.ppermute(value, axis, [(i, (i + k) % count) for i in range(count)])
        for k in range(1, count)
    ]
    stacked = jnp.stack(got)
    by_source = [
        lax.dynamic_index_in_dim(stacked, (me - src) % count, 0, keepdims=False)
        for src in range(count)
    ]
    total = by_source[0]
    for part in by_source[1:]:
        total = total + part
    return total


def local(hidden, proj_w, queries, lengths, candidates):
    mp_count = lax.axis_size("mp")
    owners = lax.axis_size("enc") * mp_count
    row_share = hidden.shape[0] // mp_count
    emb_width = proj_w.shape[1]
    qry_dev = queries.shape[0]
    query_len = queries.shape[1]
    cand_count = candidates.shape[1]
    blk_dev = row_share // BLK
    slot_count = qry_dev * cand_count
    capacity = 2 * slot_count // owners
    me = lax.axis_index("enc") * mp_count + lax.axis_index("mp")

    gathered = all_gather_many([queries, candidates], "mp")

    chunks = 1
    split_rows = hidden.reshape(mp_count, chunks, row_share // chunks, hidden.shape[1])
    partials = [
        jnp.dot(split_rows[:, k], proj_w, preferred_element_type=jnp.float32).reshape(
            mp_count * (row_share // chunks), emb_width
        )
        for k in range(chunks)
    ]
    if is_pow2(mp_count) and mp_count > 1:
        keeps, sends, bit = halving_steps(partials, "mp")
        last, gathered = lax.optimization_barrier((sends[-1], gathered))
        sends = sends[:-1] + [last]
        pieces = [k + xor_perm(t, "mp", bit) for k, t in zip(keeps, sends)]
        pieces = [p.reshape(-1, emb_width) for p in pieces]
    else:
        pieces = [
            lax.psum_scatter(p, "mp", scatter_dimension=0, tiled=True) for p in partials
        ]
    e_pre = jnp.stack(pieces).reshape(row_share, emb_width)

    all_queries, all_cand = all_gather_many(gathered, "enc")
    all_cand = all_cand.reshape(owners, slot_count)

    slot_ids = jnp.arange(slot_count, dtype=jnp.int32)
    mine = (all_cand // blk_dev) == me
    rank = jnp.cumsum(mine.astype(jnp.int32), axis=1) - 1
    ranks = jnp.arange(capacity, dtype=jnp.int32)
    pick = mine[:, None, :] & (rank[:, None, :] == ranks[None, :, None])
    valid = jnp.any(pick, axis=2)
    slot_of = jnp.sum(jnp.where(pick, slot_ids[None, None, :], 0), axis=2).astype(jnp.int32)
    block_of = jnp.take_along_axis(all_cand, slot_of, axis=1)
    local_of = block_of % blk_dev
    query_of = jnp.arange(owners, dtype=jnp.int32)[:, None] * qry_dev + slot_of // cand_count

    q_e = all_queries[query_of]


    scale = lax.rsqrt(jnp.sum(e_pre * e_pre, -1, keepdims=True) + 1e-06)
    embedded = (e_pre * scale).astype(jnp.bfloat16)
    local_blocks = embedded.reshape(blk_dev, BLK, emb_width)

    tiles = local_blocks[local_of]
    valid_mask = block_valid(block_of, lengths)
    sim_tile = jnp.einsum("scie,scje->scij", q_e, tiles, preferred_element_type=jnp.float32)
    scores, weights = soft_max_sim(sim_tile, valid_mask[:, :, None, :])

    occ_raw = jnp.einsum("scij,scie->scje", weights, q_e, preferred_element_type=jnp.float32)

    placed = jnp.sum(jnp.where(pick, scores[:, :, None], jnp.float32(0)), axis=1)
    all_scores = all_sum(all_sum(placed, "mp"), "enc").reshape(owners * qry_dev, cand_count)
    all_losses, d_score = loss_terms(all_scores)
    losses = lax.dynamic_slice_in_dim(all_losses, me * qry_dev, qry_dev)

    d_e = jnp.take_along_axis(d_score.reshape(owners, slot_count), slot_of, axis=1)
    d_e = jnp.where(valid, d_e, jnp.float32(0))
    occ_grad = (occ_raw * (d_e / query_len)[:, :, None, None]).astype(jnp.bfloat16)
    onehot = (local_of[:, :, None] == jnp.arange(blk_dev, dtype=jnp.int32)) & valid[:, :, None]
    grad_emb = jnp.einsum(
        "scb,scje->bje",
        onehot.astype(jnp.bfloat16),
        occ_grad,
        preferred_element_type=jnp.float32,
    )
    grad_flat = grad_emb.reshape(row_share, emb_width)
    dot_e = jnp.sum(e_pre * grad_flat, -1, keepdims=True)
    de_pre = (scale * grad_flat - e_pre * (scale * scale * scale) * dot_e).astype(jnp.bfloat16)
    partial_w = left_product(hidden, all_gather_rows(de_pre, "mp"))
    grad_w = all_sum(partial_w, "enc")
    return (losses, grad_w)


def solution(mesh):
    return jax.shard_map(
        local,
        mesh=mesh,
        in_specs=(
            P(("groups", "enc"), "mp"),
            P("mp", None),
            P(("groups", "enc", "mp"), None, None),
            P("groups"),
            P(("groups", "enc", "mp"), None),
        ),
        out_specs=(P(("groups", "enc", "mp")), P(("groups", "mp"), None)),
        check_vma=False,
    )
```

```python
import jax
import jax.numpy as jnp
from jax import lax
from jax.sharding import PartitionSpec as P

L = 256
BLK = 64


def block_valid(block_ids, lengths):
    per_passage = L // BLK
    passage = block_ids // per_passage
    within = block_ids % per_passage
    positions = within[..., None] * BLK + jnp.arange(BLK, dtype=jnp.int32)
    return positions < lengths[passage][..., None]


def soft_max_sim(sim_tile, valid_mask):
    masked = jnp.where(valid_mask, sim_tile, jnp.float32(-1e30))
    peak = jnp.max(masked, -1, keepdims=True)
    shifted = jnp.exp(masked - peak)
    running = jnp.sum(shifted, -1, keepdims=True)
    scores = jnp.mean(peak[..., 0] + jnp.log(running[..., 0]), -1)
    weights = (shifted / running).astype(jnp.bfloat16)
    return (scores, weights)


def loss_terms(scores):
    margins = scores[:, 1:] - scores[:, :1]
    losses = jnp.mean(jax.nn.softplus(margins), 1)
    slopes = jax.nn.sigmoid(margins) / (scores.shape[1] - 1)
    d_score = jnp.concatenate([-jnp.sum(slopes, 1, keepdims=True), slopes], 1)
    return (losses, d_score)


def left_product(left, right):
    return lax.dot_general(
        left, right, (((0,), (0,)), ((), ())), preferred_element_type=jnp.float32
    )


def xor_perm(value, axis, bit):
    count = lax.axis_size(axis)
    return lax.ppermute(value, axis, [(i, i ^ bit) for i in range(count)])


def is_pow2(count):
    return count & (count - 1) == 0


def halving_steps(values, axis):
    count = lax.axis_size(axis)
    me = lax.axis_index(axis)
    accs = [v.reshape((count, -1) + v.shape[1:]) for v in values]
    bit = 1
    while True:
        keeps, sends = [], []
        for acc in accs:
            acc = acc.reshape((acc.shape[0] // 2, 2) + acc.shape[1:])
            low = (me // bit) % 2 == 0
            keeps.append(jnp.where(low, acc[:, 0], acc[:, 1]))
            sends.append(jnp.where(low, acc[:, 1], acc[:, 0]))
        if bit * 2 >= count:
            return keeps, sends, bit
        accs = [k + xor_perm(t, axis, bit) for k, t in zip(keeps, sends)]
        bit *= 2


def all_gather_rows(value, axis):
    count = lax.axis_size(axis)
    if not is_pow2(count):
        return lax.all_gather(value, axis, axis=0, tiled=True)
    me = lax.axis_index(axis)
    arr = value[None]
    bit = count // 2
    while bit >= 1:
        low = (me // bit) % 2 == 0
        other = xor_perm(arr, axis, bit)
        first = jnp.where(low, arr, other)
        second = jnp.where(low, other, arr)
        arr = jnp.stack([first, second], axis=1).reshape((-1,) + value.shape)
        bit //= 2
    return arr.reshape((-1,) + value.shape[1:])


def all_gather_many(values, axis):
    count = lax.axis_size(axis)
    if not is_pow2(count):
        return [lax.all_gather(v, axis, axis=0, tiled=True) for v in values]
    me = lax.axis_index(axis)
    arrs = [v[None] for v in values]
    bit = count // 2
    while bit >= 1:
        low = (me // bit) % 2 == 0
        others = lax.ppermute(arrs, axis, [(i, i ^ bit) for i in range(count)])
        arrs = [
            jnp.stack([jnp.where(low, a, o), jnp.where(low, o, a)], axis=1).reshape(
                (-1,) + v.shape
            )
            for a, o, v in zip(arrs, others, values)
        ]
        bit //= 2
    return [a.reshape((-1,) + v.shape[1:]) for a, v in zip(arrs, values)]


def all_sum(value, axis):
    count = lax.axis_size(axis)
    if count > 4:
        if not is_pow2(count):
            return lax.psum(value, axis)
        bit = 1
        while bit < count:
            value = value + xor_perm(value, axis, bit)
            bit *= 2
        return value
    me = lax.axis_index(axis)
    got = [value] + [
        lax.ppermute(value, axis, [(i, (i + k) % count) for i in range(count)])
        for k in range(1, count)
    ]
    stacked = jnp.stack(got)
    by_source = [
        lax.dynamic_index_in_dim(stacked, (me - src) % count, 0, keepdims=False)
        for src in range(count)
    ]
    total = by_source[0]
    for part in by_source[1:]:
        total = total + part
    return total


def local(hidden, proj_w, queries, lengths, candidates):
    mp_count = lax.axis_size("mp")
    owners = lax.axis_size("enc") * mp_count
    row_share = hidden.shape[0] // mp_count
    emb_width = proj_w.shape[1]
    qry_dev = queries.shape[0]
    query_len = queries.shape[1]
    cand_count = candidates.shape[1]
    blk_dev = row_share // BLK
    slot_count = qry_dev * cand_count
    capacity = 2 * slot_count // owners
    me = lax.axis_index("enc") * mp_count + lax.axis_index("mp")

    gathered = all_gather_many([queries, candidates], "mp")

    chunks = 2 if row_share % (2 * BLK) == 0 else 1
    split_rows = hidden.reshape(mp_count, chunks, row_share // chunks, hidden.shape[1])
    partials = [
        jnp.dot(split_rows[:, k], proj_w, preferred_element_type=jnp.float32).reshape(
            mp_count * (row_share // chunks), emb_width
        )
        for k in range(chunks)
    ]
    if is_pow2(mp_count) and mp_count > 1:
        keeps, sends, bit = halving_steps(partials, "mp")
        first, gathered = lax.optimization_barrier((sends[0], gathered))
        sends = [first] + sends[1:]
        pieces = [k + xor_perm(t, "mp", bit) for k, t in zip(keeps, sends)]
        pieces = [p.reshape(-1, emb_width) for p in pieces]
    else:
        pieces = [
            lax.psum_scatter(p, "mp", scatter_dimension=0, tiled=True) for p in partials
        ]
    e_pre = jnp.stack(pieces).reshape(row_share, emb_width)

    all_queries, all_cand = all_gather_many(gathered, "enc")
    all_cand = all_cand.reshape(owners, slot_count)

    slot_ids = jnp.arange(slot_count, dtype=jnp.int32)
    mine = (all_cand // blk_dev) == me
    rank = jnp.cumsum(mine.astype(jnp.int32), axis=1) - 1
    ranks = jnp.arange(capacity, dtype=jnp.int32)
    pick = mine[:, None, :] & (rank[:, None, :] == ranks[None, :, None])
    valid = jnp.any(pick, axis=2)
    slot_of = jnp.sum(jnp.where(pick, slot_ids[None, None, :], 0), axis=2).astype(jnp.int32)
    block_of = jnp.take_along_axis(all_cand, slot_of, axis=1)
    local_of = block_of % blk_dev
    query_of = jnp.arange(owners, dtype=jnp.int32)[:, None] * qry_dev + slot_of // cand_count

    q_e = all_queries[query_of]


    scale = lax.rsqrt(jnp.sum(e_pre * e_pre, -1, keepdims=True) + 1e-06)
    embedded = (e_pre * scale).astype(jnp.bfloat16)
    local_blocks = embedded.reshape(blk_dev, BLK, emb_width)

    tiles = local_blocks[local_of]
    valid_mask = block_valid(block_of, lengths)
    sim_tile = jnp.einsum("scie,scje->scij", q_e, tiles, preferred_element_type=jnp.float32)
    scores, weights = soft_max_sim(sim_tile, valid_mask[:, :, None, :])

    occ_raw = jnp.einsum("scij,scie->scje", weights, q_e, preferred_element_type=jnp.float32)

    placed = jnp.sum(jnp.where(pick, scores[:, :, None], jnp.float32(0)), axis=1)
    all_scores = all_sum(all_sum(placed, "mp"), "enc").reshape(owners * qry_dev, cand_count)
    all_losses, d_score = loss_terms(all_scores)
    losses = lax.dynamic_slice_in_dim(all_losses, me * qry_dev, qry_dev)

    d_e = jnp.take_along_axis(d_score.reshape(owners, slot_count), slot_of, axis=1)
    d_e = jnp.where(valid, d_e, jnp.float32(0))
    occ_grad = (occ_raw * (d_e / query_len)[:, :, None, None]).astype(jnp.bfloat16)
    onehot = (local_of[:, :, None] == jnp.arange(blk_dev, dtype=jnp.int32)) & valid[:, :, None]
    grad_emb = jnp.einsum(
        "scb,scje->bje",
        onehot.astype(jnp.bfloat16),
        occ_grad,
        preferred_element_type=jnp.float32,
    )
    grad_flat = grad_emb.reshape(row_share, emb_width)
    dot_e = jnp.sum(e_pre * grad_flat, -1, keepdims=True)
    de_pre = (scale * grad_flat - e_pre * (scale * scale * scale) * dot_e).astype(jnp.bfloat16)
    partial_w = left_product(hidden, all_gather_rows(de_pre, "mp"))
    grad_w = all_sum(partial_w, "enc")
    return (losses, grad_w)


def solution(mesh):
    return jax.shard_map(
        local,
        mesh=mesh,
        in_specs=(
            P(("groups", "enc"), "mp"),
            P("mp", None),
            P(("groups", "enc", "mp"), None, None),
            P("groups"),
            P(("groups", "enc", "mp"), None),
        ),
        out_specs=(P(("groups", "enc", "mp")), P(("groups", "mp"), None)),
        check_vma=False,
    )
```

```python
import jax
import jax.numpy as jnp
from jax import lax
from jax.sharding import PartitionSpec as P

L = 256
BLK = 64


def block_valid(block_ids, lengths):
    per_passage = L // BLK
    passage = block_ids // per_passage
    within = block_ids % per_passage
    positions = within[..., None] * BLK + jnp.arange(BLK, dtype=jnp.int32)
    return positions < lengths[passage][..., None]


def soft_max_sim(sim_tile, valid_mask):
    masked = jnp.where(valid_mask, sim_tile, jnp.float32(-1e30))
    peak = jnp.max(masked, -1, keepdims=True)
    shifted = jnp.exp(masked - peak)
    running = jnp.sum(shifted, -1, keepdims=True)
    scores = jnp.mean(peak[..., 0] + jnp.log(running[..., 0]), -1)
    weights = (shifted / running).astype(jnp.bfloat16)
    return (scores, weights)


def loss_terms(scores):
    margins = scores[:, 1:] - scores[:, :1]
    losses = jnp.mean(jax.nn.softplus(margins), 1)
    slopes = jax.nn.sigmoid(margins) / (scores.shape[1] - 1)
    d_score = jnp.concatenate([-jnp.sum(slopes, 1, keepdims=True), slopes], 1)
    return (losses, d_score)


def left_product(left, right):
    return lax.dot_general(
        left, right, (((0,), (0,)), ((), ())), preferred_element_type=jnp.float32
    )


def xor_perm(value, axis, bit):
    count = lax.axis_size(axis)
    return lax.ppermute(value, axis, [(i, i ^ bit) for i in range(count)])


def is_pow2(count):
    return count & (count - 1) == 0


def halving_steps(values, axis):
    count = lax.axis_size(axis)
    me = lax.axis_index(axis)
    accs = [v.reshape((count, -1) + v.shape[1:]) for v in values]
    bit = 1
    while True:
        keeps, sends = [], []
        for acc in accs:
            acc = acc.reshape((acc.shape[0] // 2, 2) + acc.shape[1:])
            low = (me // bit) % 2 == 0
            keeps.append(jnp.where(low, acc[:, 0], acc[:, 1]))
            sends.append(jnp.where(low, acc[:, 1], acc[:, 0]))
        if bit * 2 >= count:
            return keeps, sends, bit
        accs = [k + xor_perm(t, axis, bit) for k, t in zip(keeps, sends)]
        bit *= 2


def all_gather_rows(value, axis):
    count = lax.axis_size(axis)
    if not is_pow2(count):
        return lax.all_gather(value, axis, axis=0, tiled=True)
    me = lax.axis_index(axis)
    arr = value[None]
    bit = count // 2
    while bit >= 1:
        low = (me // bit) % 2 == 0
        other = xor_perm(arr, axis, bit)
        first = jnp.where(low, arr, other)
        second = jnp.where(low, other, arr)
        arr = jnp.stack([first, second], axis=1).reshape((-1,) + value.shape)
        bit //= 2
    return arr.reshape((-1,) + value.shape[1:])


def all_gather_many(values, axis):
    count = lax.axis_size(axis)
    if not is_pow2(count):
        return [lax.all_gather(v, axis, axis=0, tiled=True) for v in values]
    me = lax.axis_index(axis)
    arrs = [v[None] for v in values]
    bit = count // 2
    while bit >= 1:
        low = (me // bit) % 2 == 0
        others = lax.ppermute(arrs, axis, [(i, i ^ bit) for i in range(count)])
        arrs = [
            jnp.stack([jnp.where(low, a, o), jnp.where(low, o, a)], axis=1).reshape(
                (-1,) + v.shape
            )
            for a, o, v in zip(arrs, others, values)
        ]
        bit //= 2
    return [a.reshape((-1,) + v.shape[1:]) for a, v in zip(arrs, values)]


def all_sum(value, axis):
    count = lax.axis_size(axis)
    if count > 4:
        if not is_pow2(count):
            return lax.psum(value, axis)
        bit = 1
        while bit < count:
            value = value + xor_perm(value, axis, bit)
            bit *= 2
        return value
    me = lax.axis_index(axis)
    got = [value] + [
        lax.ppermute(value, axis, [(i, (i + k) % count) for i in range(count)])
        for k in range(1, count)
    ]
    stacked = jnp.stack(got)
    by_source = [
        lax.dynamic_index_in_dim(stacked, (me - src) % count, 0, keepdims=False)
        for src in range(count)
    ]
    total = by_source[0]
    for part in by_source[1:]:
        total = total + part
    return total


def local(hidden, proj_w, queries, lengths, candidates):
    mp_count = lax.axis_size("mp")
    owners = lax.axis_size("enc") * mp_count
    row_share = hidden.shape[0] // mp_count
    emb_width = proj_w.shape[1]
    qry_dev = queries.shape[0]
    query_len = queries.shape[1]
    cand_count = candidates.shape[1]
    blk_dev = row_share // BLK
    slot_count = qry_dev * cand_count
    capacity = 2 * slot_count // owners
    me = lax.axis_index("enc") * mp_count + lax.axis_index("mp")

    gathered = all_gather_many([queries, candidates], "mp")

    chunks = 2 if row_share % (2 * BLK) == 0 else 1
    split_rows = hidden.reshape(mp_count, chunks, row_share // chunks, hidden.shape[1])
    partials = [
        jnp.dot(split_rows[:, k], proj_w, preferred_element_type=jnp.float32).reshape(
            mp_count * (row_share // chunks), emb_width
        )
        for k in range(chunks)
    ]
    if is_pow2(mp_count) and mp_count > 1:
        keeps, sends, bit = halving_steps(partials, "mp")
        pieces = [k + xor_perm(t, "mp", bit) for k, t in zip(keeps, sends)]
        pieces = [p.reshape(-1, emb_width) for p in pieces]
    else:
        pieces = [
            lax.psum_scatter(p, "mp", scatter_dimension=0, tiled=True) for p in partials
        ]
    e_pre = jnp.stack(pieces).reshape(row_share, emb_width)

    all_queries, all_cand = all_gather_many(gathered, "enc")
    all_cand = all_cand.reshape(owners, slot_count)

    slot_ids = jnp.arange(slot_count, dtype=jnp.int32)
    mine = (all_cand // blk_dev) == me
    rank = jnp.cumsum(mine.astype(jnp.int32), axis=1) - 1
    ranks = jnp.arange(capacity, dtype=jnp.int32)
    pick = mine[:, None, :] & (rank[:, None, :] == ranks[None, :, None])
    valid = jnp.any(pick, axis=2)
    slot_of = jnp.sum(jnp.where(pick, slot_ids[None, None, :], 0), axis=2).astype(jnp.int32)
    block_of = jnp.take_along_axis(all_cand, slot_of, axis=1)
    local_of = block_of % blk_dev
    query_of = jnp.arange(owners, dtype=jnp.int32)[:, None] * qry_dev + slot_of // cand_count

    q_e = all_queries[query_of]


    scale = lax.rsqrt(jnp.sum(e_pre * e_pre, -1, keepdims=True) + 1e-06)
    embedded = (e_pre * scale).astype(jnp.bfloat16)
    local_blocks = embedded.reshape(blk_dev, BLK, emb_width)

    tiles = local_blocks[local_of]
    valid_mask = block_valid(block_of, lengths)
    sim_tile = jnp.einsum("scie,scje->scij", q_e, tiles, preferred_element_type=jnp.float32)
    scores, weights = soft_max_sim(sim_tile, valid_mask[:, :, None, :])

    occ_raw = jnp.einsum("scij,scie->scje", weights, q_e, preferred_element_type=jnp.float32)

    placed = jnp.sum(jnp.where(pick, scores[:, :, None], jnp.float32(0)), axis=1)
    all_scores = all_sum(all_sum(placed, "mp"), "enc").reshape(owners * qry_dev, cand_count)
    all_losses, d_score = loss_terms(all_scores)
    losses = lax.dynamic_slice_in_dim(all_losses, me * qry_dev, qry_dev)

    d_e = jnp.take_along_axis(d_score.reshape(owners, slot_count), slot_of, axis=1)
    d_e = jnp.where(valid, d_e, jnp.float32(0))
    occ_grad = (occ_raw * (d_e / query_len)[:, :, None, None]).astype(jnp.bfloat16)
    onehot = (local_of[:, :, None] == jnp.arange(blk_dev, dtype=jnp.int32)) & valid[:, :, None]
    grad_emb = jnp.einsum(
        "scb,scje->bje",
        onehot.astype(jnp.bfloat16),
        occ_grad,
        preferred_element_type=jnp.float32,
    )
    grad_flat = grad_emb.reshape(row_share, emb_width)
    dot_e = jnp.sum(e_pre * grad_flat, -1, keepdims=True)
    de_pre = (scale * grad_flat - e_pre * (scale * scale * scale) * dot_e).astype(jnp.bfloat16)
    partial_w = left_product(hidden, all_gather_rows(de_pre, "mp"))
    grad_w = all_sum(partial_w, "enc")
    return (losses, grad_w)


def solution(mesh):
    return jax.shard_map(
        local,
        mesh=mesh,
        in_specs=(
            P(("groups", "enc"), "mp"),
            P("mp", None),
            P(("groups", "enc", "mp"), None, None),
            P("groups"),
            P(("groups", "enc", "mp"), None),
        ),
        out_specs=(P(("groups", "enc", "mp")), P(("groups", "mp"), None)),
        check_vma=False,
    )
```

```python
import jax
import jax.numpy as jnp
from jax import lax
from jax.sharding import PartitionSpec as P

L = 256
BLK = 64


def block_valid(block_ids, lengths):
    per_passage = L // BLK
    passage = block_ids // per_passage
    within = block_ids % per_passage
    positions = within[..., None] * BLK + jnp.arange(BLK, dtype=jnp.int32)
    return positions < lengths[passage][..., None]


def soft_max_sim(sim_tile, valid_mask):
    masked = jnp.where(valid_mask, sim_tile, jnp.float32(-1e30))
    peak = jnp.max(masked, -1, keepdims=True)
    shifted = jnp.exp(masked - peak)
    running = jnp.sum(shifted, -1, keepdims=True)
    scores = jnp.mean(peak[..., 0] + jnp.log(running[..., 0]), -1)
    weights = (shifted / running).astype(jnp.bfloat16)
    return (scores, weights)


def loss_terms(scores):
    margins = scores[:, 1:] - scores[:, :1]
    losses = jnp.mean(jax.nn.softplus(margins), 1)
    slopes = jax.nn.sigmoid(margins) / (scores.shape[1] - 1)
    d_score = jnp.concatenate([-jnp.sum(slopes, 1, keepdims=True), slopes], 1)
    return (losses, d_score)


def left_product(left, right):
    return lax.dot_general(
        left, right, (((0,), (0,)), ((), ())), preferred_element_type=jnp.float32
    )


def xor_perm(value, axis, bit):
    count = lax.axis_size(axis)
    return lax.ppermute(value, axis, [(i, i ^ bit) for i in range(count)])


def is_pow2(count):
    return count & (count - 1) == 0


def halving_steps(values, axis):
    count = lax.axis_size(axis)
    me = lax.axis_index(axis)
    accs = [v.reshape((count, -1) + v.shape[1:]) for v in values]
    bit = 1
    while True:
        keeps, sends = [], []
        for acc in accs:
            acc = acc.reshape((acc.shape[0] // 2, 2) + acc.shape[1:])
            low = (me // bit) % 2 == 0
            keeps.append(jnp.where(low, acc[:, 0], acc[:, 1]))
            sends.append(jnp.where(low, acc[:, 1], acc[:, 0]))
        if bit * 2 >= count:
            return keeps, sends, bit
        accs = [k + xor_perm(t, axis, bit) for k, t in zip(keeps, sends)]
        bit *= 2


def all_gather_rows(value, axis):
    count = lax.axis_size(axis)
    if not is_pow2(count):
        return lax.all_gather(value, axis, axis=0, tiled=True)
    me = lax.axis_index(axis)
    arr = value[None]
    bit = count // 2
    while bit >= 1:
        low = (me // bit) % 2 == 0
        other = xor_perm(arr, axis, bit)
        first = jnp.where(low, arr, other)
        second = jnp.where(low, other, arr)
        arr = jnp.stack([first, second], axis=1).reshape((-1,) + value.shape)
        bit //= 2
    return arr.reshape((-1,) + value.shape[1:])


def all_gather_many(values, axis):
    count = lax.axis_size(axis)
    if not is_pow2(count):
        return [lax.all_gather(v, axis, axis=0, tiled=True) for v in values]
    me = lax.axis_index(axis)
    arrs = [v[None] for v in values]
    bit = count // 2
    while bit >= 1:
        low = (me // bit) % 2 == 0
        others = lax.ppermute(arrs, axis, [(i, i ^ bit) for i in range(count)])
        arrs = [
            jnp.stack([jnp.where(low, a, o), jnp.where(low, o, a)], axis=1).reshape(
                (-1,) + v.shape
            )
            for a, o, v in zip(arrs, others, values)
        ]
        bit //= 2
    return [a.reshape((-1,) + v.shape[1:]) for a, v in zip(arrs, values)]


def all_sum(value, axis):
    count = lax.axis_size(axis)
    if count > 4:
        if not is_pow2(count):
            return lax.psum(value, axis)
        bit = 1
        while bit < count:
            value = value + xor_perm(value, axis, bit)
            bit *= 2
        return value
    me = lax.axis_index(axis)
    got = [value] + [
        lax.ppermute(value, axis, [(i, (i + k) % count) for i in range(count)])
        for k in range(1, count)
    ]
    stacked = jnp.stack(got)
    by_source = [
        lax.dynamic_index_in_dim(stacked, (me - src) % count, 0, keepdims=False)
        for src in range(count)
    ]
    total = by_source[0]
    for part in by_source[1:]:
        total = total + part
    return total


def local(hidden, proj_w, queries, lengths, candidates):
    mp_count = lax.axis_size("mp")
    owners = lax.axis_size("enc") * mp_count
    row_share = hidden.shape[0] // mp_count
    emb_width = proj_w.shape[1]
    qry_dev = queries.shape[0]
    query_len = queries.shape[1]
    cand_count = candidates.shape[1]
    blk_dev = row_share // BLK
    slot_count = qry_dev * cand_count
    capacity = 2 * slot_count // owners
    me = lax.axis_index("enc") * mp_count + lax.axis_index("mp")

    gathered = all_gather_many([queries, candidates], "mp")

    chunks = 4 if row_share % (4 * BLK) == 0 else 1
    split_rows = hidden.reshape(mp_count, chunks, row_share // chunks, hidden.shape[1])
    partials = [
        jnp.dot(split_rows[:, k], proj_w, preferred_element_type=jnp.float32).reshape(
            mp_count * (row_share // chunks), emb_width
        )
        for k in range(chunks)
    ]
    if is_pow2(mp_count) and mp_count > 1:
        keeps, sends, bit = halving_steps(partials, "mp")
        first, gathered = lax.optimization_barrier((sends[0], gathered))
        sends = [first] + sends[1:]
        pieces = [k + xor_perm(t, "mp", bit) for k, t in zip(keeps, sends)]
        pieces = [p.reshape(-1, emb_width) for p in pieces]
    else:
        pieces = [
            lax.psum_scatter(p, "mp", scatter_dimension=0, tiled=True) for p in partials
        ]
    e_pre = jnp.stack(pieces).reshape(row_share, emb_width)

    all_queries, all_cand = all_gather_many(gathered, "enc")
    all_cand = all_cand.reshape(owners, slot_count)

    slot_ids = jnp.arange(slot_count, dtype=jnp.int32)
    mine = (all_cand // blk_dev) == me
    rank = jnp.cumsum(mine.astype(jnp.int32), axis=1) - 1
    ranks = jnp.arange(capacity, dtype=jnp.int32)
    pick = mine[:, None, :] & (rank[:, None, :] == ranks[None, :, None])
    valid = jnp.any(pick, axis=2)
    slot_of = jnp.sum(jnp.where(pick, slot_ids[None, None, :], 0), axis=2).astype(jnp.int32)
    block_of = jnp.take_along_axis(all_cand, slot_of, axis=1)
    local_of = block_of % blk_dev
    query_of = jnp.arange(owners, dtype=jnp.int32)[:, None] * qry_dev + slot_of // cand_count

    q_e = all_queries[query_of]


    scale = lax.rsqrt(jnp.sum(e_pre * e_pre, -1, keepdims=True) + 1e-06)
    embedded = (e_pre * scale).astype(jnp.bfloat16)
    local_blocks = embedded.reshape(blk_dev, BLK, emb_width)

    tiles = local_blocks[local_of]
    valid_mask = block_valid(block_of, lengths)
    sim_tile = jnp.einsum("scie,scje->scij", q_e, tiles, preferred_element_type=jnp.float32)
    scores, weights = soft_max_sim(sim_tile, valid_mask[:, :, None, :])

    occ_raw = jnp.einsum("scij,scie->scje", weights, q_e, preferred_element_type=jnp.float32)

    placed = jnp.sum(jnp.where(pick, scores[:, :, None], jnp.float32(0)), axis=1)
    all_scores = all_sum(all_sum(placed, "mp"), "enc").reshape(owners * qry_dev, cand_count)
    all_losses, d_score = loss_terms(all_scores)
    losses = lax.dynamic_slice_in_dim(all_losses, me * qry_dev, qry_dev)

    d_e = jnp.take_along_axis(d_score.reshape(owners, slot_count), slot_of, axis=1)
    d_e = jnp.where(valid, d_e, jnp.float32(0))
    occ_grad = (occ_raw * (d_e / query_len)[:, :, None, None]).astype(jnp.bfloat16)
    onehot = (local_of[:, :, None] == jnp.arange(blk_dev, dtype=jnp.int32)) & valid[:, :, None]
    grad_emb = jnp.einsum(
        "scb,scje->bje",
        onehot.astype(jnp.bfloat16),
        occ_grad,
        preferred_element_type=jnp.float32,
    )
    grad_flat = grad_emb.reshape(row_share, emb_width)
    dot_e = jnp.sum(e_pre * grad_flat, -1, keepdims=True)
    de_pre = (scale * grad_flat - e_pre * (scale * scale * scale) * dot_e).astype(jnp.bfloat16)
    partial_w = left_product(hidden, all_gather_rows(de_pre, "mp"))
    grad_w = all_sum(partial_w, "enc")
    return (losses, grad_w)


def solution(mesh):
    return jax.shard_map(
        local,
        mesh=mesh,
        in_specs=(
            P(("groups", "enc"), "mp"),
            P("mp", None),
            P(("groups", "enc", "mp"), None, None),
            P("groups"),
            P(("groups", "enc", "mp"), None),
        ),
        out_specs=(P(("groups", "enc", "mp")), P(("groups", "mp"), None)),
        check_vma=False,
    )
```

```python
import jax
import jax.numpy as jnp
from jax import lax
from jax.sharding import PartitionSpec as P

L = 256
BLK = 64


def block_valid(block_ids, lengths):
    per_passage = L // BLK
    passage = block_ids // per_passage
    within = block_ids % per_passage
    positions = within[..., None] * BLK + jnp.arange(BLK, dtype=jnp.int32)
    return positions < lengths[passage][..., None]


def soft_max_sim(sim_tile, valid_mask):
    masked = jnp.where(valid_mask, sim_tile, jnp.float32(-1e30))
    peak = jnp.max(masked, -1, keepdims=True)
    shifted = jnp.exp(masked - peak)
    running = jnp.sum(shifted, -1, keepdims=True)
    scores = jnp.mean(peak[..., 0] + jnp.log(running[..., 0]), -1)
    weights = (shifted / running).astype(jnp.bfloat16)
    return (scores, weights)


def loss_terms(scores):
    margins = scores[:, 1:] - scores[:, :1]
    losses = jnp.mean(jax.nn.softplus(margins), 1)
    slopes = jax.nn.sigmoid(margins) / (scores.shape[1] - 1)
    d_score = jnp.concatenate([-jnp.sum(slopes, 1, keepdims=True), slopes], 1)
    return (losses, d_score)


def left_product(left, right):
    return lax.dot_general(
        left, right, (((0,), (0,)), ((), ())), preferred_element_type=jnp.float32
    )


def xor_perm(value, axis, bit):
    count = lax.axis_size(axis)
    return lax.ppermute(value, axis, [(i, i ^ bit) for i in range(count)])


def is_pow2(count):
    return count & (count - 1) == 0


def halving_steps(values, axis):
    count = lax.axis_size(axis)
    me = lax.axis_index(axis)
    accs = [v.reshape((count, -1) + v.shape[1:]) for v in values]
    bit = 1
    while True:
        keeps, sends = [], []
        for acc in accs:
            acc = acc.reshape((acc.shape[0] // 2, 2) + acc.shape[1:])
            low = (me // bit) % 2 == 0
            keeps.append(jnp.where(low, acc[:, 0], acc[:, 1]))
            sends.append(jnp.where(low, acc[:, 1], acc[:, 0]))
        if bit * 2 >= count:
            return keeps, sends, bit
        accs = [k + xor_perm(t, axis, bit) for k, t in zip(keeps, sends)]
        bit *= 2


def all_gather_rows(value, axis):
    count = lax.axis_size(axis)
    if not is_pow2(count):
        return lax.all_gather(value, axis, axis=0, tiled=True)
    me = lax.axis_index(axis)
    arr = value[None]
    bit = count // 2
    while bit >= 1:
        low = (me // bit) % 2 == 0
        other = xor_perm(arr, axis, bit)
        first = jnp.where(low, arr, other)
        second = jnp.where(low, other, arr)
        arr = jnp.stack([first, second], axis=1).reshape((-1,) + value.shape)
        bit //= 2
    return arr.reshape((-1,) + value.shape[1:])


def all_gather_many(values, axis):
    count = lax.axis_size(axis)
    if not is_pow2(count):
        return [lax.all_gather(v, axis, axis=0, tiled=True) for v in values]
    me = lax.axis_index(axis)
    arrs = [v[None] for v in values]
    bit = count // 2
    while bit >= 1:
        low = (me // bit) % 2 == 0
        others = lax.ppermute(arrs, axis, [(i, i ^ bit) for i in range(count)])
        arrs = [
            jnp.stack([jnp.where(low, a, o), jnp.where(low, o, a)], axis=1).reshape(
                (-1,) + v.shape
            )
            for a, o, v in zip(arrs, others, values)
        ]
        bit //= 2
    return [a.reshape((-1,) + v.shape[1:]) for a, v in zip(arrs, values)]


def all_sum(value, axis, one_step=True):
    count = lax.axis_size(axis)
    if count > 4 or not one_step:
        if not is_pow2(count):
            return lax.psum(value, axis)
        bit = 1
        while bit < count:
            value = value + xor_perm(value, axis, bit)
            bit *= 2
        return value
    me = lax.axis_index(axis)
    got = [value] + [
        lax.ppermute(value, axis, [(i, (i + k) % count) for i in range(count)])
        for k in range(1, count)
    ]
    stacked = jnp.stack(got)
    by_source = [
        lax.dynamic_index_in_dim(stacked, (me - src) % count, 0, keepdims=False)
        for src in range(count)
    ]
    total = by_source[0]
    for part in by_source[1:]:
        total = total + part
    return total


def local(hidden, proj_w, queries, lengths, candidates):
    mp_count = lax.axis_size("mp")
    owners = lax.axis_size("enc") * mp_count
    row_share = hidden.shape[0] // mp_count
    emb_width = proj_w.shape[1]
    qry_dev = queries.shape[0]
    query_len = queries.shape[1]
    cand_count = candidates.shape[1]
    blk_dev = row_share // BLK
    slot_count = qry_dev * cand_count
    capacity = 2 * slot_count // owners
    me = lax.axis_index("enc") * mp_count + lax.axis_index("mp")

    gathered = all_gather_many([queries, candidates], "mp")

    chunks = 2 if row_share % (2 * BLK) == 0 else 1
    split_rows = hidden.reshape(mp_count, chunks, row_share // chunks, hidden.shape[1])
    partials = [
        jnp.dot(split_rows[:, k], proj_w, preferred_element_type=jnp.float32).reshape(
            mp_count * (row_share // chunks), emb_width
        )
        for k in range(chunks)
    ]
    if is_pow2(mp_count) and mp_count > 1:
        keeps, sends, bit = halving_steps(partials, "mp")
        first, gathered = lax.optimization_barrier((sends[0], gathered))
        sends = [first] + sends[1:]
        pieces = [k + xor_perm(t, "mp", bit) for k, t in zip(keeps, sends)]
        pieces = [p.reshape(-1, emb_width) for p in pieces]
    else:
        pieces = [
            lax.psum_scatter(p, "mp", scatter_dimension=0, tiled=True) for p in partials
        ]
    e_pre = jnp.stack(pieces).reshape(row_share, emb_width)

    all_queries, all_cand = all_gather_many(gathered, "enc")
    all_cand = all_cand.reshape(owners, slot_count)

    slot_ids = jnp.arange(slot_count, dtype=jnp.int32)
    mine = (all_cand // blk_dev) == me
    rank = jnp.cumsum(mine.astype(jnp.int32), axis=1) - 1
    ranks = jnp.arange(capacity, dtype=jnp.int32)
    pick = mine[:, None, :] & (rank[:, None, :] == ranks[None, :, None])
    valid = jnp.any(pick, axis=2)
    slot_of = jnp.sum(jnp.where(pick, slot_ids[None, None, :], 0), axis=2).astype(jnp.int32)
    block_of = jnp.take_along_axis(all_cand, slot_of, axis=1)
    local_of = block_of % blk_dev
    query_of = jnp.arange(owners, dtype=jnp.int32)[:, None] * qry_dev + slot_of // cand_count

    q_e = all_queries[query_of]


    scale = lax.rsqrt(jnp.sum(e_pre * e_pre, -1, keepdims=True) + 1e-06)
    embedded = (e_pre * scale).astype(jnp.bfloat16)
    local_blocks = embedded.reshape(blk_dev, BLK, emb_width)

    tiles = local_blocks[local_of]
    valid_mask = block_valid(block_of, lengths)
    sim_tile = jnp.einsum("scie,scje->scij", q_e, tiles, preferred_element_type=jnp.float32)
    scores, weights = soft_max_sim(sim_tile, valid_mask[:, :, None, :])

    occ_raw = jnp.einsum("scij,scie->scje", weights, q_e, preferred_element_type=jnp.float32)

    placed = jnp.sum(jnp.where(pick, scores[:, :, None], jnp.float32(0)), axis=1)
    all_scores = all_sum(all_sum(placed, "mp"), "enc").reshape(owners * qry_dev, cand_count)
    all_losses, d_score = loss_terms(all_scores)
    losses = lax.dynamic_slice_in_dim(all_losses, me * qry_dev, qry_dev)

    d_e = jnp.take_along_axis(d_score.reshape(owners, slot_count), slot_of, axis=1)
    d_e = jnp.where(valid, d_e, jnp.float32(0))
    occ_grad = (occ_raw * (d_e / query_len)[:, :, None, None]).astype(jnp.bfloat16)
    onehot = (local_of[:, :, None] == jnp.arange(blk_dev, dtype=jnp.int32)) & valid[:, :, None]
    grad_emb = jnp.einsum(
        "scb,scje->bje",
        onehot.astype(jnp.bfloat16),
        occ_grad,
        preferred_element_type=jnp.float32,
    )
    grad_flat = grad_emb.reshape(row_share, emb_width)
    dot_e = jnp.sum(e_pre * grad_flat, -1, keepdims=True)
    de_pre = (scale * grad_flat - e_pre * (scale * scale * scale) * dot_e).astype(jnp.bfloat16)
    partial_w = left_product(hidden, all_gather_rows(de_pre, "mp"))
    grad_w = all_sum(partial_w, "enc", one_step=False)
    return (losses, grad_w)


def solution(mesh):
    return jax.shard_map(
        local,
        mesh=mesh,
        in_specs=(
            P(("groups", "enc"), "mp"),
            P("mp", None),
            P(("groups", "enc", "mp"), None, None),
            P("groups"),
            P(("groups", "enc", "mp"), None),
        ),
        out_specs=(P(("groups", "enc", "mp")), P(("groups", "mp"), None)),
        check_vma=False,
    )
```

```python
import jax
import jax.numpy as jnp
from jax import lax
from jax.sharding import PartitionSpec as P

L = 256
BLK = 64


def block_valid(block_ids, lengths):
    per_passage = L // BLK
    passage = block_ids // per_passage
    within = block_ids % per_passage
    positions = within[..., None] * BLK + jnp.arange(BLK, dtype=jnp.int32)
    return positions < lengths[passage][..., None]


def soft_max_sim(sim_tile, valid_mask):
    masked = jnp.where(valid_mask, sim_tile, jnp.float32(-1e30))
    peak = jnp.max(masked, -1, keepdims=True)
    shifted = jnp.exp(masked - peak)
    running = jnp.sum(shifted, -1, keepdims=True)
    scores = jnp.mean(peak[..., 0] + jnp.log(running[..., 0]), -1)
    weights = (shifted / running).astype(jnp.bfloat16)
    return (scores, weights)


def loss_terms(scores):
    margins = scores[:, 1:] - scores[:, :1]
    losses = jnp.mean(jax.nn.softplus(margins), 1)
    slopes = jax.nn.sigmoid(margins) / (scores.shape[1] - 1)
    d_score = jnp.concatenate([-jnp.sum(slopes, 1, keepdims=True), slopes], 1)
    return (losses, d_score)


def left_product(left, right):
    return lax.dot_general(
        left, right, (((0,), (0,)), ((), ())), preferred_element_type=jnp.float32
    )


def xor_perm(value, axis, bit):
    count = lax.axis_size(axis)
    return lax.ppermute(value, axis, [(i, i ^ bit) for i in range(count)])


def is_pow2(count):
    return count & (count - 1) == 0


def halving_steps(values, axis):
    count = lax.axis_size(axis)
    me = lax.axis_index(axis)
    accs = [v.reshape((count, -1) + v.shape[1:]) for v in values]
    bit = 1
    while True:
        keeps, sends = [], []
        for acc in accs:
            acc = acc.reshape((acc.shape[0] // 2, 2) + acc.shape[1:])
            low = (me // bit) % 2 == 0
            keeps.append(jnp.where(low, acc[:, 0], acc[:, 1]))
            sends.append(jnp.where(low, acc[:, 1], acc[:, 0]))
        if bit * 2 >= count:
            return keeps, sends, bit
        accs = [k + xor_perm(t, axis, bit) for k, t in zip(keeps, sends)]
        bit *= 2


def all_gather_rows(value, axis):
    count = lax.axis_size(axis)
    if not is_pow2(count):
        return lax.all_gather(value, axis, axis=0, tiled=True)
    me = lax.axis_index(axis)
    arr = value[None]
    bit = count // 2
    while bit >= 1:
        low = (me // bit) % 2 == 0
        other = xor_perm(arr, axis, bit)
        first = jnp.where(low, arr, other)
        second = jnp.where(low, other, arr)
        arr = jnp.stack([first, second], axis=1).reshape((-1,) + value.shape)
        bit //= 2
    return arr.reshape((-1,) + value.shape[1:])


def all_gather_many(values, axis):
    count = lax.axis_size(axis)
    if not is_pow2(count):
        return [lax.all_gather(v, axis, axis=0, tiled=True) for v in values]
    me = lax.axis_index(axis)
    arrs = [v[None] for v in values]
    bit = count // 2
    while bit >= 1:
        low = (me // bit) % 2 == 0
        others = lax.ppermute(arrs, axis, [(i, i ^ bit) for i in range(count)])
        arrs = [
            jnp.stack([jnp.where(low, a, o), jnp.where(low, o, a)], axis=1).reshape(
                (-1,) + v.shape
            )
            for a, o, v in zip(arrs, others, values)
        ]
        bit //= 2
    return [a.reshape((-1,) + v.shape[1:]) for a, v in zip(arrs, values)]


def all_sum(value, axis, one_step=True):
    count = lax.axis_size(axis)
    if count > 4 or not one_step:
        if not is_pow2(count):
            return lax.psum(value, axis)
        bit = 1
        while bit < count:
            value = value + xor_perm(value, axis, bit)
            bit *= 2
        return value
    me = lax.axis_index(axis)
    got = [value] + [
        lax.ppermute(value, axis, [(i, (i + k) % count) for i in range(count)])
        for k in range(1, count)
    ]
    stacked = jnp.stack(got)
    by_source = [
        lax.dynamic_index_in_dim(stacked, (me - src) % count, 0, keepdims=False)
        for src in range(count)
    ]
    total = by_source[0]
    for part in by_source[1:]:
        total = total + part
    return total


def local(hidden, proj_w, queries, lengths, candidates):
    mp_count = lax.axis_size("mp")
    owners = lax.axis_size("enc") * mp_count
    row_share = hidden.shape[0] // mp_count
    emb_width = proj_w.shape[1]
    qry_dev = queries.shape[0]
    query_len = queries.shape[1]
    cand_count = candidates.shape[1]
    blk_dev = row_share // BLK
    slot_count = qry_dev * cand_count
    capacity = 2 * slot_count // owners
    me = lax.axis_index("enc") * mp_count + lax.axis_index("mp")

    gathered = all_gather_many([queries, candidates], "mp")

    chunks = 2 if row_share % (2 * BLK) == 0 else 1
    split_rows = hidden.reshape(mp_count, chunks, row_share // chunks, hidden.shape[1])
    partials = [
        jnp.dot(split_rows[:, k], proj_w, preferred_element_type=jnp.float32).reshape(
            mp_count * (row_share // chunks), emb_width
        )
        for k in range(chunks)
    ]
    if is_pow2(mp_count) and mp_count > 1:
        keeps, sends, bit = halving_steps(partials, "mp")
        first, gathered = lax.optimization_barrier((sends[0], gathered))
        sends = [first] + sends[1:]
        pieces = [k + xor_perm(t, "mp", bit) for k, t in zip(keeps, sends)]
        pieces = [p.reshape(-1, emb_width) for p in pieces]
    else:
        pieces = [
            lax.psum_scatter(p, "mp", scatter_dimension=0, tiled=True) for p in partials
        ]
    e_pre = jnp.stack(pieces).reshape(row_share, emb_width)

    all_queries, all_cand = all_gather_many(gathered, "enc")
    all_cand = all_cand.reshape(owners, slot_count)

    slot_ids = jnp.arange(slot_count, dtype=jnp.int32)
    mine = (all_cand // blk_dev) == me
    rank = jnp.cumsum(mine.astype(jnp.int32), axis=1) - 1
    ranks = jnp.arange(capacity, dtype=jnp.int32)
    pick = mine[:, None, :] & (rank[:, None, :] == ranks[None, :, None])
    valid = jnp.any(pick, axis=2)
    slot_of = jnp.sum(jnp.where(pick, slot_ids[None, None, :], 0), axis=2).astype(jnp.int32)
    block_of = jnp.take_along_axis(all_cand, slot_of, axis=1)
    local_of = block_of % blk_dev
    query_of = jnp.arange(owners, dtype=jnp.int32)[:, None] * qry_dev + slot_of // cand_count

    q_e = all_queries[query_of]


    scale = lax.rsqrt(jnp.sum(e_pre * e_pre, -1, keepdims=True) + 1e-06)
    embedded = (e_pre * scale).astype(jnp.bfloat16)
    local_blocks = embedded.reshape(blk_dev, BLK, emb_width)

    tiles = local_blocks[local_of]
    valid_mask = block_valid(block_of, lengths)
    sim_tile = jnp.einsum("scie,scje->scij", q_e, tiles, preferred_element_type=jnp.float32)
    scores, weights = soft_max_sim(sim_tile, valid_mask[:, :, None, :])

    occ_raw = jnp.einsum("scij,scie->scje", weights, q_e, preferred_element_type=jnp.float32)

    placed = jnp.sum(jnp.where(pick, scores[:, :, None], jnp.float32(0)), axis=1)
    all_scores = all_sum(all_sum(placed, "mp", one_step=False), "enc", one_step=False).reshape(owners * qry_dev, cand_count)
    all_losses, d_score = loss_terms(all_scores)
    losses = lax.dynamic_slice_in_dim(all_losses, me * qry_dev, qry_dev)

    d_e = jnp.take_along_axis(d_score.reshape(owners, slot_count), slot_of, axis=1)
    d_e = jnp.where(valid, d_e, jnp.float32(0))
    occ_grad = (occ_raw * (d_e / query_len)[:, :, None, None]).astype(jnp.bfloat16)
    onehot = (local_of[:, :, None] == jnp.arange(blk_dev, dtype=jnp.int32)) & valid[:, :, None]
    grad_emb = jnp.einsum(
        "scb,scje->bje",
        onehot.astype(jnp.bfloat16),
        occ_grad,
        preferred_element_type=jnp.float32,
    )
    grad_flat = grad_emb.reshape(row_share, emb_width)
    dot_e = jnp.sum(e_pre * grad_flat, -1, keepdims=True)
    de_pre = (scale * grad_flat - e_pre * (scale * scale * scale) * dot_e).astype(jnp.bfloat16)
    partial_w = left_product(hidden, all_gather_rows(de_pre, "mp"))
    grad_w = all_sum(partial_w, "enc", one_step=False)
    return (losses, grad_w)


def solution(mesh):
    return jax.shard_map(
        local,
        mesh=mesh,
        in_specs=(
            P(("groups", "enc"), "mp"),
            P("mp", None),
            P(("groups", "enc", "mp"), None, None),
            P("groups"),
            P(("groups", "enc", "mp"), None),
        ),
        out_specs=(P(("groups", "enc", "mp")), P(("groups", "mp"), None)),
        check_vma=False,
    )
```

```python
import jax
import jax.numpy as jnp
from jax import lax
from jax.sharding import PartitionSpec as P

L = 256
BLK = 64


def block_valid(block_ids, lengths):
    per_passage = L // BLK
    passage = block_ids // per_passage
    within = block_ids % per_passage
    positions = within[..., None] * BLK + jnp.arange(BLK, dtype=jnp.int32)
    return positions < lengths[passage][..., None]


def soft_max_sim(sim_tile, valid_mask):
    masked = jnp.where(valid_mask, sim_tile, jnp.float32(-1e30))
    peak = jnp.max(masked, -1, keepdims=True)
    shifted = jnp.exp(masked - peak)
    running = jnp.sum(shifted, -1, keepdims=True)
    scores = jnp.mean(peak[..., 0] + jnp.log(running[..., 0]), -1)
    weights = (shifted / running).astype(jnp.bfloat16)
    return (scores, weights)


def loss_terms(scores):
    margins = scores[:, 1:] - scores[:, :1]
    losses = jnp.mean(jax.nn.softplus(margins), 1)
    slopes = jax.nn.sigmoid(margins) / (scores.shape[1] - 1)
    d_score = jnp.concatenate([-jnp.sum(slopes, 1, keepdims=True), slopes], 1)
    return (losses, d_score)


def left_product(left, right):
    return lax.dot_general(
        left, right, (((0,), (0,)), ((), ())), preferred_element_type=jnp.float32
    )


def xor_perm(value, axis, bit):
    count = lax.axis_size(axis)
    return lax.ppermute(value, axis, [(i, i ^ bit) for i in range(count)])


def is_pow2(count):
    return count & (count - 1) == 0


def halving_steps(values, axis):
    count = lax.axis_size(axis)
    me = lax.axis_index(axis)
    accs = [v.reshape((count, -1) + v.shape[1:]) for v in values]
    bit = 1
    while True:
        keeps, sends = [], []
        for acc in accs:
            acc = acc.reshape((acc.shape[0] // 2, 2) + acc.shape[1:])
            low = (me // bit) % 2 == 0
            keeps.append(jnp.where(low, acc[:, 0], acc[:, 1]))
            sends.append(jnp.where(low, acc[:, 1], acc[:, 0]))
        if bit * 2 >= count:
            return keeps, sends, bit
        accs = [k + xor_perm(t, axis, bit) for k, t in zip(keeps, sends)]
        bit *= 2


def all_gather_rows(value, axis):
    count = lax.axis_size(axis)
    if not is_pow2(count):
        return lax.all_gather(value, axis, axis=0, tiled=True)
    me = lax.axis_index(axis)
    arr = value[None]
    bit = count // 2
    while bit >= 1:
        low = (me // bit) % 2 == 0
        other = xor_perm(arr, axis, bit)
        first = jnp.where(low, arr, other)
        second = jnp.where(low, other, arr)
        arr = jnp.stack([first, second], axis=1).reshape((-1,) + value.shape)
        bit //= 2
    return arr.reshape((-1,) + value.shape[1:])


def all_gather_many(values, axis):
    count = lax.axis_size(axis)
    if not is_pow2(count):
        return [lax.all_gather(v, axis, axis=0, tiled=True) for v in values]
    me = lax.axis_index(axis)
    arrs = [v[None] for v in values]
    bit = count // 2
    while bit >= 1:
        low = (me // bit) % 2 == 0
        others = lax.ppermute(arrs, axis, [(i, i ^ bit) for i in range(count)])
        arrs = [
            jnp.stack([jnp.where(low, a, o), jnp.where(low, o, a)], axis=1).reshape(
                (-1,) + v.shape
            )
            for a, o, v in zip(arrs, others, values)
        ]
        bit //= 2
    return [a.reshape((-1,) + v.shape[1:]) for a, v in zip(arrs, values)]


def all_sum(value, axis, one_step=True):
    count = lax.axis_size(axis)
    if count > 4 or not one_step:
        if not is_pow2(count):
            return lax.psum(value, axis)
        bit = 1
        while bit < count:
            value = value + xor_perm(value, axis, bit)
            bit *= 2
        return value
    me = lax.axis_index(axis)
    got = [value] + [
        lax.ppermute(value, axis, [(i, (i + k) % count) for i in range(count)])
        for k in range(1, count)
    ]
    stacked = jnp.stack(got)
    by_source = [
        lax.dynamic_index_in_dim(stacked, (me - src) % count, 0, keepdims=False)
        for src in range(count)
    ]
    total = by_source[0]
    for part in by_source[1:]:
        total = total + part
    return total


def local(hidden, proj_w, queries, lengths, candidates):
    mp_count = lax.axis_size("mp")
    owners = lax.axis_size("enc") * mp_count
    row_share = hidden.shape[0] // mp_count
    emb_width = proj_w.shape[1]
    qry_dev = queries.shape[0]
    query_len = queries.shape[1]
    cand_count = candidates.shape[1]
    blk_dev = row_share // BLK
    slot_count = qry_dev * cand_count
    capacity = 2 * slot_count // owners
    me = lax.axis_index("enc") * mp_count + lax.axis_index("mp")

    gathered = all_gather_many([queries, candidates], "mp")

    chunks = 2 if row_share % (2 * BLK) == 0 else 1
    split_rows = hidden.reshape(mp_count, chunks, row_share // chunks, hidden.shape[1])
    partials = [
        jnp.dot(split_rows[:, k], proj_w, preferred_element_type=jnp.float32).reshape(
            mp_count * (row_share // chunks), emb_width
        )
        for k in range(chunks)
    ]
    if is_pow2(mp_count) and mp_count > 1:
        keeps, sends, bit = halving_steps(partials, "mp")
        first, gathered = lax.optimization_barrier((sends[0], gathered))
        sends = [first] + sends[1:]
        pieces = [k + xor_perm(t, "mp", bit) for k, t in zip(keeps, sends)]
        pieces = [p.reshape(-1, emb_width) for p in pieces]
    else:
        pieces = [
            lax.psum_scatter(p, "mp", scatter_dimension=0, tiled=True) for p in partials
        ]
    e_pre = jnp.stack(pieces).reshape(row_share, emb_width)

    all_queries, all_cand = all_gather_many(gathered, "enc")
    all_cand = all_cand.reshape(owners, slot_count)

    slot_ids = jnp.arange(slot_count, dtype=jnp.int32)
    mine = (all_cand // blk_dev) == me
    rank = jnp.cumsum(mine.astype(jnp.int32), axis=1) - 1
    ranks = jnp.arange(capacity, dtype=jnp.int32)
    pick = mine[:, None, :] & (rank[:, None, :] == ranks[None, :, None])
    valid = jnp.any(pick, axis=2)
    slot_of = jnp.sum(jnp.where(pick, slot_ids[None, None, :], 0), axis=2).astype(jnp.int32)
    block_of = jnp.take_along_axis(all_cand, slot_of, axis=1)
    local_of = block_of % blk_dev
    query_of = jnp.arange(owners, dtype=jnp.int32)[:, None] * qry_dev + slot_of // cand_count

    q_e = all_queries[query_of]


    scale = lax.rsqrt(jnp.sum(e_pre * e_pre, -1, keepdims=True) + 1e-06)
    embedded = (e_pre * scale).astype(jnp.bfloat16)
    local_blocks = embedded.reshape(blk_dev, BLK, emb_width)

    tiles = local_blocks[local_of]
    valid_mask = block_valid(block_of, lengths)
    sim_tile = jnp.einsum("scie,scje->scij", q_e, tiles, preferred_element_type=jnp.float32)
    scores, weights = soft_max_sim(sim_tile, valid_mask[:, :, None, :])

    occ_raw = jnp.einsum("scij,scie->scje", weights, q_e, preferred_element_type=jnp.float32)

    placed = jnp.sum(jnp.where(pick, scores[:, :, None], jnp.float32(0)), axis=1)
    all_scores = all_sum(all_sum(placed, "mp", one_step=False), "enc", one_step=False).reshape(owners * qry_dev, cand_count)
    all_losses, d_score = loss_terms(all_scores)
    losses = lax.dynamic_slice_in_dim(all_losses, me * qry_dev, qry_dev)

    d_e = jnp.take_along_axis(d_score.reshape(owners, slot_count), slot_of, axis=1)
    d_e = jnp.where(valid, d_e, jnp.float32(0))
    occ_grad = (occ_raw * (d_e / query_len)[:, :, None, None]).astype(jnp.bfloat16)
    onehot = (local_of[:, :, None] == jnp.arange(blk_dev, dtype=jnp.int32)) & valid[:, :, None]
    grad_emb = jnp.einsum(
        "scb,scje->bje",
        onehot.astype(jnp.bfloat16),
        occ_grad,
        preferred_element_type=jnp.float32,
    )
    grad_flat = grad_emb.reshape(row_share, emb_width)
    dot_e = jnp.sum(e_pre * grad_flat, -1, keepdims=True)
    de_pre = (scale * grad_flat - e_pre * (scale * scale * scale) * dot_e).astype(jnp.bfloat16)
    if mp_count == 4:
        low_bit = lax.axis_index("mp") % 2
        far_low = (lax.axis_index("mp") // 2) % 2 == 0
        rows_by = hidden.reshape(2, 2, row_share, hidden.shape[1])
        mine = de_pre[None]
        other = xor_perm(mine, "mp", 2)
        pair = jnp.concatenate(
            [jnp.where(far_low, mine, other), jnp.where(far_low, other, mine)], axis=0
        )
        near = lax.dynamic_index_in_dim(rows_by, low_bit, 1, keepdims=False)
        partial_w = left_product(near.reshape(-1, hidden.shape[1]), pair.reshape(-1, emb_width))
        partner_pair = xor_perm(pair, "mp", 1)
        away = lax.dynamic_index_in_dim(rows_by, 1 - low_bit, 1, keepdims=False)
        partial_w = partial_w + left_product(
            away.reshape(-1, hidden.shape[1]), partner_pair.reshape(-1, emb_width)
        )
    else:
        partial_w = left_product(hidden, all_gather_rows(de_pre, "mp"))
    grad_w = all_sum(partial_w, "enc", one_step=False)
    return (losses, grad_w)


def solution(mesh):
    return jax.shard_map(
        local,
        mesh=mesh,
        in_specs=(
            P(("groups", "enc"), "mp"),
            P("mp", None),
            P(("groups", "enc", "mp"), None, None),
            P("groups"),
            P(("groups", "enc", "mp"), None),
        ),
        out_specs=(P(("groups", "enc", "mp")), P(("groups", "mp"), None)),
        check_vma=False,
    )
```

```python
import jax
import jax.numpy as jnp
from jax import lax
from jax.sharding import PartitionSpec as P

L = 256
BLK = 64


def block_valid(block_ids, lengths):
    per_passage = L // BLK
    passage = block_ids // per_passage
    within = block_ids % per_passage
    positions = within[..., None] * BLK + jnp.arange(BLK, dtype=jnp.int32)
    return positions < lengths[passage][..., None]


def soft_max_sim(sim_tile, valid_mask):
    masked = jnp.where(valid_mask, sim_tile, jnp.float32(-1e30))
    peak = jnp.max(masked, -1, keepdims=True)
    shifted = jnp.exp(masked - peak)
    running = jnp.sum(shifted, -1, keepdims=True)
    scores = jnp.mean(peak[..., 0] + jnp.log(running[..., 0]), -1)
    weights = (shifted / running).astype(jnp.bfloat16)
    return (scores, weights)


def loss_terms(scores):
    margins = scores[:, 1:] - scores[:, :1]
    losses = jnp.mean(jax.nn.softplus(margins), 1)
    slopes = jax.nn.sigmoid(margins) / (scores.shape[1] - 1)
    d_score = jnp.concatenate([-jnp.sum(slopes, 1, keepdims=True), slopes], 1)
    return (losses, d_score)


def left_product(left, right):
    return lax.dot_general(
        left, right, (((0,), (0,)), ((), ())), preferred_element_type=jnp.float32
    )


def xor_perm(value, axis, bit):
    count = lax.axis_size(axis)
    return lax.ppermute(value, axis, [(i, i ^ bit) for i in range(count)])


def is_pow2(count):
    return count & (count - 1) == 0


def halving_steps(values, axis):
    count = lax.axis_size(axis)
    me = lax.axis_index(axis)
    accs = [v.reshape((count, -1) + v.shape[1:]) for v in values]
    bit = 1
    while True:
        keeps, sends = [], []
        for acc in accs:
            acc = acc.reshape((acc.shape[0] // 2, 2) + acc.shape[1:])
            low = (me // bit) % 2 == 0
            keeps.append(jnp.where(low, acc[:, 0], acc[:, 1]))
            sends.append(jnp.where(low, acc[:, 1], acc[:, 0]))
        if bit * 2 >= count:
            return keeps, sends, bit
        accs = [k + xor_perm(t, axis, bit) for k, t in zip(keeps, sends)]
        bit *= 2


def all_gather_rows(value, axis):
    count = lax.axis_size(axis)
    if not is_pow2(count):
        return lax.all_gather(value, axis, axis=0, tiled=True)
    me = lax.axis_index(axis)
    arr = value[None]
    bit = count // 2
    while bit >= 1:
        low = (me // bit) % 2 == 0
        other = xor_perm(arr, axis, bit)
        first = jnp.where(low, arr, other)
        second = jnp.where(low, other, arr)
        arr = jnp.stack([first, second], axis=1).reshape((-1,) + value.shape)
        bit //= 2
    return arr.reshape((-1,) + value.shape[1:])


def all_gather_many(values, axis):
    count = lax.axis_size(axis)
    if not is_pow2(count):
        return [lax.all_gather(v, axis, axis=0, tiled=True) for v in values]
    me = lax.axis_index(axis)
    arrs = [v[None] for v in values]
    bit = count // 2
    while bit >= 1:
        low = (me // bit) % 2 == 0
        others = lax.ppermute(arrs, axis, [(i, i ^ bit) for i in range(count)])
        arrs = [
            jnp.stack([jnp.where(low, a, o), jnp.where(low, o, a)], axis=1).reshape(
                (-1,) + v.shape
            )
            for a, o, v in zip(arrs, others, values)
        ]
        bit //= 2
    return [a.reshape((-1,) + v.shape[1:]) for a, v in zip(arrs, values)]


def all_sum(value, axis, one_step=True):
    count = lax.axis_size(axis)
    if count > 4 or not one_step:
        if not is_pow2(count):
            return lax.psum(value, axis)
        bit = count // 2
        while bit >= 1:
            value = value + xor_perm(value, axis, bit)
            bit //= 2
        return value
    me = lax.axis_index(axis)
    got = [value] + [
        lax.ppermute(value, axis, [(i, (i + k) % count) for i in range(count)])
        for k in range(1, count)
    ]
    stacked = jnp.stack(got)
    by_source = [
        lax.dynamic_index_in_dim(stacked, (me - src) % count, 0, keepdims=False)
        for src in range(count)
    ]
    total = by_source[0]
    for part in by_source[1:]:
        total = total + part
    return total


def local(hidden, proj_w, queries, lengths, candidates):
    mp_count = lax.axis_size("mp")
    owners = lax.axis_size("enc") * mp_count
    row_share = hidden.shape[0] // mp_count
    emb_width = proj_w.shape[1]
    qry_dev = queries.shape[0]
    query_len = queries.shape[1]
    cand_count = candidates.shape[1]
    blk_dev = row_share // BLK
    slot_count = qry_dev * cand_count
    capacity = 2 * slot_count // owners
    me = lax.axis_index("enc") * mp_count + lax.axis_index("mp")

    gathered = all_gather_many([queries, candidates], "mp")

    chunks = 2 if row_share % (2 * BLK) == 0 else 1
    split_rows = hidden.reshape(mp_count, chunks, row_share // chunks, hidden.shape[1])
    partials = [
        jnp.dot(split_rows[:, k], proj_w, preferred_element_type=jnp.float32).reshape(
            mp_count * (row_share // chunks), emb_width
        )
        for k in range(chunks)
    ]
    if is_pow2(mp_count) and mp_count > 1:
        keeps, sends, bit = halving_steps(partials, "mp")
        first, gathered = lax.optimization_barrier((sends[0], gathered))
        sends = [first] + sends[1:]
        pieces = [k + xor_perm(t, "mp", bit) for k, t in zip(keeps, sends)]
        pieces = [p.reshape(-1, emb_width) for p in pieces]
    else:
        pieces = [
            lax.psum_scatter(p, "mp", scatter_dimension=0, tiled=True) for p in partials
        ]
    e_pre = jnp.stack(pieces).reshape(row_share, emb_width)

    all_queries, all_cand = all_gather_many(gathered, "enc")
    all_cand = all_cand.reshape(owners, slot_count)

    slot_ids = jnp.arange(slot_count, dtype=jnp.int32)
    mine = (all_cand // blk_dev) == me
    rank = jnp.cumsum(mine.astype(jnp.int32), axis=1) - 1
    ranks = jnp.arange(capacity, dtype=jnp.int32)
    pick = mine[:, None, :] & (rank[:, None, :] == ranks[None, :, None])
    valid = jnp.any(pick, axis=2)
    slot_of = jnp.sum(jnp.where(pick, slot_ids[None, None, :], 0), axis=2).astype(jnp.int32)
    block_of = jnp.take_along_axis(all_cand, slot_of, axis=1)
    local_of = block_of % blk_dev
    query_of = jnp.arange(owners, dtype=jnp.int32)[:, None] * qry_dev + slot_of // cand_count

    q_e = all_queries[query_of]


    scale = lax.rsqrt(jnp.sum(e_pre * e_pre, -1, keepdims=True) + 1e-06)
    embedded = (e_pre * scale).astype(jnp.bfloat16)
    local_blocks = embedded.reshape(blk_dev, BLK, emb_width)

    tiles = local_blocks[local_of]
    valid_mask = block_valid(block_of, lengths)
    sim_tile = jnp.einsum("scie,scje->scij", q_e, tiles, preferred_element_type=jnp.float32)
    scores, weights = soft_max_sim(sim_tile, valid_mask[:, :, None, :])

    occ_raw = jnp.einsum("scij,scie->scje", weights, q_e, preferred_element_type=jnp.float32)

    placed = jnp.sum(jnp.where(pick, scores[:, :, None], jnp.float32(0)), axis=1)
    all_scores = all_sum(all_sum(placed, "mp", one_step=False), "enc", one_step=False).reshape(owners * qry_dev, cand_count)
    all_losses, d_score = loss_terms(all_scores)
    losses = lax.dynamic_slice_in_dim(all_losses, me * qry_dev, qry_dev)

    d_e = jnp.take_along_axis(d_score.reshape(owners, slot_count), slot_of, axis=1)
    d_e = jnp.where(valid, d_e, jnp.float32(0))
    occ_grad = (occ_raw * (d_e / query_len)[:, :, None, None]).astype(jnp.bfloat16)
    onehot = (local_of[:, :, None] == jnp.arange(blk_dev, dtype=jnp.int32)) & valid[:, :, None]
    grad_emb = jnp.einsum(
        "scb,scje->bje",
        onehot.astype(jnp.bfloat16),
        occ_grad,
        preferred_element_type=jnp.float32,
    )
    grad_flat = grad_emb.reshape(row_share, emb_width)
    dot_e = jnp.sum(e_pre * grad_flat, -1, keepdims=True)
    de_pre = (scale * grad_flat - e_pre * (scale * scale * scale) * dot_e).astype(jnp.bfloat16)
    if mp_count == 4:
        low_bit = lax.axis_index("mp") % 2
        far_low = (lax.axis_index("mp") // 2) % 2 == 0
        rows_by = hidden.reshape(2, 2, row_share, hidden.shape[1])
        mine = de_pre[None]
        other = xor_perm(mine, "mp", 2)
        pair = jnp.concatenate(
            [jnp.where(far_low, mine, other), jnp.where(far_low, other, mine)], axis=0
        )
        near = lax.dynamic_index_in_dim(rows_by, low_bit, 1, keepdims=False)
        partial_w = left_product(near.reshape(-1, hidden.shape[1]), pair.reshape(-1, emb_width))
        partner_pair = xor_perm(pair, "mp", 1)
        away = lax.dynamic_index_in_dim(rows_by, 1 - low_bit, 1, keepdims=False)
        partial_w = partial_w + left_product(
            away.reshape(-1, hidden.shape[1]), partner_pair.reshape(-1, emb_width)
        )
    else:
        partial_w = left_product(hidden, all_gather_rows(de_pre, "mp"))
    grad_w = all_sum(partial_w, "enc", one_step=False)
    return (losses, grad_w)


def solution(mesh):
    return jax.shard_map(
        local,
        mesh=mesh,
        in_specs=(
            P(("groups", "enc"), "mp"),
            P("mp", None),
            P(("groups", "enc", "mp"), None, None),
            P("groups"),
            P(("groups", "enc", "mp"), None),
        ),
        out_specs=(P(("groups", "enc", "mp")), P(("groups", "mp"), None)),
        check_vma=False,
    )
```
